32 devices in a mesh: groups: 2 (over y), dom: 4 (over x, core), sub: 4 (over z).
Axes of the slice: x: 2, y: 2, z: 4, core: 2. Of those that a mesh axis runs over, the one named last changes fastest.
Arguments:
- node_states: float32 [8192, 512], P(('groups', 'dom', 'sub')), parts along dimension 0, may hold values from -6 to 6
- node_pre: float32 [8192, 512], P(('groups', 'dom', 'sub')), parts along dimension 0, may hold values from -6 to 6
- edge_states: float32 [4096, 512], P(('groups', 'dom', 'sub')), parts along dimension 0, may hold values from -6 to 6
- edge_pre: float32 [4096, 512], P(('groups', 'dom', 'sub')), parts along dimension 0, may hold values from -6 to 6
- node_cotangent: float32 [8192, 512], P(('groups', 'dom', 'sub')), parts along dimension 0, may hold values from -6 to 6
- edge_cotangent: float32 [4096, 512], P(('groups', 'dom', 'sub')), parts along dimension 0, may hold values from -6 to 6
- endpoints: int32 [2, 4096], P(None, ('groups', 'dom', 'sub')), parts along dimension 1, may hold values from 0 to 319, as said below
- send_lists: int32 [32, 4, 16], P(('groups', 'dom', 'sub')), parts along dimension 0, may hold values from 0 to 255, as said below
- node_counts: int32 [32], P(('groups', 'dom', 'sub')), parts along dimension 0, may hold values from 128 to 256
- edge_blocks: int32 [32], P(('groups', 'dom', 'sub')), parts along dimension 0, may hold values from 1 to 1
- edge_first: float32 [1536, 512], P(('dom', 'sub')), may hold values from -0.15625 to 0.15625
- edge_second: float32 [512, 512], P(('dom', 'sub')), may hold values from -0.25 to 0.25
- edge_bias: float32 [512], P(('dom', 'sub')), may hold values from -3 to 3
- edge_gain: float32 [512], P(('dom', 'sub')), may hold values from 0.5 to 1.5
- edge_shift: float32 [512], P(('dom', 'sub')), may hold values from -3 to 3
- node_first: float32 [1024, 512], P(('dom', 'sub')), may hold values from -0.1875 to 0.1875
- node_second: float32 [512, 512], P(('dom', 'sub')), may hold values from -0.25 to 0.25
- node_bias: float32 [512], P(('dom', 'sub')), may hold values from -3 to 3
- node_gain: float32 [512], P(('dom', 'sub')), may hold values from 0.5 to 1.5
Outputs:
- edge_grads: float32 [4096, 512], P(('groups', 'dom', 'sub')), parts along dimension 0
- node_grads: float32 [8192, 512], P(('groups', 'dom', 'sub')), parts along dimension 0
- edge_first_grad: float32 [3072, 512], P(('groups', 'dom', 'sub')), parts along dimension 0
- edge_second_grad: float32 [1024, 512], P(('groups', 'dom', 'sub')), parts along dimension 0
- node_first_grad: float32 [2048, 512], P(('groups', 'dom', 'sub')), parts along dimension 0
- node_second_grad: float32 [1024, 512], P(('groups', 'dom', 'sub')), parts along dimension 0
The draws below stay inside these ranges and needn't reach their ends.
There are 2 independent parts, one for each index of `groups`. The reference program is written for one: setup_inputs(seed, part) draws one part's arguments, and reference() takes and returns one part's arrays. A program takes and returns all parts, laid end to end along the dimension named above; an argument that names none is the same for every part. Nothing has to cross between parts.
Inputs may be any that keep to these rules, and one draw needn't show every extreme that they name: `endpoints`: sender slots are a live local node below node_counts of the device, or a ghost slot 256 + k * 16 + j whose neighbour k exists; receiver slots are live local nodes. `send_lists`: every entry is a live node of its device.
All inputs are finite; a program needn't handle non-finite values.
Results may differ from the reference program's by a relative error of at most 0.0003.
Values sent between devices are 32-bit elements; how exact they have to be, the bound alone decides.
No kernel may reach another device: no remote copies, remote signals or barrier semaphores. Data moves between devices by JAX's collectives and lax.ppermute only.
A program may use at most 128 MiB of HBM per device.

```python
import jax
import jax.numpy as jnp
from jax import lax

D = 512
E_DEV = 128
N_DEV = 256
G = 16
DOMS = 4
SUBS = 4
DEVS = 16
BLOCKS = 1
EDGES = 2048
NODES = 4096


def fullest_device(key):
    base = jax.random.fold_in(key, 101)
    first, second = jax.random.split(base)
    return (first, jax.random.randint(second, (), 0, DEVS))


def live_counts(key):
    first, fullest = fullest_device(key)
    counts = jax.random.randint(first, (DEVS,), N_DEV // 2, N_DEV + 1)
    return jnp.where(jnp.arange(DEVS) == fullest, N_DEV, counts).astype(jnp.int32)


def draw_node_counts(key, part):
    return live_counts(key)


def draw_edge_blocks(key, part):
    base = jax.random.fold_in(key, 202)
    first, second = jax.random.split(base)
    blocks = jax.random.randint(first, (DEVS,), max(1, BLOCKS // 2), BLOCKS + 1)
    fullest = jax.random.randint(second, (), 0, DEVS)
    return jnp.where(jnp.arange(DEVS) == fullest, BLOCKS, blocks).astype(jnp.int32)


def draw_send_lists(key, part):
    counts = live_counts(key)
    first, fullest = fullest_device(key)
    stream = jax.random.fold_in(key, 303)
    lists = jax.random.randint(stream, (DEVS, 4, G), 0, counts[:, None, None]).astype(jnp.int32)
    lists = lists.at[fullest, 0, 0].set(N_DEV - 1)
    lists = lists.at[fullest, 0, 1].set(0)
    return lists.astype(jnp.int32)


def draw_endpoints(key, part):
    counts = live_counts(key)
    streams = jax.random.split(jax.random.fold_in(key, 404), 5)
    target = jax.random.randint(streams[0], (DEVS, E_DEV), 0, counts[:, None])
    local_source = jax.random.randint(streams[1], (DEVS, E_DEV), 0, counts[:, None])
    direction = jax.random.randint(streams[2], (DEVS, E_DEV), 0, 4)
    ghost_slot = jax.random.randint(streams[3], (DEVS, E_DEV), 0, G)
    ghost_coin = jax.random.randint(streams[4], (DEVS, E_DEV), 0, 4)
    device = jnp.arange(DEVS)[:, None]
    dom_place = device // SUBS
    sub_place = device % SUBS
    exists = jnp.where(direction == 0, dom_place > 0, jnp.where(direction == 1, dom_place < DOMS - 1, jnp.where(direction == 2, sub_place > 0, sub_place < SUBS - 1)))
    source = jnp.where((ghost_coin == 0) & exists, N_DEV + direction * G + ghost_slot, local_source)
    source = source.at[0, 0].set(N_DEV + 4 * G - 1)
    target = target.at[0, 0].set(0)
    return jnp.stack([source.reshape(-1), target.reshape(-1)]).astype(jnp.int32)


def shard_levels(key, shape, cuts, smallest, largest):
    loudness, own = 1.0, jax.random.fold_in(key, 6)
    for dim, shards_of in cuts:
        draws = jnp.exp(jax.random.uniform(jax.random.fold_in(own, dim), (shards_of,), jnp.float32, smallest / len(cuts), largest / len(cuts)))
        loudness = loudness * jnp.repeat(draws, shape[dim] // shards_of).reshape([-1 if axis == dim else 1 for axis in range(len(shape))])
    return loudness


def bell_draw(stream_key, extent, scale, most, cuts=(), held_as=jnp.bfloat16):
    drawn = jax.random.normal(stream_key, extent, jnp.float32) * scale
    if len(cuts) > 0:
        drawn = shard_levels(stream_key, extent, cuts, -0.22, 0.18) * drawn
    return jnp.clip(drawn, min=-most, max=most).astype(held_as)


def setup_inputs(seed: int = 0, part: int = 0) -> dict:
    seeds = jax.random.split(jax.random.key(seed), 20)
    part_keys = jax.random.split(jax.random.fold_in(seeds[19], part), 20)
    return {
        "node_states": bell_draw(part_keys[0], (NODES, D), 1.0, 6.0, ((0, 16),), jnp.float32),
        "node_pre": bell_draw(part_keys[1], (NODES, D), 1.0, 6.0, ((0, 16),), jnp.float32),
        "edge_states": bell_draw(part_keys[2], (EDGES, D), 1.0, 6.0, ((0, 16),), jnp.float32),
        "edge_pre": bell_draw(part_keys[3], (EDGES, D), 1.0, 6.0, ((0, 16),), jnp.float32),
        "node_cotangent": bell_draw(part_keys[4], (NODES, D), 1.0, 6.0, ((0, 16),), jnp.float32),
        "edge_cotangent": bell_draw(part_keys[5], (EDGES, D), 1.0, 6.0, ((0, 16),), jnp.float32),
        "endpoints": draw_endpoints(jax.random.fold_in(jax.random.fold_in(seeds[19], part), 71), part),
        "send_lists": draw_send_lists(jax.random.fold_in(jax.random.fold_in(seeds[19], part), 71), part),
        "node_counts": draw_node_counts(jax.random.fold_in(jax.random.fold_in(seeds[19], part), 71), part),
        "edge_blocks": draw_edge_blocks(jax.random.fold_in(jax.random.fold_in(seeds[19], part), 71), part),
        "edge_first": bell_draw(seeds[10], (3 * D, D), (3 * D) ** -0.5, 0.15625, ((0, 16),), jnp.float32),
        "edge_second": bell_draw(seeds[11], (D, D), D ** -0.5, 0.25, ((0, 16),), jnp.float32),
        "edge_bias": bell_draw(seeds[12], (D,), 0.5, 3.0, ((0, 16),), jnp.float32),
        "edge_gain": jnp.clip(0.5 + 1.0 * jax.random.uniform(seeds[13], (D,), jnp.float32) ** shard_levels(seeds[13], (D,), ((0, 16),), -0.2, 0.2), 0.5, 1.5),
        "edge_shift": bell_draw(seeds[14], (D,), 0.5, 3.0, ((0, 16),), jnp.float32),
        "node_first": bell_draw(seeds[15], (2 * D, D), (2 * D) ** -0.5, 0.1875, ((0, 16),), jnp.float32),
        "node_second": bell_draw(seeds[16], (D, D), D ** -0.5, 0.25, ((0, 16),), jnp.float32),
        "node_bias": bell_draw(seeds[17], (D,), 0.5, 3.0, ((0, 16),), jnp.float32),
        "node_gain": jnp.clip(0.5 + 1.0 * jax.random.uniform(seeds[18], (D,), jnp.float32) ** shard_levels(seeds[18], (D,), ((0, 16),), -0.2, 0.2), 0.5, 1.5),
    }


EPSILON = 1e-05

def matmul(left, right):
    return jnp.dot(left, right, precision=lax.Precision.HIGHEST, preferred_element_type=jnp.float32)

def layer_norm(values):
    center = values - lax.optimization_barrier(jnp.mean(values, axis=-1, keepdims=True))
    inverse = 1.0 / jnp.sqrt(lax.optimization_barrier(jnp.mean(center * center, axis=-1, keepdims=True)) + EPSILON)
    return (center * inverse, inverse)

def norm_back(upstream, normed, inverse):
    first = lax.optimization_barrier(jnp.mean(upstream, axis=-1, keepdims=True))
    second = lax.optimization_barrier(jnp.mean(upstream * normed, axis=-1, keepdims=True))
    return inverse * (upstream - first - normed * second)

def ghost_rows(node_blocks, send_lists):
    sent = jax.vmap(lambda table, picks: jnp.take(table, picks, axis=0))(node_blocks, send_lists)
    sent = sent.reshape(DOMS, SUBS, 4, G, D)
    empty_dom = jnp.zeros((1, SUBS, G, D), jnp.float32)
    empty_sub = jnp.zeros((DOMS, 1, G, D), jnp.float32)
    group_zero = jnp.concatenate([empty_dom, sent[:-1, :, 0]], axis=0)
    group_one = jnp.concatenate([sent[1:, :, 1], empty_dom], axis=0)
    group_two = jnp.concatenate([empty_sub, sent[:, :-1, 2]], axis=1)
    group_three = jnp.concatenate([sent[:, 1:, 3], empty_sub], axis=1)
    stacked = jnp.stack([group_zero, group_one, group_two, group_three], axis=2)
    return stacked.reshape(DEVS, 4 * G, D)

def return_rows(grads):
    shaped = grads.reshape(DOMS, SUBS, 4, G, D)
    empty_dom = jnp.zeros((1, SUBS, G, D), jnp.float32)
    empty_sub = jnp.zeros((DOMS, 1, G, D), jnp.float32)
    list_zero = jnp.concatenate([shaped[1:, :, 0], empty_dom], axis=0)
    list_one = jnp.concatenate([empty_dom, shaped[:-1, :, 1]], axis=0)
    list_two = jnp.concatenate([shaped[:, 1:, 2], empty_sub], axis=1)
    list_three = jnp.concatenate([empty_sub, shaped[:, :-1, 3]], axis=1)
    stacked = jnp.stack([list_zero, list_one, list_two, list_three], axis=2)
    return stacked.reshape(DEVS, 4, G, D)

def reference(node_states, node_pre, edge_states, edge_pre, node_cotangent, edge_cotangent, endpoints, send_lists, node_counts, edge_blocks, edge_first, edge_second, edge_bias, edge_gain, edge_shift, node_first, node_second, node_bias, node_gain):
    node_blocks = node_states.reshape(DEVS, N_DEV, D)
    ghosts = ghost_rows(node_blocks, send_lists)
    device_items = (node_blocks, node_pre.reshape(DEVS, N_DEV, D), edge_states.reshape(DEVS, E_DEV, D), edge_pre.reshape(DEVS, E_DEV, D), node_cotangent.reshape(DEVS, N_DEV, D), edge_cotangent.reshape(DEVS, E_DEV, D), endpoints[0].reshape(DEVS, E_DEV), endpoints[1].reshape(DEVS, E_DEV), node_counts, edge_blocks, ghosts)

    def device_step(totals, device_item):
        states, pre_nodes, edges_here, pre_edges, cot_nodes, cot_edges, source, target, live_count, live_blocks, ghost_here = device_item
        live_nodes = (jnp.arange(N_DEV) < live_count).astype(jnp.float32)[:, None]
        live_edges = (jnp.arange(E_DEV) < live_blocks * 128).astype(jnp.float32)[:, None]
        edge_act = jnp.maximum(pre_edges, 0.0)
        edge_normed, edge_inverse = layer_norm(matmul(edge_act, edge_second) + edge_bias)
        message = (edge_normed * edge_gain + edge_shift) * live_edges
        aggregate = jax.ops.segment_sum(message, target, N_DEV)
        node_act = jnp.maximum(pre_nodes, 0.0)
        node_normed, node_inverse = layer_norm(matmul(node_act, node_second) + node_bias)
        node_upstream = cot_nodes * live_nodes
        node_grad_z = norm_back(node_upstream * node_gain, node_normed, node_inverse)
        node_grad_pre = matmul(node_grad_z, node_second.T) * (pre_nodes > 0).astype(jnp.float32)
        node_input = jnp.concatenate([states, aggregate], axis=1)
        node_grad_input = matmul(node_grad_pre, node_first.T)
        state_grads = node_upstream + node_grad_input[:, :D]
        edge_upstream = (cot_edges + jnp.take(node_grad_input[:, D:], target, axis=0)) * live_edges
        edge_grad_z = norm_back(edge_upstream * edge_gain, edge_normed, edge_inverse)
        edge_grad_pre = matmul(edge_grad_z, edge_second.T) * (pre_edges > 0).astype(jnp.float32)
        extended = jnp.concatenate([states, ghost_here], axis=0)
        features = jnp.concatenate([edges_here, jnp.take(extended, source, axis=0), jnp.take(extended, target, axis=0)], axis=1)
        edge_grad_input = matmul(edge_grad_pre, edge_first.T)
        edge_out = (cot_edges + edge_grad_input[:, :D]) * live_edges
        extended_grads = jax.ops.segment_sum(edge_grad_input[:, D:2 * D], source, N_DEV + 4 * G)
        extended_grads = extended_grads + jax.ops.segment_sum(edge_grad_input[:, 2 * D:], target, N_DEV + 4 * G)
        state_grads = state_grads + extended_grads[:N_DEV]
        returned = extended_grads[N_DEV:].reshape(4, G, D)
        new_totals = (totals[0] + matmul(features.T, edge_grad_pre), totals[1] + matmul(edge_act.T, edge_grad_z), totals[2] + matmul(node_input.T, node_grad_pre), totals[3] + matmul(node_act.T, node_grad_z))
        return (new_totals, (edge_out, state_grads, returned))
    start = (jnp.zeros((3 * D, D), jnp.float32), jnp.zeros((D, D), jnp.float32), jnp.zeros((2 * D, D), jnp.float32), jnp.zeros((D, D), jnp.float32))
    totals, outputs = lax.scan(device_step, start, device_items)
    edge_out, state_grads, returned = outputs
    backward = return_rows(returned)
    added = jax.vmap(lambda rows, picks: jax.ops.segment_sum(rows.reshape(-1, D), picks.reshape(-1), N_DEV))(backward, send_lists)
    state_grads = state_grads + added
    edge_scale = 1.0 / jnp.sqrt(jnp.float32(EDGES))
    node_scale = 1.0 / jnp.sqrt(jnp.float32(NODES))
    return (edge_out.reshape(EDGES, D), state_grads.reshape(NODES, D), totals[0] * edge_scale, totals[1] * edge_scale, totals[2] * node_scale, totals[3] * node_scale)
```

```python
import math

import jax
import jax.numpy as jnp
from jax import lax
from jax.sharding import PartitionSpec as P

EPSILON = 1e-05


def padded(cells, sides, width):
    for axis, dim in sides:
        count = lax.axis_size(axis)
        ends = count - 1
        head = lax.slice_in_dim(cells, 0, width, axis=dim)
        tail = lax.slice_in_dim(cells, cells.shape[dim] - width, cells.shape[dim], axis=dim)
        cells = jnp.concatenate(
            [
                lax.ppermute(tail, axis, [(i, (i + 1) % count) for i in range(ends)]),
                cells,
                lax.ppermute(head, axis, [((i + 1) % count, i) for i in range(ends)]),
            ],
            axis=dim,
        )
    return cells


def matmul(left, right):
    return jnp.dot(left, right, precision=lax.Precision.HIGHEST, preferred_element_type=jnp.float32)


def inner(left, right):
    return lax.dot_general(
        left,
        right,
        (((0,), (0,)), ((), ())),
        precision=lax.Precision.HIGHEST,
        preferred_element_type=jnp.float32,
    )


def outer_back(left, right):
    return lax.dot_general(
        left,
        right,
        (((1,), (1,)), ((), ())),
        precision=lax.Precision.HIGHEST,
        preferred_element_type=jnp.float32,
    )


def layer_norm(values):
    center = values - jnp.mean(values, axis=-1, keepdims=True)
    inverse = 1.0 / jnp.sqrt(jnp.mean(center * center, axis=-1, keepdims=True) + EPSILON)
    return (center * inverse, inverse)


def norm_back(upstream, normed, inverse):
    first = jnp.mean(upstream, axis=-1, keepdims=True)
    second = jnp.mean(upstream * normed, axis=-1, keepdims=True)
    return inverse * (upstream - first - normed * second)


def shards(
    node_states,
    node_pre,
    edge_states,
    edge_pre,
    node_cotangent,
    edge_cotangent,
    endpoints,
    send_lists,
    node_counts,
    edge_blocks,
    edge_first,
    edge_second,
    edge_bias,
    edge_gain,
    edge_shift,
    node_first,
    node_second,
    node_bias,
    node_gain,
):
    node_rows, width = node_states.shape
    edge_rows = edge_states.shape[0]
    ghost = send_lists.shape[2]
    dom_count = lax.axis_size("dom")
    sub_count = lax.axis_size("sub")
    peer_count = dom_count * sub_count
    lists = send_lists[0]
    outgoing = jnp.take(node_states, lists.reshape(-1), axis=0).reshape(4, ghost, width)
    dom_side = padded(jnp.stack([outgoing[1], outgoing[0]]), (("dom", 0),), 1)
    sub_side = padded(jnp.stack([outgoing[3], outgoing[2]]), (("sub", 0),), 1)
    ghosts = jnp.stack([dom_side[0], dom_side[3], sub_side[0], sub_side[3]])
    ghosts = ghosts.reshape(4 * ghost, width)
    peers = ("dom", "sub")
    matrices = (edge_first, edge_second, node_first, node_second)
    vectors = jnp.concatenate([edge_bias, edge_gain, edge_shift, node_bias, node_gain])
    vector_rows = -(-vectors.shape[0] // width)
    vectors = jnp.pad(vectors, (0, vector_rows * width - vectors.shape[0])).reshape(vector_rows, width)
    packed = jnp.concatenate(list(matrices) + [vectors], axis=0)
    gathered = lax.all_gather(packed, peers, axis=0, tiled=False)
    pieces = []
    offset = 0
    for rows in [m.shape[0] for m in matrices] + [vector_rows]:
        pieces.append(gathered[:, offset : offset + rows, :])
        offset += rows
    full_edge_first, full_edge_second, full_node_first, full_node_second = (
        piece.reshape(-1, width) for piece in pieces[:4]
    )
    vector_count = edge_bias.shape[0]
    all_vectors = pieces[4].reshape(pieces[4].shape[0], -1)[:, : 5 * vector_count]
    all_vectors = all_vectors.reshape(-1, 5, vector_count).transpose(1, 0, 2).reshape(5, -1)
    full_edge_bias, full_edge_gain, full_edge_shift, full_node_bias, full_node_gain = (
        all_vectors[i] for i in range(5)
    )
    live_nodes = (jnp.arange(node_rows) < node_counts[0]).astype(jnp.float32)[:, None]
    live_edges = (jnp.arange(edge_rows) < edge_blocks[0] * 128).astype(jnp.float32)[:, None]
    source = endpoints[0]
    target = endpoints[1]
    edge_scale = 1.0 / math.sqrt(edge_rows * peer_count)
    node_scale = 1.0 / math.sqrt(node_rows * peer_count)
    edge_act = jnp.maximum(edge_pre, 0.0)
    edge_normed, edge_inverse = layer_norm(matmul(edge_act, full_edge_second) + full_edge_bias)
    message = (edge_normed * full_edge_gain + full_edge_shift) * live_edges
    aggregate = jax.ops.segment_sum(message, target, node_rows)
    node_act = jnp.maximum(node_pre, 0.0)
    node_normed, node_inverse = layer_norm(matmul(node_act, full_node_second) + full_node_bias)
    node_upstream = node_cotangent * live_nodes
    node_grad_z = norm_back(node_upstream * full_node_gain, node_normed, node_inverse)
    node_grad_pre = outer_back(node_grad_z, full_node_second) * (node_pre > 0).astype(jnp.float32)
    node_input = jnp.concatenate([node_states, aggregate], axis=1)
    node_first_part = inner(node_input, node_grad_pre) * node_scale
    node_second_part = inner(node_act, node_grad_z) * node_scale
    node_grad_input = outer_back(node_grad_pre, full_node_first)
    state_grads = node_upstream + node_grad_input[:, :width]
    edge_upstream = (
        edge_cotangent + jnp.take(node_grad_input[:, width:], target, axis=0)
    ) * live_edges
    edge_grad_z = norm_back(edge_upstream * full_edge_gain, edge_normed, edge_inverse)
    edge_grad_pre = outer_back(edge_grad_z, full_edge_second) * (edge_pre > 0).astype(jnp.float32)
    edge_second_part = inner(edge_act, edge_grad_z) * edge_scale
    extended = jnp.concatenate([node_states, ghosts], axis=0)
    features = jnp.concatenate(
        [edge_states, jnp.take(extended, source, axis=0), jnp.take(extended, target, axis=0)],
        axis=1,
    )
    edge_first_part = inner(features, edge_grad_pre) * edge_scale
    parts = (edge_first_part, edge_second_part, node_first_part, node_second_part)
    blocked = jnp.concatenate(
        [part.reshape(peer_count, -1, width) for part in parts], axis=1
    )
    reduced = lax.psum_scatter(blocked, peers, scatter_dimension=0, tiled=True)[0]
    grads = []
    offset = 0
    for rows in [m.shape[0] for m in matrices]:
        grads.append(reduced[offset : offset + rows])
        offset += rows
    edge_first_grad, edge_second_grad, node_first_grad, node_second_grad = grads
    edge_grad_input = outer_back(edge_grad_pre, full_edge_first)
    edge_grads = (edge_cotangent + edge_grad_input[:, :width]) * live_edges
    extended_grads = jax.ops.segment_sum(
        edge_grad_input[:, width : 2 * width], source, node_rows + 4 * ghost
    )
    extended_grads = extended_grads + jax.ops.segment_sum(
        edge_grad_input[:, 2 * width :], target, node_rows + 4 * ghost
    )
    state_grads = state_grads + extended_grads[:node_rows]
    ghost_grads = extended_grads[node_rows:].reshape(4, ghost, width)
    dom_back = padded(jnp.stack([ghost_grads[0], ghost_grads[1]]), (("dom", 0),), 1)
    sub_back = padded(jnp.stack([ghost_grads[2], ghost_grads[3]]), (("sub", 0),), 1)
    returned = jnp.stack([dom_back[3], dom_back[0], sub_back[3], sub_back[0]])
    state_grads = state_grads + jax.ops.segment_sum(
        returned.reshape(-1, width), lists.reshape(-1), node_rows
    )
    return (
        edge_grads,
        state_grads,
        edge_first_grad,
        edge_second_grad,
        node_first_grad,
        node_second_grad,
    )


def solution(mesh):
    in_specs = (
        P(("groups", "dom", "sub"), None),
        P(("groups", "dom", "sub"), None),
        P(("groups", "dom", "sub"), None),
        P(("groups", "dom", "sub"), None),
        P(("groups", "dom", "sub"), None),
        P(("groups", "dom", "sub"), None),
        P(None, ("groups", "dom", "sub")),
        P(("groups", "dom", "sub"), None, None),
        P(("groups", "dom", "sub")),
        P(("groups", "dom", "sub")),
        P(("dom", "sub"), None),
        P(("dom", "sub"), None),
        P(("dom", "sub")),
        P(("dom", "sub")),
        P(("dom", "sub")),
        P(("dom", "sub"), None),
        P(("dom", "sub"), None),
        P(("dom", "sub")),
        P(("dom", "sub")),
    )
    out_specs = (
        P(("groups", "dom", "sub"), None),
        P(("groups", "dom", "sub"), None),
        P(("groups", "dom", "sub"), None),
        P(("groups", "dom", "sub"), None),
        P(("groups", "dom", "sub"), None),
        P(("groups", "dom", "sub"), None),
    )
    return jax.shard_map(shards, mesh=mesh, in_specs=in_specs, out_specs=out_specs, check_vma=False)
```

```python
import math

import jax
import jax.numpy as jnp
from jax import lax
from jax.sharding import Mesh
from jax.sharding import PartitionSpec as P

EPSILON = 1e-05
DOM = ("domx", "core")


def axis_count(axis):
    if isinstance(axis, tuple):
        return math.prod(lax.axis_size(name) for name in axis)
    return lax.axis_size(axis)


def padded(cells, sides, width):
    for axis, dim in sides:
        count = axis_count(axis)
        ends = count - 1
        head = lax.slice_in_dim(cells, 0, width, axis=dim)
        tail = lax.slice_in_dim(cells, cells.shape[dim] - width, cells.shape[dim], axis=dim)
        cells = jnp.concatenate(
            [
                lax.ppermute(tail, axis, [(i, (i + 1) % count) for i in range(ends)]),
                cells,
                lax.ppermute(head, axis, [((i + 1) % count, i) for i in range(ends)]),
            ],
            axis=dim,
        )
    return cells


def matmul(left, right):
    return jnp.dot(left, right, precision=lax.Precision.HIGHEST, preferred_element_type=jnp.float32)


def inner(left, right):
    return lax.dot_general(
        left,
        right,
        (((0,), (0,)), ((), ())),
        precision=lax.Precision.HIGHEST,
        preferred_element_type=jnp.float32,
    )


def outer_back(left, right):
    return lax.dot_general(
        left,
        right,
        (((1,), (1,)), ((), ())),
        precision=lax.Precision.HIGHEST,
        preferred_element_type=jnp.float32,
    )


def layer_norm(values):
    center = values - jnp.mean(values, axis=-1, keepdims=True)
    inverse = 1.0 / jnp.sqrt(jnp.mean(center * center, axis=-1, keepdims=True) + EPSILON)
    return (center * inverse, inverse)


def norm_back(upstream, normed, inverse):
    first = jnp.mean(upstream, axis=-1, keepdims=True)
    second = jnp.mean(upstream * normed, axis=-1, keepdims=True)
    return inverse * (upstream - first - normed * second)


def shards(
    node_states,
    node_pre,
    edge_states,
    edge_pre,
    node_cotangent,
    edge_cotangent,
    endpoints,
    send_lists,
    node_counts,
    edge_blocks,
    edge_first,
    edge_second,
    edge_bias,
    edge_gain,
    edge_shift,
    node_first,
    node_second,
    node_bias,
    node_gain,
):
    node_rows, width = node_states.shape
    edge_rows = edge_states.shape[0]
    ghost = send_lists.shape[2]
    dom_count = axis_count(DOM)
    sub_count = lax.axis_size("sub")
    peer_count = dom_count * sub_count
    lists = send_lists[0]
    outgoing = jnp.take(node_states, lists.reshape(-1), axis=0).reshape(4, ghost, width)
    dom_side = padded(jnp.stack([outgoing[1], outgoing[0]]), ((DOM, 0),), 1)
    sub_side = padded(jnp.stack([outgoing[3], outgoing[2]]), (("sub", 0),), 1)
    ghosts = jnp.stack([dom_side[0], dom_side[3], sub_side[0], sub_side[3]])
    ghosts = ghosts.reshape(4 * ghost, width)
    chips = ("domx", "sub")
    core = lax.axis_index("core")
    swap = [(0, 1), (1, 0)]
    chip_rows = lax.axis_size("domx")
    matrices = (edge_first, edge_second, node_first, node_second)
    vectors = jnp.concatenate([edge_bias, edge_gain, edge_shift, node_bias, node_gain])
    vector_rows = -(-vectors.shape[0] // width)
    vectors = jnp.pad(vectors, (0, vector_rows * width - vectors.shape[0])).reshape(vector_rows, width)
    packed = jnp.concatenate(list(matrices) + [vectors], axis=0)
    mine = lax.all_gather(packed, chips, axis=0, tiled=False)
    theirs = lax.ppermute(mine, "core", swap)
    mine = mine.reshape(chip_rows, 1, sub_count, *packed.shape)
    theirs = theirs.reshape(chip_rows, 1, sub_count, *packed.shape)
    low = core == 0
    gathered = jnp.concatenate(
        [jnp.where(low, mine, theirs), jnp.where(low, theirs, mine)], axis=1
    ).reshape(peer_count, *packed.shape)
    pieces = []
    offset = 0
    for rows in [m.shape[0] for m in matrices] + [vector_rows]:
        pieces.append(gathered[:, offset : offset + rows, :])
        offset += rows
    full_edge_first, full_edge_second, full_node_first, full_node_second = (
        piece.reshape(-1, width) for piece in pieces[:4]
    )
    vector_count = edge_bias.shape[0]
    all_vectors = pieces[4].reshape(pieces[4].shape[0], -1)[:, : 5 * vector_count]
    all_vectors = all_vectors.reshape(-1, 5, vector_count).transpose(1, 0, 2).reshape(5, -1)
    full_edge_bias, full_edge_gain, full_edge_shift, full_node_bias, full_node_gain = (
        all_vectors[i] for i in range(5)
    )
    live_nodes = (jnp.arange(node_rows) < node_counts[0]).astype(jnp.float32)[:, None]
    live_edges = (jnp.arange(edge_rows) < edge_blocks[0] * 128).astype(jnp.float32)[:, None]
    source = endpoints[0]
    target = endpoints[1]
    edge_scale = 1.0 / math.sqrt(edge_rows * peer_count)
    node_scale = 1.0 / math.sqrt(node_rows * peer_count)
    edge_act = jnp.maximum(edge_pre, 0.0)
    edge_normed, edge_inverse = layer_norm(matmul(edge_act, full_edge_second) + full_edge_bias)
    message = (edge_normed * full_edge_gain + full_edge_shift) * live_edges
    aggregate = jax.ops.segment_sum(message, target, node_rows)
    node_act = jnp.maximum(node_pre, 0.0)
    node_normed, node_inverse = layer_norm(matmul(node_act, full_node_second) + full_node_bias)
    node_upstream = node_cotangent * live_nodes
    node_grad_z = norm_back(node_upstream * full_node_gain, node_normed, node_inverse)
    node_grad_pre = outer_back(node_grad_z, full_node_second) * (node_pre > 0).astype(jnp.float32)
    node_input = jnp.concatenate([node_states, aggregate], axis=1)
    node_first_part = inner(node_input, node_grad_pre) * node_scale
    node_second_part = inner(node_act, node_grad_z) * node_scale
    node_grad_input = outer_back(node_grad_pre, full_node_first)
    state_grads = node_upstream + node_grad_input[:, :width]
    edge_upstream = (
        edge_cotangent + jnp.take(node_grad_input[:, width:], target, axis=0)
    ) * live_edges
    edge_grad_z = norm_back(edge_upstream * full_edge_gain, edge_normed, edge_inverse)
    edge_grad_pre = outer_back(edge_grad_z, full_edge_second) * (edge_pre > 0).astype(jnp.float32)
    edge_second_part = inner(edge_act, edge_grad_z) * edge_scale
    extended = jnp.concatenate([node_states, ghosts], axis=0)
    features = jnp.concatenate(
        [edge_states, jnp.take(extended, source, axis=0), jnp.take(extended, target, axis=0)],
        axis=1,
    )
    edge_first_part = inner(features, edge_grad_pre) * edge_scale
    parts = (edge_first_part, edge_second_part, node_first_part, node_second_part)
    blocked = jnp.concatenate(
        [part.reshape(peer_count, -1, width) for part in parts], axis=1
    )
    blocked = blocked.reshape(chip_rows, 2, sub_count, *blocked.shape[1:])
    own = jnp.where(low, blocked[:, 0], blocked[:, 1])
    other = jnp.where(low, blocked[:, 1], blocked[:, 0])
    own = own + lax.ppermute(other, "core", swap)
    own = own.reshape(chip_rows * sub_count, *own.shape[2:])
    reduced = lax.psum_scatter(own, chips, scatter_dimension=0, tiled=True)[0]
    grads = []
    offset = 0
    for rows in [m.shape[0] for m in matrices]:
        grads.append(reduced[offset : offset + rows])
        offset += rows
    edge_first_grad, edge_second_grad, node_first_grad, node_second_grad = grads
    edge_grad_input = outer_back(edge_grad_pre, full_edge_first)
    edge_grads = (edge_cotangent + edge_grad_input[:, :width]) * live_edges
    extended_grads = jax.ops.segment_sum(
        edge_grad_input[:, width : 2 * width], source, node_rows + 4 * ghost
    )
    extended_grads = extended_grads + jax.ops.segment_sum(
        edge_grad_input[:, 2 * width :], target, node_rows + 4 * ghost
    )
    state_grads = state_grads + extended_grads[:node_rows]
    ghost_grads = extended_grads[node_rows:].reshape(4, ghost, width)
    dom_back = padded(jnp.stack([ghost_grads[0], ghost_grads[1]]), ((DOM, 0),), 1)
    sub_back = padded(jnp.stack([ghost_grads[2], ghost_grads[3]]), (("sub", 0),), 1)
    returned = jnp.stack([dom_back[3], dom_back[0], sub_back[3], sub_back[0]])
    state_grads = state_grads + jax.ops.segment_sum(
        returned.reshape(-1, width), lists.reshape(-1), node_rows
    )
    return (
        edge_grads,
        state_grads,
        edge_first_grad,
        edge_second_grad,
        node_first_grad,
        node_second_grad,
    )


def solution(mesh):
    in_specs = (
        P(("groups", "dom", "sub"), None),
        P(("groups", "dom", "sub"), None),
        P(("groups", "dom", "sub"), None),
        P(("groups", "dom", "sub"), None),
        P(("groups", "dom", "sub"), None),
        P(("groups", "dom", "sub"), None),
        P(None, ("groups", "dom", "sub")),
        P(("groups", "dom", "sub"), None, None),
        P(("groups", "dom", "sub")),
        P(("groups", "dom", "sub")),
        P(("dom", "sub"), None),
        P(("dom", "sub"), None),
        P(("dom", "sub")),
        P(("dom", "sub")),
        P(("dom", "sub")),
        P(("dom", "sub"), None),
        P(("dom", "sub"), None),
        P(("dom", "sub")),
        P(("dom", "sub")),
    )
    out_specs = (
        P(("groups", "dom", "sub"), None),
        P(("groups", "dom", "sub"), None),
        P(("groups", "dom", "sub"), None),
        P(("groups", "dom", "sub"), None),
        P(("groups", "dom", "sub"), None),
        P(("groups", "dom", "sub"), None),
    )
    groups, doms, subs = mesh.devices.shape
    split = Mesh(mesh.devices.reshape(groups, doms // 2, 2, subs), ("groups", "domx", "core", "sub"))

    def spec(parts):
        return P(*[tuple(n for a in p for n in (DOM if a == "dom" else (a,))) if isinstance(p, tuple) else p for p in parts])

    in_specs = tuple(spec(s) for s in in_specs)
    out_specs = tuple(spec(s) for s in out_specs)
    return jax.shard_map(shards, mesh=split, in_specs=in_specs, out_specs=out_specs, check_vma=False)
```

```python
import math

import jax
import jax.numpy as jnp
from jax import lax
from jax.sharding import PartitionSpec as P

EPSILON = 1e-05


def padded(cells, sides, width):
    for axis, dim in sides:
        count = lax.axis_size(axis)
        ends = count - 1
        head = lax.slice_in_dim(cells, 0, width, axis=dim)
        tail = lax.slice_in_dim(cells, cells.shape[dim] - width, cells.shape[dim], axis=dim)
        cells = jnp.concatenate(
            [
                lax.ppermute(tail, axis, [(i, (i + 1) % count) for i in range(ends)]),
                cells,
                lax.ppermute(head, axis, [((i + 1) % count, i) for i in range(ends)]),
            ],
            axis=dim,
        )
    return cells


def matmul(left, right):
    return jnp.dot(left, right, precision=lax.Precision.HIGH, preferred_element_type=jnp.float32)


def inner(left, right):
    return lax.dot_general(
        left,
        right,
        (((0,), (0,)), ((), ())),
        precision=lax.Precision.HIGH,
        preferred_element_type=jnp.float32,
    )


def outer_back(left, right):
    return lax.dot_general(
        left,
        right,
        (((1,), (1,)), ((), ())),
        precision=lax.Precision.HIGH,
        preferred_element_type=jnp.float32,
    )


def layer_norm(values):
    center = values - jnp.mean(values, axis=-1, keepdims=True)
    inverse = 1.0 / jnp.sqrt(jnp.mean(center * center, axis=-1, keepdims=True) + EPSILON)
    return (center * inverse, inverse)


def norm_back(upstream, normed, inverse):
    first = jnp.mean(upstream, axis=-1, keepdims=True)
    second = jnp.mean(upstream * normed, axis=-1, keepdims=True)
    return inverse * (upstream - first - normed * second)


def shards(
    node_states,
    node_pre,
    edge_states,
    edge_pre,
    node_cotangent,
    edge_cotangent,
    endpoints,
    send_lists,
    node_counts,
    edge_blocks,
    edge_first,
    edge_second,
    edge_bias,
    edge_gain,
    edge_shift,
    node_first,
    node_second,
    node_bias,
    node_gain,
):
    node_rows, width = node_states.shape
    edge_rows = edge_states.shape[0]
    ghost = send_lists.shape[2]
    dom_count = lax.axis_size("dom")
    sub_count = lax.axis_size("sub")
    peer_count = dom_count * sub_count
    lists = send_lists[0]
    outgoing = jnp.take(node_states, lists.reshape(-1), axis=0).reshape(4, ghost, width)
    dom_side = padded(jnp.stack([outgoing[1], outgoing[0]]), (("dom", 0),), 1)
    sub_side = padded(jnp.stack([outgoing[3], outgoing[2]]), (("sub", 0),), 1)
    ghosts = jnp.stack([dom_side[0], dom_side[3], sub_side[0], sub_side[3]])
    ghosts = ghosts.reshape(4 * ghost, width)
    peers = ("dom", "sub")
    matrices = (edge_first, edge_second, node_first, node_second)
    vectors = jnp.concatenate([edge_bias, edge_gain, edge_shift, node_bias, node_gain])
    vector_rows = -(-vectors.shape[0] // width)
    vectors = jnp.pad(vectors, (0, vector_rows * width - vectors.shape[0])).reshape(vector_rows, width)
    packed = jnp.concatenate(list(matrices) + [vectors], axis=0)
    gathered = lax.all_gather(packed, peers, axis=0, tiled=False)
    pieces = []
    offset = 0
    for rows in [m.shape[0] for m in matrices] + [vector_rows]:
        pieces.append(gathered[:, offset : offset + rows, :])
        offset += rows
    full_edge_first, full_edge_second, full_node_first, full_node_second = (
        piece.reshape(-1, width) for piece in pieces[:4]
    )
    vector_count = edge_bias.shape[0]
    all_vectors = pieces[4].reshape(pieces[4].shape[0], -1)[:, : 5 * vector_count]
    all_vectors = all_vectors.reshape(-1, 5, vector_count).transpose(1, 0, 2).reshape(5, -1)
    full_edge_bias, full_edge_gain, full_edge_shift, full_node_bias, full_node_gain = (
        all_vectors[i] for i in range(5)
    )
    live_nodes = (jnp.arange(node_rows) < node_counts[0]).astype(jnp.float32)[:, None]
    live_edges = (jnp.arange(edge_rows) < edge_blocks[0] * 128).astype(jnp.float32)[:, None]
    source = endpoints[0]
    target = endpoints[1]
    edge_scale = 1.0 / math.sqrt(edge_rows * peer_count)
    node_scale = 1.0 / math.sqrt(node_rows * peer_count)
    edge_act = jnp.maximum(edge_pre, 0.0)
    edge_normed, edge_inverse = layer_norm(matmul(edge_act, full_edge_second) + full_edge_bias)
    message = (edge_normed * full_edge_gain + full_edge_shift) * live_edges
    aggregate = jax.ops.segment_sum(message, target, node_rows)
    node_act = jnp.maximum(node_pre, 0.0)
    node_normed, node_inverse = layer_norm(matmul(node_act, full_node_second) + full_node_bias)
    node_upstream = node_cotangent * live_nodes
    node_grad_z = norm_back(node_upstream * full_node_gain, node_normed, node_inverse)
    node_grad_pre = outer_back(node_grad_z, full_node_second) * (node_pre > 0).astype(jnp.float32)
    node_input = jnp.concatenate([node_states, aggregate], axis=1)
    node_first_part = inner(node_input, node_grad_pre) * node_scale
    node_second_part = inner(node_act, node_grad_z) * node_scale
    node_grad_input = outer_back(node_grad_pre, full_node_first)
    state_grads = node_upstream + node_grad_input[:, :width]
    edge_upstream = (
        edge_cotangent + jnp.take(node_grad_input[:, width:], target, axis=0)
    ) * live_edges
    edge_grad_z = norm_back(edge_upstream * full_edge_gain, edge_normed, edge_inverse)
    edge_grad_pre = outer_back(edge_grad_z, full_edge_second) * (edge_pre > 0).astype(jnp.float32)
    edge_second_part = inner(edge_act, edge_grad_z) * edge_scale
    extended = jnp.concatenate([node_states, ghosts], axis=0)
    features = jnp.concatenate(
        [edge_states, jnp.take(extended, source, axis=0), jnp.take(extended, target, axis=0)],
        axis=1,
    )
    edge_first_part = inner(features, edge_grad_pre) * edge_scale
    parts = (edge_first_part, edge_second_part, node_first_part, node_second_part)
    blocked = jnp.concatenate(
        [part.reshape(peer_count, -1, width) for part in parts], axis=1
    )
    reduced = lax.psum_scatter(blocked, peers, scatter_dimension=0, tiled=True)[0]
    grads = []
    offset = 0
    for rows in [m.shape[0] for m in matrices]:
        grads.append(reduced[offset : offset + rows])
        offset += rows
    edge_first_grad, edge_second_grad, node_first_grad, node_second_grad = grads
    edge_grad_input = outer_back(edge_grad_pre, full_edge_first)
    edge_grads = (edge_cotangent + edge_grad_input[:, :width]) * live_edges
    extended_grads = jax.ops.segment_sum(
        edge_grad_input[:, width : 2 * width], source, node_rows + 4 * ghost
    )
    extended_grads = extended_grads + jax.ops.segment_sum(
        edge_grad_input[:, 2 * width :], target, node_rows + 4 * ghost
    )
    state_grads = state_grads + extended_grads[:node_rows]
    ghost_grads = extended_grads[node_rows:].reshape(4, ghost, width)
    dom_back = padded(jnp.stack([ghost_grads[0], ghost_grads[1]]), (("dom", 0),), 1)
    sub_back = padded(jnp.stack([ghost_grads[2], ghost_grads[3]]), (("sub", 0),), 1)
    returned = jnp.stack([dom_back[3], dom_back[0], sub_back[3], sub_back[0]])
    state_grads = state_grads + jax.ops.segment_sum(
        returned.reshape(-1, width), lists.reshape(-1), node_rows
    )
    return (
        edge_grads,
        state_grads,
        edge_first_grad,
        edge_second_grad,
        node_first_grad,
        node_second_grad,
    )


def solution(mesh):
    in_specs = (
        P(("groups", "dom", "sub"), None),
        P(("groups", "dom", "sub"), None),
        P(("groups", "dom", "sub"), None),
        P(("groups", "dom", "sub"), None),
        P(("groups", "dom", "sub"), None),
        P(("groups", "dom", "sub"), None),
        P(None, ("groups", "dom", "sub")),
        P(("groups", "dom", "sub"), None, None),
        P(("groups", "dom", "sub")),
        P(("groups", "dom", "sub")),
        P(("dom", "sub"), None),
        P(("dom", "sub"), None),
        P(("dom", "sub")),
        P(("dom", "sub")),
        P(("dom", "sub")),
        P(("dom", "sub"), None),
        P(("dom", "sub"), None),
        P(("dom", "sub")),
        P(("dom", "sub")),
    )
    out_specs = (
        P(("groups", "dom", "sub"), None),
        P(("groups", "dom", "sub"), None),
        P(("groups", "dom", "sub"), None),
        P(("groups", "dom", "sub"), None),
        P(("groups", "dom", "sub"), None),
        P(("groups", "dom", "sub"), None),
    )
    return jax.shard_map(shards, mesh=mesh, in_specs=in_specs, out_specs=out_specs, check_vma=False)
```

```python
import math

import jax
import jax.numpy as jnp
from jax import lax
from jax.experimental import pallas as pl
from jax.sharding import PartitionSpec as P

EPSILON = 1e-05


def padded(cells, sides, width):
    for axis, dim in sides:
        count = lax.axis_size(axis)
        ends = count - 1
        head = lax.slice_in_dim(cells, 0, width, axis=dim)
        tail = lax.slice_in_dim(cells, cells.shape[dim] - width, cells.shape[dim], axis=dim)
        cells = jnp.concatenate(
            [
                lax.ppermute(tail, axis, [(i, (i + 1) % count) for i in range(ends)]),
                cells,
                lax.ppermute(head, axis, [((i + 1) % count, i) for i in range(ends)]),
            ],
            axis=dim,
        )
    return cells


def row_offsets(sizes):
    offsets = [0]
    for size in sizes:
        offsets.append(offsets[-1] + size)
    return offsets


def pack_rows(pieces):
    offsets = row_offsets([piece.shape[0] for piece in pieces])

    def kernel(*refs):
        out = refs[-1]
        for index, ref in enumerate(refs[:-1]):
            out[offsets[index] : offsets[index + 1], :] = ref[...]

    return pl.pallas_call(
        kernel,
        out_shape=jax.ShapeDtypeStruct((offsets[-1], pieces[0].shape[1]), pieces[0].dtype),
    )(*pieces)


def split_rows(packed, sizes):
    offsets = row_offsets(sizes)

    def kernel(source, *outs):
        for index, out in enumerate(outs):
            out[...] = source[offsets[index] : offsets[index + 1], :]

    return pl.pallas_call(
        kernel,
        out_shape=tuple(jax.ShapeDtypeStruct((size, packed.shape[1]), packed.dtype) for size in sizes),
    )(packed)


def matmul(left, right):
    return jnp.dot(left, right, precision=lax.Precision.HIGH, preferred_element_type=jnp.float32)


def inner(left, right):
    return lax.dot_general(
        left,
        right,
        (((0,), (0,)), ((), ())),
        precision=lax.Precision.HIGH,
        preferred_element_type=jnp.float32,
    )


def outer_back(left, right):
    return lax.dot_general(
        left,
        right,
        (((1,), (1,)), ((), ())),
        precision=lax.Precision.HIGH,
        preferred_element_type=jnp.float32,
    )


def layer_norm(values):
    center = values - jnp.mean(values, axis=-1, keepdims=True)
    inverse = 1.0 / jnp.sqrt(jnp.mean(center * center, axis=-1, keepdims=True) + EPSILON)
    return (center * inverse, inverse)


def norm_back(upstream, normed, inverse):
    first = jnp.mean(upstream, axis=-1, keepdims=True)
    second = jnp.mean(upstream * normed, axis=-1, keepdims=True)
    return inverse * (upstream - first - normed * second)


def shards(
    node_states,
    node_pre,
    edge_states,
    edge_pre,
    node_cotangent,
    edge_cotangent,
    endpoints,
    send_lists,
    node_counts,
    edge_blocks,
    edge_first,
    edge_second,
    edge_bias,
    edge_gain,
    edge_shift,
    node_first,
    node_second,
    node_bias,
    node_gain,
):
    node_rows, width = node_states.shape
    edge_rows = edge_states.shape[0]
    ghost = send_lists.shape[2]
    dom_count = lax.axis_size("dom")
    sub_count = lax.axis_size("sub")
    peer_count = dom_count * sub_count
    lists = send_lists[0]
    outgoing = jnp.take(node_states, lists.reshape(-1), axis=0).reshape(4, ghost, width)
    dom_side = padded(jnp.stack([outgoing[1], outgoing[0]]), (("dom", 0),), 1)
    sub_side = padded(jnp.stack([outgoing[3], outgoing[2]]), (("sub", 0),), 1)
    ghosts = jnp.stack([dom_side[0], dom_side[3], sub_side[0], sub_side[3]])
    ghosts = ghosts.reshape(4 * ghost, width)
    peers = ("dom", "sub")
    matrices = (edge_first, edge_second, node_first, node_second)
    vectors = jnp.concatenate([edge_bias, edge_gain, edge_shift, node_bias, node_gain])
    vector_rows = -(-vectors.shape[0] // width)
    vectors = jnp.pad(vectors, (0, vector_rows * width - vectors.shape[0])).reshape(vector_rows, width)
    packed = pack_rows(list(matrices) + [vectors])
    gathered = lax.all_gather(packed, peers, axis=0, tiled=False)
    pieces = []
    offset = 0
    for rows in [m.shape[0] for m in matrices] + [vector_rows]:
        pieces.append(gathered[:, offset : offset + rows, :])
        offset += rows
    full_edge_first, full_edge_second, full_node_first, full_node_second = (
        piece.reshape(-1, width) for piece in pieces[:4]
    )
    vector_count = edge_bias.shape[0]
    all_vectors = pieces[4].reshape(pieces[4].shape[0], -1)[:, : 5 * vector_count]
    all_vectors = all_vectors.reshape(-1, 5, vector_count).transpose(1, 0, 2).reshape(5, -1)
    full_edge_bias, full_edge_gain, full_edge_shift, full_node_bias, full_node_gain = (
        all_vectors[i] for i in range(5)
    )
    live_nodes = (jnp.arange(node_rows) < node_counts[0]).astype(jnp.float32)[:, None]
    live_edges = (jnp.arange(edge_rows) < edge_blocks[0] * 128).astype(jnp.float32)[:, None]
    source = endpoints[0]
    target = endpoints[1]
    edge_scale = 1.0 / math.sqrt(edge_rows * peer_count)
    node_scale = 1.0 / math.sqrt(node_rows * peer_count)
    edge_act = jnp.maximum(edge_pre, 0.0)
    edge_normed, edge_inverse = layer_norm(matmul(edge_act, full_edge_second) + full_edge_bias)
    message = (edge_normed * full_edge_gain + full_edge_shift) * live_edges
    aggregate = jax.ops.segment_sum(message, target, node_rows)
    node_act = jnp.maximum(node_pre, 0.0)
    node_normed, node_inverse = layer_norm(matmul(node_act, full_node_second) + full_node_bias)
    node_upstream = node_cotangent * live_nodes
    node_grad_z = norm_back(node_upstream * full_node_gain, node_normed, node_inverse)
    node_grad_pre = outer_back(node_grad_z, full_node_second) * (node_pre > 0).astype(jnp.float32)
    node_input = jnp.concatenate([node_states, aggregate], axis=1)
    node_first_part = inner(node_input, node_grad_pre) * node_scale
    node_second_part = inner(node_act, node_grad_z) * node_scale
    node_grad_input = outer_back(node_grad_pre, full_node_first)
    state_grads = node_upstream + node_grad_input[:, :width]
    edge_upstream = (
        edge_cotangent + jnp.take(node_grad_input[:, width:], target, axis=0)
    ) * live_edges
    edge_grad_z = norm_back(edge_upstream * full_edge_gain, edge_normed, edge_inverse)
    edge_grad_pre = outer_back(edge_grad_z, full_edge_second) * (edge_pre > 0).astype(jnp.float32)
    edge_second_part = inner(edge_act, edge_grad_z) * edge_scale
    extended = jnp.concatenate([node_states, ghosts], axis=0)
    features = jnp.concatenate(
        [edge_states, jnp.take(extended, source, axis=0), jnp.take(extended, target, axis=0)],
        axis=1,
    )
    edge_first_part = inner(features, edge_grad_pre) * edge_scale
    parts = (edge_first_part, edge_second_part, node_first_part, node_second_part)
    blocked = jnp.concatenate(
        [part.reshape(peer_count, -1, width) for part in parts], axis=1
    )
    reduced = lax.psum_scatter(blocked, peers, scatter_dimension=0, tiled=True)[0]
    edge_first_grad, edge_second_grad, node_first_grad, node_second_grad = split_rows(
        reduced, [m.shape[0] for m in matrices]
    )
    edge_grad_input = outer_back(edge_grad_pre, full_edge_first)
    edge_grads = (edge_cotangent + edge_grad_input[:, :width]) * live_edges
    extended_grads = jax.ops.segment_sum(
        edge_grad_input[:, width : 2 * width], source, node_rows + 4 * ghost
    )
    extended_grads = extended_grads + jax.ops.segment_sum(
        edge_grad_input[:, 2 * width :], target, node_rows + 4 * ghost
    )
    state_grads = state_grads + extended_grads[:node_rows]
    ghost_grads = extended_grads[node_rows:].reshape(4, ghost, width)
    dom_back = padded(jnp.stack([ghost_grads[0], ghost_grads[1]]), (("dom", 0),), 1)
    sub_back = padded(jnp.stack([ghost_grads[2], ghost_grads[3]]), (("sub", 0),), 1)
    returned = jnp.stack([dom_back[3], dom_back[0], sub_back[3], sub_back[0]])
    state_grads = state_grads + jax.ops.segment_sum(
        returned.reshape(-1, width), lists.reshape(-1), node_rows
    )
    return (
        edge_grads,
        state_grads,
        edge_first_grad,
        edge_second_grad,
        node_first_grad,
        node_second_grad,
    )


def solution(mesh):
    in_specs = (
        P(("groups", "dom", "sub"), None),
        P(("groups", "dom", "sub"), None),
        P(("groups", "dom", "sub"), None),
        P(("groups", "dom", "sub"), None),
        P(("groups", "dom", "sub"), None),
        P(("groups", "dom", "sub"), None),
        P(None, ("groups", "dom", "sub")),
        P(("groups", "dom", "sub"), None, None),
        P(("groups", "dom", "sub")),
        P(("groups", "dom", "sub")),
        P(("dom", "sub"), None),
        P(("dom", "sub"), None),
        P(("dom", "sub")),
        P(("dom", "sub")),
        P(("dom", "sub")),
        P(("dom", "sub"), None),
        P(("dom", "sub"), None),
        P(("dom", "sub")),
        P(("dom", "sub")),
    )
    out_specs = (
        P(("groups", "dom", "sub"), None),
        P(("groups", "dom", "sub"), None),
        P(("groups", "dom", "sub"), None),
        P(("groups", "dom", "sub"), None),
        P(("groups", "dom", "sub"), None),
        P(("groups", "dom", "sub"), None),
    )
    return jax.shard_map(shards, mesh=mesh, in_specs=in_specs, out_specs=out_specs, check_vma=False)
```

```python
import math

import jax
import jax.numpy as jnp
from jax import lax
from jax.experimental import pallas as pl
from jax.sharding import PartitionSpec as P

EPSILON = 1e-05


def padded(cells, sides, width):
    for axis, dim in sides:
        count = lax.axis_size(axis)
        ends = count - 1
        head = lax.slice_in_dim(cells, 0, width, axis=dim)
        tail = lax.slice_in_dim(cells, cells.shape[dim] - width, cells.shape[dim], axis=dim)
        cells = jnp.concatenate(
            [
                lax.ppermute(tail, axis, [(i, (i + 1) % count) for i in range(ends)]),
                cells,
                lax.ppermute(head, axis, [((i + 1) % count, i) for i in range(ends)]),
            ],
            axis=dim,
        )
    return cells


def row_offsets(sizes):
    offsets = [0]
    for size in sizes:
        offsets.append(offsets[-1] + size)
    return offsets


def pack_rows(pieces, vectors):
    offsets = row_offsets([piece.shape[0] for piece in pieces])
    width = pieces[0].shape[1]
    length = vectors[0].shape[1]
    count = len(pieces)

    def kernel(*refs):
        out = refs[-1]
        for index, ref in enumerate(refs[:count]):
            out[0, offsets[index] : offsets[index + 1], :] = ref[...]
        row = jnp.concatenate(
            [ref[...] for ref in refs[count:-1]]
            + [jnp.zeros((1, width - len(vectors) * length), jnp.float32)],
            axis=1,
        )
        out[0, offsets[-1] : offsets[-1] + 1, :] = row

    return pl.pallas_call(
        kernel,
        out_shape=jax.ShapeDtypeStruct((1, offsets[-1] + 1, width), pieces[0].dtype),
    )(*pieces, *vectors)


def split_rows(packed, sizes):
    offsets = row_offsets(sizes)

    def kernel(source, *outs):
        for index, out in enumerate(outs):
            out[...] = source[offsets[index] : offsets[index + 1], :]

    return pl.pallas_call(
        kernel,
        out_shape=tuple(jax.ShapeDtypeStruct((size, packed.shape[1]), packed.dtype) for size in sizes),
    )(packed)


def matmul(left, right):
    return jnp.dot(left, right, precision=lax.Precision.HIGH, preferred_element_type=jnp.float32)


def inner(left, right):
    return lax.dot_general(
        left,
        right,
        (((0,), (0,)), ((), ())),
        precision=lax.Precision.HIGH,
        preferred_element_type=jnp.float32,
    )


def outer_back(left, right):
    return lax.dot_general(
        left,
        right,
        (((1,), (1,)), ((), ())),
        precision=lax.Precision.HIGH,
        preferred_element_type=jnp.float32,
    )


def layer_norm(values):
    center = values - jnp.mean(values, axis=-1, keepdims=True)
    inverse = 1.0 / jnp.sqrt(jnp.mean(center * center, axis=-1, keepdims=True) + EPSILON)
    return (center * inverse, inverse)


def norm_back(upstream, normed, inverse):
    first = jnp.mean(upstream, axis=-1, keepdims=True)
    second = jnp.mean(upstream * normed, axis=-1, keepdims=True)
    return inverse * (upstream - first - normed * second)


def shards(
    node_states,
    node_pre,
    edge_states,
    edge_pre,
    node_cotangent,
    edge_cotangent,
    endpoints,
    send_lists,
    node_counts,
    edge_blocks,
    edge_first,
    edge_second,
    edge_bias,
    edge_gain,
    edge_shift,
    node_first,
    node_second,
    node_bias,
    node_gain,
):
    node_rows, width = node_states.shape
    edge_rows = edge_states.shape[0]
    ghost = send_lists.shape[2]
    dom_count = lax.axis_size("dom")
    sub_count = lax.axis_size("sub")
    peer_count = dom_count * sub_count
    lists = send_lists[0]
    outgoing = jnp.take(node_states, lists.reshape(-1), axis=0).reshape(4, ghost, width)
    dom_side = padded(jnp.stack([outgoing[1], outgoing[0]]), (("dom", 0),), 1)
    sub_side = padded(jnp.stack([outgoing[3], outgoing[2]]), (("sub", 0),), 1)
    ghosts = jnp.stack([dom_side[0], dom_side[3], sub_side[0], sub_side[3]])
    ghosts = ghosts.reshape(4 * ghost, width)
    peers = ("dom", "sub")
    matrices = (edge_first, edge_second, node_first, node_second)
    vectors = [v.reshape(1, -1) for v in (edge_bias, edge_gain, edge_shift, node_bias, node_gain)]
    vector_rows = 1
    packed = pack_rows(list(matrices), vectors)
    gathered = lax.all_gather(packed, peers, axis=0, tiled=True)
    pieces = []
    offset = 0
    for rows in [m.shape[0] for m in matrices] + [vector_rows]:
        pieces.append(gathered[:, offset : offset + rows, :])
        offset += rows
    full_edge_first, full_edge_second, full_node_first, full_node_second = (
        piece.reshape(-1, width) for piece in pieces[:4]
    )
    vector_count = edge_bias.shape[0]
    all_vectors = pieces[4].reshape(pieces[4].shape[0], -1)[:, : 5 * vector_count]
    all_vectors = all_vectors.reshape(-1, 5, vector_count).transpose(1, 0, 2).reshape(5, -1)
    full_edge_bias, full_edge_gain, full_edge_shift, full_node_bias, full_node_gain = (
        all_vectors[i] for i in range(5)
    )
    live_nodes = (jnp.arange(node_rows) < node_counts[0]).astype(jnp.float32)[:, None]
    live_edges = (jnp.arange(edge_rows) < edge_blocks[0] * 128).astype(jnp.float32)[:, None]
    source = endpoints[0]
    target = endpoints[1]
    edge_scale = 1.0 / math.sqrt(edge_rows * peer_count)
    node_scale = 1.0 / math.sqrt(node_rows * peer_count)
    edge_act = jnp.maximum(edge_pre, 0.0)
    edge_normed, edge_inverse = layer_norm(matmul(edge_act, full_edge_second) + full_edge_bias)
    message = (edge_normed * full_edge_gain + full_edge_shift) * live_edges
    aggregate = jax.ops.segment_sum(message, target, node_rows)
    node_act = jnp.maximum(node_pre, 0.0)
    node_normed, node_inverse = layer_norm(matmul(node_act, full_node_second) + full_node_bias)
    node_upstream = node_cotangent * live_nodes
    node_grad_z = norm_back(node_upstream * full_node_gain, node_normed, node_inverse)
    node_grad_pre = outer_back(node_grad_z, full_node_second) * (node_pre > 0).astype(jnp.float32)
    node_input = jnp.concatenate([node_states, aggregate], axis=1)
    node_first_part = inner(node_input, node_grad_pre) * node_scale
    node_second_part = inner(node_act, node_grad_z) * node_scale
    node_grad_input = outer_back(node_grad_pre, full_node_first)
    state_grads = node_upstream + node_grad_input[:, :width]
    edge_upstream = (
        edge_cotangent + jnp.take(node_grad_input[:, width:], target, axis=0)
    ) * live_edges
    edge_grad_z = norm_back(edge_upstream * full_edge_gain, edge_normed, edge_inverse)
    edge_grad_pre = outer_back(edge_grad_z, full_edge_second) * (edge_pre > 0).astype(jnp.float32)
    edge_second_part = inner(edge_act, edge_grad_z) * edge_scale
    extended = jnp.concatenate([node_states, ghosts], axis=0)
    features = jnp.concatenate(
        [edge_states, jnp.take(extended, source, axis=0), jnp.take(extended, target, axis=0)],
        axis=1,
    )
    edge_first_part = inner(features, edge_grad_pre) * edge_scale
    parts = (edge_first_part, edge_second_part, node_first_part, node_second_part)
    blocked = jnp.concatenate(
        [part.reshape(peer_count, -1, width) for part in parts], axis=1
    )
    reduced = lax.psum_scatter(blocked, peers, scatter_dimension=0, tiled=True)[0]
    edge_first_grad, edge_second_grad, node_first_grad, node_second_grad = split_rows(
        reduced, [m.shape[0] for m in matrices]
    )
    edge_grad_input = outer_back(edge_grad_pre, full_edge_first)
    edge_grads = (edge_cotangent + edge_grad_input[:, :width]) * live_edges
    extended_grads = jax.ops.segment_sum(
        edge_grad_input[:, width : 2 * width], source, node_rows + 4 * ghost
    )
    extended_grads = extended_grads + jax.ops.segment_sum(
        edge_grad_input[:, 2 * width :], target, node_rows + 4 * ghost
    )
    state_grads = state_grads + extended_grads[:node_rows]
    ghost_grads = extended_grads[node_rows:].reshape(4, ghost, width)
    dom_back = padded(jnp.stack([ghost_grads[0], ghost_grads[1]]), (("dom", 0),), 1)
    sub_back = padded(jnp.stack([ghost_grads[2], ghost_grads[3]]), (("sub", 0),), 1)
    returned = jnp.stack([dom_back[3], dom_back[0], sub_back[3], sub_back[0]])
    state_grads = state_grads + jax.ops.segment_sum(
        returned.reshape(-1, width), lists.reshape(-1), node_rows
    )
    return (
        edge_grads,
        state_grads,
        edge_first_grad,
        edge_second_grad,
        node_first_grad,
        node_second_grad,
    )


def solution(mesh):
    in_specs = (
        P(("groups", "dom", "sub"), None),
        P(("groups", "dom", "sub"), None),
        P(("groups", "dom", "sub"), None),
        P(("groups", "dom", "sub"), None),
        P(("groups", "dom", "sub"), None),
        P(("groups", "dom", "sub"), None),
        P(None, ("groups", "dom", "sub")),
        P(("groups", "dom", "sub"), None, None),
        P(("groups", "dom", "sub")),
        P(("groups", "dom", "sub")),
        P(("dom", "sub"), None),
        P(("dom", "sub"), None),
        P(("dom", "sub")),
        P(("dom", "sub")),
        P(("dom", "sub")),
        P(("dom", "sub"), None),
        P(("dom", "sub"), None),
        P(("dom", "sub")),
        P(("dom", "sub")),
    )
    out_specs = (
        P(("groups", "dom", "sub"), None),
        P(("groups", "dom", "sub"), None),
        P(("groups", "dom", "sub"), None),
        P(("groups", "dom", "sub"), None),
        P(("groups", "dom", "sub"), None),
        P(("groups", "dom", "sub"), None),
    )
    return jax.shard_map(shards, mesh=mesh, in_specs=in_specs, out_specs=out_specs, check_vma=False)
```

```python
import math

import jax
import jax.numpy as jnp
from jax import lax
from jax.experimental import pallas as pl
from jax.sharding import PartitionSpec as P

EPSILON = 1e-05


def padded(cells, sides, width):
    for axis, dim in sides:
        count = lax.axis_size(axis)
        ends = count - 1
        head = lax.slice_in_dim(cells, 0, width, axis=dim)
        tail = lax.slice_in_dim(cells, cells.shape[dim] - width, cells.shape[dim], axis=dim)
        cells = jnp.concatenate(
            [
                lax.ppermute(tail, axis, [(i, (i + 1) % count) for i in range(ends)]),
                cells,
                lax.ppermute(head, axis, [((i + 1) % count, i) for i in range(ends)]),
            ],
            axis=dim,
        )
    return cells


def row_offsets(sizes):
    offsets = [0]
    for size in sizes:
        offsets.append(offsets[-1] + size)
    return offsets


def pack_rows(pieces, vectors):
    offsets = row_offsets([piece.shape[0] for piece in pieces])
    width = pieces[0].shape[1]
    length = vectors[0].shape[1]
    count = len(pieces)

    def kernel(*refs):
        out = refs[-1]
        for index, ref in enumerate(refs[:count]):
            out[0, offsets[index] : offsets[index + 1], :] = ref[...]
        row = jnp.concatenate(
            [ref[...] for ref in refs[count:-1]]
            + [jnp.zeros((1, width - len(vectors) * length), jnp.float32)],
            axis=1,
        )
        out[0, offsets[-1] : offsets[-1] + 1, :] = row

    return pl.pallas_call(
        kernel,
        out_shape=jax.ShapeDtypeStruct((1, offsets[-1] + 1, width), pieces[0].dtype),
    )(*pieces, *vectors)


def split_rows(packed, sizes):
    offsets = row_offsets(sizes)

    def kernel(source, *outs):
        for index, out in enumerate(outs):
            out[...] = source[offsets[index] : offsets[index + 1], :]

    return pl.pallas_call(
        kernel,
        out_shape=tuple(jax.ShapeDtypeStruct((size, packed.shape[1]), packed.dtype) for size in sizes),
    )(packed)


def matmul(left, right):
    return jnp.dot(left, right, precision=lax.Precision.HIGH, preferred_element_type=jnp.float32)


def inner(left, right):
    return lax.dot_general(
        left,
        right,
        (((0,), (0,)), ((), ())),
        precision=lax.Precision.HIGH,
        preferred_element_type=jnp.float32,
    )


def outer_back(left, right):
    return lax.dot_general(
        left,
        right,
        (((1,), (1,)), ((), ())),
        precision=lax.Precision.HIGH,
        preferred_element_type=jnp.float32,
    )


def layer_norm(values):
    center = values - jnp.mean(values, axis=-1, keepdims=True)
    inverse = 1.0 / jnp.sqrt(jnp.mean(center * center, axis=-1, keepdims=True) + EPSILON)
    return (center * inverse, inverse)


def norm_back(upstream, normed, inverse):
    first = jnp.mean(upstream, axis=-1, keepdims=True)
    second = jnp.mean(upstream * normed, axis=-1, keepdims=True)
    return inverse * (upstream - first - normed * second)


def shards(
    node_states,
    node_pre,
    edge_states,
    edge_pre,
    node_cotangent,
    edge_cotangent,
    endpoints,
    send_lists,
    node_counts,
    edge_blocks,
    edge_first,
    edge_second,
    edge_bias,
    edge_gain,
    edge_shift,
    node_first,
    node_second,
    node_bias,
    node_gain,
):
    node_rows, width = node_states.shape
    edge_rows = edge_states.shape[0]
    ghost = send_lists.shape[2]
    dom_count = lax.axis_size("dom")
    sub_count = lax.axis_size("sub")
    peer_count = dom_count * sub_count
    lists = send_lists[0]
    outgoing = jnp.take(node_states, lists.reshape(-1), axis=0).reshape(4, ghost, width)
    dom_side = padded(jnp.stack([outgoing[1], outgoing[0]]), (("dom", 0),), 1)
    sub_side = padded(jnp.stack([outgoing[3], outgoing[2]]), (("sub", 0),), 1)
    ghosts = jnp.stack([dom_side[0], dom_side[3], sub_side[0], sub_side[3]])
    ghosts = ghosts.reshape(4 * ghost, width)
    peers = ("dom", "sub")
    matrices = (edge_first, edge_second, node_first, node_second)
    vectors = [v.reshape(1, -1) for v in (edge_bias, edge_gain, edge_shift, node_bias, node_gain)]
    vector_rows = 1
    packed = pack_rows(list(matrices), vectors)
    gathered = lax.all_gather(packed, peers, axis=0, tiled=True)
    pieces = []
    offset = 0
    for rows in [m.shape[0] for m in matrices] + [vector_rows]:
        pieces.append(gathered[:, offset : offset + rows, :])
        offset += rows
    full_edge_first, full_edge_second, full_node_first, full_node_second = (
        piece.reshape(-1, width) for piece in pieces[:4]
    )
    vector_count = edge_bias.shape[0]
    all_vectors = pieces[4].reshape(pieces[4].shape[0], -1)[:, : 5 * vector_count]
    all_vectors = all_vectors.reshape(-1, 5, vector_count).transpose(1, 0, 2).reshape(5, -1)
    full_edge_bias, full_edge_gain, full_edge_shift, full_node_bias, full_node_gain = (
        all_vectors[i] for i in range(5)
    )
    live_nodes = (jnp.arange(node_rows) < node_counts[0]).astype(jnp.float32)[:, None]
    live_edges = (jnp.arange(edge_rows) < edge_blocks[0] * 128).astype(jnp.float32)[:, None]
    source = endpoints[0]
    target = endpoints[1]
    edge_scale = 1.0 / math.sqrt(edge_rows * peer_count)
    node_scale = 1.0 / math.sqrt(node_rows * peer_count)
    edge_act = jnp.maximum(edge_pre, 0.0)
    edge_normed, edge_inverse = layer_norm(matmul(edge_act, full_edge_second) + full_edge_bias)
    message = (edge_normed * full_edge_gain + full_edge_shift) * live_edges
    node_act = jnp.maximum(node_pre, 0.0)
    node_normed, node_inverse = layer_norm(matmul(node_act, full_node_second) + full_node_bias)
    node_upstream = node_cotangent * live_nodes
    node_grad_z = norm_back(node_upstream * full_node_gain, node_normed, node_inverse)
    node_grad_pre = outer_back(node_grad_z, full_node_second) * (node_pre > 0).astype(jnp.float32)
    node_first_part = jnp.concatenate(
        [
            inner(node_states, node_grad_pre),
            inner(message, jnp.take(node_grad_pre, target, axis=0)),
        ],
        axis=0,
    ) * node_scale
    node_second_part = inner(node_act, node_grad_z) * node_scale
    aggregate_grads = outer_back(node_grad_pre, full_node_first[width:])
    edge_upstream = (edge_cotangent + jnp.take(aggregate_grads, target, axis=0)) * live_edges
    edge_grad_z = norm_back(edge_upstream * full_edge_gain, edge_normed, edge_inverse)
    edge_grad_pre = outer_back(edge_grad_z, full_edge_second) * (edge_pre > 0).astype(jnp.float32)
    edge_second_part = inner(edge_act, edge_grad_z) * edge_scale
    extended = jnp.concatenate([node_states, ghosts], axis=0)
    features = jnp.concatenate(
        [edge_states, jnp.take(extended, source, axis=0), jnp.take(extended, target, axis=0)],
        axis=1,
    )
    edge_first_part = inner(features, edge_grad_pre) * edge_scale
    parts = (edge_first_part, edge_second_part, node_first_part, node_second_part)
    blocked = jnp.concatenate(
        [part.reshape(peer_count, -1, width) for part in parts], axis=1
    )
    reduced = lax.psum_scatter(blocked, peers, scatter_dimension=0, tiled=True)[0]
    edge_first_grad, edge_second_grad, node_first_grad, node_second_grad = split_rows(
        reduced, [m.shape[0] for m in matrices]
    )
    edge_grad_input = outer_back(edge_grad_pre, full_edge_first)
    edge_grads = (edge_cotangent + edge_grad_input[:, :width]) * live_edges
    extended_grads = jax.ops.segment_sum(
        edge_grad_input[:, width : 2 * width], source, node_rows + 4 * ghost
    )
    extended_grads = extended_grads + jax.ops.segment_sum(
        edge_grad_input[:, 2 * width :], target, node_rows + 4 * ghost
    )
    state_grads = node_upstream + outer_back(node_grad_pre, full_node_first[:width])
    state_grads = state_grads + extended_grads[:node_rows]
    ghost_grads = extended_grads[node_rows:].reshape(4, ghost, width)
    dom_back = padded(jnp.stack([ghost_grads[0], ghost_grads[1]]), (("dom", 0),), 1)
    sub_back = padded(jnp.stack([ghost_grads[2], ghost_grads[3]]), (("sub", 0),), 1)
    returned = jnp.stack([dom_back[3], dom_back[0], sub_back[3], sub_back[0]])
    state_grads = state_grads + jax.ops.segment_sum(
        returned.reshape(-1, width), lists.reshape(-1), node_rows
    )
    return (
        edge_grads,
        state_grads,
        edge_first_grad,
        edge_second_grad,
        node_first_grad,
        node_second_grad,
    )


def solution(mesh):
    in_specs = (
        P(("groups", "dom", "sub"), None),
        P(("groups", "dom", "sub"), None),
        P(("groups", "dom", "sub"), None),
        P(("groups", "dom", "sub"), None),
        P(("groups", "dom", "sub"), None),
        P(("groups", "dom", "sub"), None),
        P(None, ("groups", "dom", "sub")),
        P(("groups", "dom", "sub"), None, None),
        P(("groups", "dom", "sub")),
        P(("groups", "dom", "sub")),
        P(("dom", "sub"), None),
        P(("dom", "sub"), None),
        P(("dom", "sub")),
        P(("dom", "sub")),
        P(("dom", "sub")),
        P(("dom", "sub"), None),
        P(("dom", "sub"), None),
        P(("dom", "sub")),
        P(("dom", "sub")),
    )
    out_specs = (
        P(("groups", "dom", "sub"), None),
        P(("groups", "dom", "sub"), None),
        P(("groups", "dom", "sub"), None),
        P(("groups", "dom", "sub"), None),
        P(("groups", "dom", "sub"), None),
        P(("groups", "dom", "sub"), None),
    )
    return jax.shard_map(shards, mesh=mesh, in_specs=in_specs, out_specs=out_specs, check_vma=False)
```

```python
import math

import jax
import jax.numpy as jnp
from jax import lax
from jax.experimental import pallas as pl
from jax.sharding import PartitionSpec as P

EPSILON = 1e-05


def padded(cells, sides, width):
    for axis, dim in sides:
        count = lax.axis_size(axis)
        ends = count - 1
        head = lax.slice_in_dim(cells, 0, width, axis=dim)
        tail = lax.slice_in_dim(cells, cells.shape[dim] - width, cells.shape[dim], axis=dim)
        cells = jnp.concatenate(
            [
                lax.ppermute(tail, axis, [(i, (i + 1) % count) for i in range(ends)]),
                cells,
                lax.ppermute(head, axis, [((i + 1) % count, i) for i in range(ends)]),
            ],
            axis=dim,
        )
    return cells


def row_offsets(sizes):
    offsets = [0]
    for size in sizes:
        offsets.append(offsets[-1] + size)
    return offsets


def pack_rows(pieces, vectors):
    offsets = row_offsets([piece.shape[0] for piece in pieces])
    width = pieces[0].shape[1]
    length = vectors[0].shape[1]
    count = len(pieces)

    def kernel(*refs):
        out = refs[-1]
        for index, ref in enumerate(refs[:count]):
            out[0, offsets[index] : offsets[index + 1], :] = ref[...]
        row = jnp.concatenate(
            [ref[...] for ref in refs[count:-1]]
            + [jnp.zeros((1, width - len(vectors) * length), jnp.float32)],
            axis=1,
        )
        out[0, offsets[-1] : offsets[-1] + 1, :] = row

    return pl.pallas_call(
        kernel,
        out_shape=jax.ShapeDtypeStruct((1, offsets[-1] + 1, width), pieces[0].dtype),
    )(*pieces, *vectors)


def split_rows(packed, sizes):
    offsets = row_offsets(sizes)

    def kernel(source, *outs):
        for index, out in enumerate(outs):
            out[...] = source[offsets[index] : offsets[index + 1], :]

    return pl.pallas_call(
        kernel,
        out_shape=tuple(jax.ShapeDtypeStruct((size, packed.shape[1]), packed.dtype) for size in sizes),
    )(packed)


def split_bf16(values):
    high = values.astype(jnp.bfloat16)
    low = (values - high.astype(jnp.float32)).astype(jnp.bfloat16)
    return high, low


def inner_three(left, right):
    left_high, left_low = split_bf16(left.T)
    right_high, right_low = split_bf16(right)

    def dot(a, b):
        return jnp.dot(a, b, preferred_element_type=jnp.float32)

    return dot(left_high, right_high) + dot(left_low, right_high) + dot(left_high, right_low)


def blocked_grads(edge_terms, node_terms, blocks, edge_scale, node_scale):
    terms = [(pieces, right, edge_scale) for pieces, right in edge_terms] + [
        (pieces, right, node_scale) for pieces, right in node_terms
    ]
    rows = [sum(p.shape[1] for p in pieces) // blocks for pieces, _, _ in terms]
    offsets = row_offsets(rows)
    inputs = []
    layout = []
    for pieces, right, scale in terms:
        layout.append((len(inputs), len(pieces), scale))
        inputs.extend(pieces)
        inputs.append(right)
    width = terms[0][1].shape[1]

    def kernel(*refs):
        out = refs[-1]
        for index, (start, count, scale) in enumerate(layout):
            right = refs[start + count][...]
            product = jnp.concatenate(
                [inner_three(refs[start + k][...], right) for k in range(count)], axis=0
            ) * scale
            size = rows[index]
            for block in range(blocks):
                out[block, offsets[index] : offsets[index + 1], :] = product[block * size : (block + 1) * size]

    return pl.pallas_call(
        kernel,
        out_shape=jax.ShapeDtypeStruct((blocks, offsets[-1], width), jnp.float32),
    )(*inputs)


def matmul(left, right):
    return jnp.dot(left, right, precision=lax.Precision.HIGH, preferred_element_type=jnp.float32)


def inner(left, right):
    return lax.dot_general(
        left,
        right,
        (((0,), (0,)), ((), ())),
        precision=lax.Precision.HIGH,
        preferred_element_type=jnp.float32,
    )


def outer_back(left, right):
    return lax.dot_general(
        left,
        right,
        (((1,), (1,)), ((), ())),
        precision=lax.Precision.HIGH,
        preferred_element_type=jnp.float32,
    )


def layer_norm(values):
    center = values - jnp.mean(values, axis=-1, keepdims=True)
    inverse = 1.0 / jnp.sqrt(jnp.mean(center * center, axis=-1, keepdims=True) + EPSILON)
    return (center * inverse, inverse)


def norm_back(upstream, normed, inverse):
    first = jnp.mean(upstream, axis=-1, keepdims=True)
    second = jnp.mean(upstream * normed, axis=-1, keepdims=True)
    return inverse * (upstream - first - normed * second)


def shards(
    node_states,
    node_pre,
    edge_states,
    edge_pre,
    node_cotangent,
    edge_cotangent,
    endpoints,
    send_lists,
    node_counts,
    edge_blocks,
    edge_first,
    edge_second,
    edge_bias,
    edge_gain,
    edge_shift,
    node_first,
    node_second,
    node_bias,
    node_gain,
):
    node_rows, width = node_states.shape
    edge_rows = edge_states.shape[0]
    ghost = send_lists.shape[2]
    dom_count = lax.axis_size("dom")
    sub_count = lax.axis_size("sub")
    peer_count = dom_count * sub_count
    lists = send_lists[0]
    outgoing = jnp.take(node_states, lists.reshape(-1), axis=0).reshape(4, ghost, width)
    dom_side = padded(jnp.stack([outgoing[1], outgoing[0]]), (("dom", 0),), 1)
    sub_side = padded(jnp.stack([outgoing[3], outgoing[2]]), (("sub", 0),), 1)
    ghosts = jnp.stack([dom_side[0], dom_side[3], sub_side[0], sub_side[3]])
    ghosts = ghosts.reshape(4 * ghost, width)
    peers = ("dom", "sub")
    matrices = (edge_first, edge_second, node_first, node_second)
    vectors = [v.reshape(1, -1) for v in (edge_bias, edge_gain, edge_shift, node_bias, node_gain)]
    vector_rows = 1
    packed = pack_rows(list(matrices), vectors)
    gathered = lax.all_gather(packed, peers, axis=0, tiled=True)
    pieces = []
    offset = 0
    for rows in [m.shape[0] for m in matrices] + [vector_rows]:
        pieces.append(gathered[:, offset : offset + rows, :])
        offset += rows
    full_edge_first, full_edge_second, full_node_first, full_node_second = (
        piece.reshape(-1, width) for piece in pieces[:4]
    )
    vector_count = edge_bias.shape[0]
    all_vectors = pieces[4].reshape(pieces[4].shape[0], -1)[:, : 5 * vector_count]
    all_vectors = all_vectors.reshape(-1, 5, vector_count).transpose(1, 0, 2).reshape(5, -1)
    full_edge_bias, full_edge_gain, full_edge_shift, full_node_bias, full_node_gain = (
        all_vectors[i] for i in range(5)
    )
    live_nodes = (jnp.arange(node_rows) < node_counts[0]).astype(jnp.float32)[:, None]
    live_edges = (jnp.arange(edge_rows) < edge_blocks[0] * 128).astype(jnp.float32)[:, None]
    source = endpoints[0]
    target = endpoints[1]
    edge_scale = 1.0 / math.sqrt(edge_rows * peer_count)
    node_scale = 1.0 / math.sqrt(node_rows * peer_count)
    edge_act = jnp.maximum(edge_pre, 0.0)
    edge_normed, edge_inverse = layer_norm(matmul(edge_act, full_edge_second) + full_edge_bias)
    message = (edge_normed * full_edge_gain + full_edge_shift) * live_edges
    aggregate = jax.ops.segment_sum(message, target, node_rows)
    node_act = jnp.maximum(node_pre, 0.0)
    node_normed, node_inverse = layer_norm(matmul(node_act, full_node_second) + full_node_bias)
    node_upstream = node_cotangent * live_nodes
    node_grad_z = norm_back(node_upstream * full_node_gain, node_normed, node_inverse)
    node_grad_pre = outer_back(node_grad_z, full_node_second) * (node_pre > 0).astype(jnp.float32)
    node_terms = [([node_states, aggregate], node_grad_pre), ([node_act], node_grad_z)]
    node_grad_input = outer_back(node_grad_pre, full_node_first)
    state_grads = node_upstream + node_grad_input[:, :width]
    edge_upstream = (
        edge_cotangent + jnp.take(node_grad_input[:, width:], target, axis=0)
    ) * live_edges
    edge_grad_z = norm_back(edge_upstream * full_edge_gain, edge_normed, edge_inverse)
    edge_grad_pre = outer_back(edge_grad_z, full_edge_second) * (edge_pre > 0).astype(jnp.float32)
    extended = jnp.concatenate([node_states, ghosts], axis=0)
    sent = jnp.take(extended, source, axis=0)
    received = jnp.take(extended, target, axis=0)
    edge_terms = [([edge_states, sent, received], edge_grad_pre), ([edge_act], edge_grad_z)]
    if all(m.shape[0] % 8 == 0 for m in matrices):
        blocked = blocked_grads(edge_terms, node_terms, peer_count, edge_scale, node_scale)
    else:
        parts = [
            jnp.concatenate([inner(p, right) for p in pieces], axis=0) * scale
            for (pieces, right), scale in zip(
                edge_terms + node_terms, [edge_scale] * 2 + [node_scale] * 2
            )
        ]
        blocked = jnp.concatenate(
            [part.reshape(peer_count, -1, width) for part in parts], axis=1
        )
    reduced = lax.psum_scatter(blocked, peers, scatter_dimension=0, tiled=True)[0]
    edge_first_grad, edge_second_grad, node_first_grad, node_second_grad = split_rows(
        reduced, [m.shape[0] for m in matrices]
    )
    edge_grad_input = outer_back(edge_grad_pre, full_edge_first)
    edge_grads = (edge_cotangent + edge_grad_input[:, :width]) * live_edges
    extended_grads = jax.ops.segment_sum(
        edge_grad_input[:, width : 2 * width], source, node_rows + 4 * ghost
    )
    extended_grads = extended_grads + jax.ops.segment_sum(
        edge_grad_input[:, 2 * width :], target, node_rows + 4 * ghost
    )
    state_grads = state_grads + extended_grads[:node_rows]
    ghost_grads = extended_grads[node_rows:].reshape(4, ghost, width)
    dom_back = padded(jnp.stack([ghost_grads[0], ghost_grads[1]]), (("dom", 0),), 1)
    sub_back = padded(jnp.stack([ghost_grads[2], ghost_grads[3]]), (("sub", 0),), 1)
    returned = jnp.stack([dom_back[3], dom_back[0], sub_back[3], sub_back[0]])
    state_grads = state_grads + jax.ops.segment_sum(
        returned.reshape(-1, width), lists.reshape(-1), node_rows
    )
    return (
        edge_grads,
        state_grads,
        edge_first_grad,
        edge_second_grad,
        node_first_grad,
        node_second_grad,
    )


def solution(mesh):
    in_specs = (
        P(("groups", "dom", "sub"), None),
        P(("groups", "dom", "sub"), None),
        P(("groups", "dom", "sub"), None),
        P(("groups", "dom", "sub"), None),
        P(("groups", "dom", "sub"), None),
        P(("groups", "dom", "sub"), None),
        P(None, ("groups", "dom", "sub")),
        P(("groups", "dom", "sub"), None, None),
        P(("groups", "dom", "sub")),
        P(("groups", "dom", "sub")),
        P(("dom", "sub"), None),
        P(("dom", "sub"), None),
        P(("dom", "sub")),
        P(("dom", "sub")),
        P(("dom", "sub")),
        P(("dom", "sub"), None),
        P(("dom", "sub"), None),
        P(("dom", "sub")),
        P(("dom", "sub")),
    )
    out_specs = (
        P(("groups", "dom", "sub"), None),
        P(("groups", "dom", "sub"), None),
        P(("groups", "dom", "sub"), None),
        P(("groups", "dom", "sub"), None),
        P(("groups", "dom", "sub"), None),
        P(("groups", "dom", "sub"), None),
    )
    return jax.shard_map(shards, mesh=mesh, in_specs=in_specs, out_specs=out_specs, check_vma=False)
```

```python
import math

import jax
import jax.numpy as jnp
from jax import lax
from jax.experimental import pallas as pl
from jax.experimental.pallas import tpu as pltpu
from jax.sharding import PartitionSpec as P

EPSILON = 1e-05


def padded(cells, sides, width):
    for axis, dim in sides:
        count = lax.axis_size(axis)
        ends = count - 1
        head = lax.slice_in_dim(cells, 0, width, axis=dim)
        tail = lax.slice_in_dim(cells, cells.shape[dim] - width, cells.shape[dim], axis=dim)
        cells = jnp.concatenate(
            [
                lax.ppermute(tail, axis, [(i, (i + 1) % count) for i in range(ends)]),
                cells,
                lax.ppermute(head, axis, [((i + 1) % count, i) for i in range(ends)]),
            ],
            axis=dim,
        )
    return cells


def row_offsets(sizes):
    offsets = [0]
    for size in sizes:
        offsets.append(offsets[-1] + size)
    return offsets


def pack_rows(pieces, vectors):
    offsets = row_offsets([piece.shape[0] for piece in pieces])
    width = pieces[0].shape[1]
    length = vectors[0].shape[1]
    count = len(pieces)

    def kernel(*refs):
        out = refs[-1]
        for index, ref in enumerate(refs[:count]):
            out[0, offsets[index] : offsets[index + 1], :] = ref[...]
        row = jnp.concatenate(
            [ref[...] for ref in refs[count:-1]]
            + [jnp.zeros((1, width - len(vectors) * length), jnp.float32)],
            axis=1,
        )
        out[0, offsets[-1] : offsets[-1] + 1, :] = row

    return pl.pallas_call(
        kernel,
        out_shape=jax.ShapeDtypeStruct((1, offsets[-1] + 1, width), pieces[0].dtype),
    )(*pieces, *vectors)


def split_rows(packed, sizes):
    offsets = row_offsets(sizes)

    def kernel(source, *outs):
        for index, out in enumerate(outs):
            out[...] = source[offsets[index] : offsets[index + 1], :]

    return pl.pallas_call(
        kernel,
        out_shape=tuple(jax.ShapeDtypeStruct((size, packed.shape[1]), packed.dtype) for size in sizes),
    )(packed)


def split_bf16(values):
    high = values.astype(jnp.bfloat16)
    low = (values - high.astype(jnp.float32)).astype(jnp.bfloat16)
    return high, low


def inner_three(left, right):
    left_high, left_low = split_bf16(left.T)
    right_high, right_low = split_bf16(right)

    def dot(a, b):
        return jnp.dot(a, b, preferred_element_type=jnp.float32)

    return dot(left_high, right_high) + dot(left_low, right_high) + dot(left_high, right_low)


def blocked_grads(edge_terms, node_terms, blocks, edge_scale, node_scale):
    terms = [(pieces, right, edge_scale) for pieces, right in edge_terms] + [
        (pieces, right, node_scale) for pieces, right in node_terms
    ]
    rows = [sum(p.shape[1] for p in pieces) // blocks for pieces, _, _ in terms]
    offsets = row_offsets(rows)
    inputs = []
    layout = []
    for pieces, right, scale in terms:
        layout.append((len(inputs), len(pieces), scale))
        inputs.extend(pieces)
        inputs.append(right)
    width = terms[0][1].shape[1]

    order = sorted(range(len(terms)), key=lambda index: -rows[index] * terms[index][1].shape[0])
    count_in = len(inputs)

    def kernel(*refs):
        sources = refs[:count_in]
        out = refs[count_in]
        staged = refs[count_in + 1 : 2 * count_in + 1]
        results = refs[2 * count_in + 1 : 2 * count_in + 1 + len(terms)]
        in_sems = refs[-2]
        out_sems = refs[-1]
        loads = [
            pltpu.make_async_copy(sources[k], staged[k], in_sems.at[k]) for k in range(count_in)
        ]
        for load in loads:
            load.start()
        stores = []
        for index in order:
            start, count, scale = layout[index]
            for k in range(start, start + count + 1):
                loads[k].wait()
            right = staged[start + count][...]
            product = jnp.concatenate(
                [inner_three(staged[start + k][...], right) for k in range(count)], axis=0
            ) * scale
            results[index][...] = product.reshape(blocks, rows[index], width)
            store = pltpu.make_async_copy(
                results[index], out.at[:, offsets[index] : offsets[index + 1], :], out_sems.at[index]
            )
            store.start()
            stores.append(store)
        for store in stores:
            store.wait()

    any_space = pl.BlockSpec(memory_space=pl.ANY)
    return pl.pallas_call(
        kernel,
        out_shape=jax.ShapeDtypeStruct((blocks, offsets[-1], width), jnp.float32),
        in_specs=[any_space] * count_in,
        out_specs=any_space,
        scratch_shapes=[pltpu.VMEM(x.shape, x.dtype) for x in inputs]
        + [pltpu.VMEM((blocks, size, width), jnp.float32) for size in rows]
        + [pltpu.SemaphoreType.DMA((count_in,)), pltpu.SemaphoreType.DMA((len(terms),))],
    )(*inputs)


def matmul(left, right):
    return jnp.dot(left, right, precision=lax.Precision.HIGH, preferred_element_type=jnp.float32)


def inner(left, right):
    return lax.dot_general(
        left,
        right,
        (((0,), (0,)), ((), ())),
        precision=lax.Precision.HIGH,
        preferred_element_type=jnp.float32,
    )


def outer_back(left, right):
    return lax.dot_general(
        left,
        right,
        (((1,), (1,)), ((), ())),
        precision=lax.Precision.HIGH,
        preferred_element_type=jnp.float32,
    )


def layer_norm(values):
    center = values - jnp.mean(values, axis=-1, keepdims=True)
    inverse = 1.0 / jnp.sqrt(jnp.mean(center * center, axis=-1, keepdims=True) + EPSILON)
    return (center * inverse, inverse)


def norm_back(upstream, normed, inverse):
    first = jnp.mean(upstream, axis=-1, keepdims=True)
    second = jnp.mean(upstream * normed, axis=-1, keepdims=True)
    return inverse * (upstream - first - normed * second)


def shards(
    node_states,
    node_pre,
    edge_states,
    edge_pre,
    node_cotangent,
    edge_cotangent,
    endpoints,
    send_lists,
    node_counts,
    edge_blocks,
    edge_first,
    edge_second,
    edge_bias,
    edge_gain,
    edge_shift,
    node_first,
    node_second,
    node_bias,
    node_gain,
):
    node_rows, width = node_states.shape
    edge_rows = edge_states.shape[0]
    ghost = send_lists.shape[2]
    dom_count = lax.axis_size("dom")
    sub_count = lax.axis_size("sub")
    peer_count = dom_count * sub_count
    lists = send_lists[0]
    outgoing = jnp.take(node_states, lists.reshape(-1), axis=0).reshape(4, ghost, width)
    dom_side = padded(jnp.stack([outgoing[1], outgoing[0]]), (("dom", 0),), 1)
    sub_side = padded(jnp.stack([outgoing[3], outgoing[2]]), (("sub", 0),), 1)
    ghosts = jnp.stack([dom_side[0], dom_side[3], sub_side[0], sub_side[3]])
    ghosts = ghosts.reshape(4 * ghost, width)
    peers = ("dom", "sub")
    matrices = (edge_first, edge_second, node_first, node_second)
    vectors = [v.reshape(1, -1) for v in (edge_bias, edge_gain, edge_shift, node_bias, node_gain)]
    vector_rows = 1
    packed = pack_rows(list(matrices), vectors)
    gathered = lax.all_gather(packed, peers, axis=0, tiled=True)
    pieces = []
    offset = 0
    for rows in [m.shape[0] for m in matrices] + [vector_rows]:
        pieces.append(gathered[:, offset : offset + rows, :])
        offset += rows
    full_edge_first, full_edge_second, full_node_first, full_node_second = (
        piece.reshape(-1, width) for piece in pieces[:4]
    )
    vector_count = edge_bias.shape[0]
    all_vectors = pieces[4].reshape(pieces[4].shape[0], -1)[:, : 5 * vector_count]
    all_vectors = all_vectors.reshape(-1, 5, vector_count).transpose(1, 0, 2).reshape(5, -1)
    full_edge_bias, full_edge_gain, full_edge_shift, full_node_bias, full_node_gain = (
        all_vectors[i] for i in range(5)
    )
    live_nodes = (jnp.arange(node_rows) < node_counts[0]).astype(jnp.float32)[:, None]
    live_edges = (jnp.arange(edge_rows) < edge_blocks[0] * 128).astype(jnp.float32)[:, None]
    source = endpoints[0]
    target = endpoints[1]
    edge_scale = 1.0 / math.sqrt(edge_rows * peer_count)
    node_scale = 1.0 / math.sqrt(node_rows * peer_count)
    edge_act = jnp.maximum(edge_pre, 0.0)
    edge_normed, edge_inverse = layer_norm(matmul(edge_act, full_edge_second) + full_edge_bias)
    message = (edge_normed * full_edge_gain + full_edge_shift) * live_edges
    aggregate = jax.ops.segment_sum(message, target, node_rows)
    node_act = jnp.maximum(node_pre, 0.0)
    node_normed, node_inverse = layer_norm(matmul(node_act, full_node_second) + full_node_bias)
    node_upstream = node_cotangent * live_nodes
    node_grad_z = norm_back(node_upstream * full_node_gain, node_normed, node_inverse)
    node_grad_pre = outer_back(node_grad_z, full_node_second) * (node_pre > 0).astype(jnp.float32)
    node_terms = [([node_states, aggregate], node_grad_pre), ([node_act], node_grad_z)]
    node_grad_input = outer_back(node_grad_pre, full_node_first)
    state_grads = node_upstream + node_grad_input[:, :width]
    edge_upstream = (
        edge_cotangent + jnp.take(node_grad_input[:, width:], target, axis=0)
    ) * live_edges
    edge_grad_z = norm_back(edge_upstream * full_edge_gain, edge_normed, edge_inverse)
    edge_grad_pre = outer_back(edge_grad_z, full_edge_second) * (edge_pre > 0).astype(jnp.float32)
    extended = jnp.concatenate([node_states, ghosts], axis=0)
    sent = jnp.take(extended, source, axis=0)
    received = jnp.take(extended, target, axis=0)
    edge_terms = [([edge_states, sent, received], edge_grad_pre), ([edge_act], edge_grad_z)]
    if all(m.shape[0] % 8 == 0 for m in matrices):
        blocked = blocked_grads(edge_terms, node_terms, peer_count, edge_scale, node_scale)
    else:
        parts = [
            jnp.concatenate([inner(p, right) for p in pieces], axis=0) * scale
            for (pieces, right), scale in zip(
                edge_terms + node_terms, [edge_scale] * 2 + [node_scale] * 2
            )
        ]
        blocked = jnp.concatenate(
            [part.reshape(peer_count, -1, width) for part in parts], axis=1
        )
    reduced = lax.psum_scatter(blocked, peers, scatter_dimension=0, tiled=True)[0]
    edge_first_grad, edge_second_grad, node_first_grad, node_second_grad = split_rows(
        reduced, [m.shape[0] for m in matrices]
    )
    edge_grad_input = outer_back(edge_grad_pre, full_edge_first)
    edge_grads = (edge_cotangent + edge_grad_input[:, :width]) * live_edges
    extended_grads = jax.ops.segment_sum(
        edge_grad_input[:, width : 2 * width], source, node_rows + 4 * ghost
    )
    extended_grads = extended_grads + jax.ops.segment_sum(
        edge_grad_input[:, 2 * width :], target, node_rows + 4 * ghost
    )
    state_grads = state_grads + extended_grads[:node_rows]
    ghost_grads = extended_grads[node_rows:].reshape(4, ghost, width)
    dom_back = padded(jnp.stack([ghost_grads[0], ghost_grads[1]]), (("dom", 0),), 1)
    sub_back = padded(jnp.stack([ghost_grads[2], ghost_grads[3]]), (("sub", 0),), 1)
    returned = jnp.stack([dom_back[3], dom_back[0], sub_back[3], sub_back[0]])
    state_grads = state_grads + jax.ops.segment_sum(
        returned.reshape(-1, width), lists.reshape(-1), node_rows
    )
    return (
        edge_grads,
        state_grads,
        edge_first_grad,
        edge_second_grad,
        node_first_grad,
        node_second_grad,
    )


def solution(mesh):
    in_specs = (
        P(("groups", "dom", "sub"), None),
        P(("groups", "dom", "sub"), None),
        P(("groups", "dom", "sub"), None),
        P(("groups", "dom", "sub"), None),
        P(("groups", "dom", "sub"), None),
        P(("groups", "dom", "sub"), None),
        P(None, ("groups", "dom", "sub")),
        P(("groups", "dom", "sub"), None, None),
        P(("groups", "dom", "sub")),
        P(("groups", "dom", "sub")),
        P(("dom", "sub"), None),
        P(("dom", "sub"), None),
        P(("dom", "sub")),
        P(("dom", "sub")),
        P(("dom", "sub")),
        P(("dom", "sub"), None),
        P(("dom", "sub"), None),
        P(("dom", "sub")),
        P(("dom", "sub")),
    )
    out_specs = (
        P(("groups", "dom", "sub"), None),
        P(("groups", "dom", "sub"), None),
        P(("groups", "dom", "sub"), None),
        P(("groups", "dom", "sub"), None),
        P(("groups", "dom", "sub"), None),
        P(("groups", "dom", "sub"), None),
    )
    return jax.shard_map(shards, mesh=mesh, in_specs=in_specs, out_specs=out_specs, check_vma=False)
```

```python
import math

import jax
import jax.numpy as jnp
from jax import lax
from jax.experimental import pallas as pl
from jax.experimental.pallas import tpu as pltpu
from jax.sharding import PartitionSpec as P

EPSILON = 1e-05


def padded(cells, sides, width):
    for axis, dim in sides:
        count = lax.axis_size(axis)
        ends = count - 1
        head = lax.slice_in_dim(cells, 0, width, axis=dim)
        tail = lax.slice_in_dim(cells, cells.shape[dim] - width, cells.shape[dim], axis=dim)
        cells = jnp.concatenate(
            [
                lax.ppermute(tail, axis, [(i, (i + 1) % count) for i in range(ends)]),
                cells,
                lax.ppermute(head, axis, [((i + 1) % count, i) for i in range(ends)]),
            ],
            axis=dim,
        )
    return cells


def row_offsets(sizes):
    offsets = [0]
    for size in sizes:
        offsets.append(offsets[-1] + size)
    return offsets


def pack_rows(pieces, vectors):
    offsets = row_offsets([piece.shape[0] for piece in pieces])
    width = pieces[0].shape[1]
    length = vectors[0].shape[1]
    count = len(pieces)

    def kernel(*refs):
        out = refs[-1]
        for index, ref in enumerate(refs[:count]):
            out[0, offsets[index] : offsets[index + 1], :] = ref[...]
        row = jnp.concatenate(
            [ref[...] for ref in refs[count:-1]]
            + [jnp.zeros((1, width - len(vectors) * length), jnp.float32)],
            axis=1,
        )
        out[0, offsets[-1] : offsets[-1] + 1, :] = row

    return pl.pallas_call(
        kernel,
        out_shape=jax.ShapeDtypeStruct((1, offsets[-1] + 1, width), pieces[0].dtype),
    )(*pieces, *vectors)


def split_rows(packed, sizes):
    offsets = row_offsets(sizes)

    def kernel(source, *outs):
        for index, out in enumerate(outs):
            out[...] = source[offsets[index] : offsets[index + 1], :]

    return pl.pallas_call(
        kernel,
        out_shape=tuple(jax.ShapeDtypeStruct((size, packed.shape[1]), packed.dtype) for size in sizes),
    )(packed)


def split_bf16(values):
    high = values.astype(jnp.bfloat16)
    low = (values - high.astype(jnp.float32)).astype(jnp.bfloat16)
    return high, low


def inner_three(left, right_high, right_low):
    left_high, left_low = split_bf16(left)

    def dot(a, b):
        return lax.dot_general(
            a, b, (((0,), (0,)), ((), ())), preferred_element_type=jnp.float32
        )

    return dot(left_high, right_high) + dot(left_low, right_high) + dot(left_high, right_low)


def blocked_grads(edge_terms, node_terms, blocks, edge_scale, node_scale):
    terms = [(pieces, right, edge_scale) for pieces, right in edge_terms] + [
        (pieces, right, node_scale) for pieces, right in node_terms
    ]
    rows = [sum(p.shape[1] for p in pieces) // blocks for pieces, _, _ in terms]
    offsets = row_offsets(rows)
    inputs = []
    layout = []
    for pieces, right, scale in terms:
        layout.append((len(inputs), len(pieces), scale))
        inputs.extend(pieces)
        inputs.append(right)
    width = terms[0][1].shape[1]

    order = sorted(range(len(terms)), key=lambda index: -rows[index] * terms[index][1].shape[0])
    count_in = len(inputs)

    def kernel(*refs):
        sources = refs[:count_in]
        out = refs[count_in]
        staged = refs[count_in + 1 : 2 * count_in + 1]
        results = refs[2 * count_in + 1 : 2 * count_in + 1 + len(terms)]
        in_sems = refs[-2]
        out_sems = refs[-1]
        loads = [
            pltpu.make_async_copy(sources[k], staged[k], in_sems.at[k]) for k in range(count_in)
        ]
        for load in loads:
            load.start()
        stores = []
        for index in order:
            start, count, scale = layout[index]
            for k in range(start, start + count + 1):
                loads[k].wait()
            right_high, right_low = split_bf16(staged[start + count][...])
            product = jnp.concatenate(
                [inner_three(staged[start + k][...], right_high, right_low) for k in range(count)],
                axis=0,
            ) * scale
            results[index][...] = product.reshape(blocks, rows[index], width)
            store = pltpu.make_async_copy(
                results[index], out.at[:, offsets[index] : offsets[index + 1], :], out_sems.at[index]
            )
            store.start()
            stores.append(store)
        for store in stores:
            store.wait()

    any_space = pl.BlockSpec(memory_space=pl.ANY)
    return pl.pallas_call(
        kernel,
        out_shape=jax.ShapeDtypeStruct((blocks, offsets[-1], width), jnp.float32),
        in_specs=[any_space] * count_in,
        out_specs=any_space,
        scratch_shapes=[pltpu.VMEM(x.shape, x.dtype) for x in inputs]
        + [pltpu.VMEM((blocks, size, width), jnp.float32) for size in rows]
        + [pltpu.SemaphoreType.DMA((count_in,)), pltpu.SemaphoreType.DMA((len(terms),))],
    )(*inputs)


def matmul(left, right):
    return jnp.dot(left, right, precision=lax.Precision.HIGH, preferred_element_type=jnp.float32)


def inner(left, right):
    return lax.dot_general(
        left,
        right,
        (((0,), (0,)), ((), ())),
        precision=lax.Precision.HIGH,
        preferred_element_type=jnp.float32,
    )


def outer_back(left, right):
    return lax.dot_general(
        left,
        right,
        (((1,), (1,)), ((), ())),
        precision=lax.Precision.HIGH,
        preferred_element_type=jnp.float32,
    )


def layer_norm(values):
    center = values - jnp.mean(values, axis=-1, keepdims=True)
    inverse = 1.0 / jnp.sqrt(jnp.mean(center * center, axis=-1, keepdims=True) + EPSILON)
    return (center * inverse, inverse)


def norm_back(upstream, normed, inverse):
    first = jnp.mean(upstream, axis=-1, keepdims=True)
    second = jnp.mean(upstream * normed, axis=-1, keepdims=True)
    return inverse * (upstream - first - normed * second)


def shards(
    node_states,
    node_pre,
    edge_states,
    edge_pre,
    node_cotangent,
    edge_cotangent,
    endpoints,
    send_lists,
    node_counts,
    edge_blocks,
    edge_first,
    edge_second,
    edge_bias,
    edge_gain,
    edge_shift,
    node_first,
    node_second,
    node_bias,
    node_gain,
):
    node_rows, width = node_states.shape
    edge_rows = edge_states.shape[0]
    ghost = send_lists.shape[2]
    dom_count = lax.axis_size("dom")
    sub_count = lax.axis_size("sub")
    peer_count = dom_count * sub_count
    lists = send_lists[0]
    outgoing = jnp.take(node_states, lists.reshape(-1), axis=0).reshape(4, ghost, width)
    dom_side = padded(jnp.stack([outgoing[1], outgoing[0]]), (("dom", 0),), 1)
    sub_side = padded(jnp.stack([outgoing[3], outgoing[2]]), (("sub", 0),), 1)
    ghosts = jnp.stack([dom_side[0], dom_side[3], sub_side[0], sub_side[3]])
    ghosts = ghosts.reshape(4 * ghost, width)
    peers = ("dom", "sub")
    matrices = (edge_first, edge_second, node_first, node_second)
    vectors = [v.reshape(1, -1) for v in (edge_bias, edge_gain, edge_shift, node_bias, node_gain)]
    vector_rows = 1
    packed = pack_rows(list(matrices), vectors)
    gathered = lax.all_gather(packed, peers, axis=0, tiled=True)
    pieces = []
    offset = 0
    for rows in [m.shape[0] for m in matrices] + [vector_rows]:
        pieces.append(gathered[:, offset : offset + rows, :])
        offset += rows
    full_edge_first, full_edge_second, full_node_first, full_node_second = (
        piece.reshape(-1, width) for piece in pieces[:4]
    )
    vector_count = edge_bias.shape[0]
    all_vectors = pieces[4].reshape(pieces[4].shape[0], -1)[:, : 5 * vector_count]
    all_vectors = all_vectors.reshape(-1, 5, vector_count).transpose(1, 0, 2).reshape(5, -1)
    full_edge_bias, full_edge_gain, full_edge_shift, full_node_bias, full_node_gain = (
        all_vectors[i] for i in range(5)
    )
    live_nodes = (jnp.arange(node_rows) < node_counts[0]).astype(jnp.float32)[:, None]
    live_edges = (jnp.arange(edge_rows) < edge_blocks[0] * 128).astype(jnp.float32)[:, None]
    source = endpoints[0]
    target = endpoints[1]
    edge_scale = 1.0 / math.sqrt(edge_rows * peer_count)
    node_scale = 1.0 / math.sqrt(node_rows * peer_count)
    edge_act = jnp.maximum(edge_pre, 0.0)
    edge_normed, edge_inverse = layer_norm(matmul(edge_act, full_edge_second) + full_edge_bias)
    message = (edge_normed * full_edge_gain + full_edge_shift) * live_edges
    aggregate = jax.ops.segment_sum(message, target, node_rows)
    node_act = jnp.maximum(node_pre, 0.0)
    node_normed, node_inverse = layer_norm(matmul(node_act, full_node_second) + full_node_bias)
    node_upstream = node_cotangent * live_nodes
    node_grad_z = norm_back(node_upstream * full_node_gain, node_normed, node_inverse)
    node_grad_pre = outer_back(node_grad_z, full_node_second) * (node_pre > 0).astype(jnp.float32)
    node_terms = [([node_states, aggregate], node_grad_pre), ([node_act], node_grad_z)]
    node_grad_input = outer_back(node_grad_pre, full_node_first)
    state_grads = node_upstream + node_grad_input[:, :width]
    edge_upstream = (
        edge_cotangent + jnp.take(node_grad_input[:, width:], target, axis=0)
    ) * live_edges
    edge_grad_z = norm_back(edge_upstream * full_edge_gain, edge_normed, edge_inverse)
    edge_grad_pre = outer_back(edge_grad_z, full_edge_second) * (edge_pre > 0).astype(jnp.float32)
    extended = jnp.concatenate([node_states, ghosts], axis=0)
    sent = jnp.take(extended, source, axis=0)
    received = jnp.take(extended, target, axis=0)
    edge_terms = [([edge_states, sent, received], edge_grad_pre), ([edge_act], edge_grad_z)]
    if all(m.shape[0] % 8 == 0 for m in matrices):
        blocked = blocked_grads(edge_terms, node_terms, peer_count, edge_scale, node_scale)
    else:
        parts = [
            jnp.concatenate([inner(p, right) for p in pieces], axis=0) * scale
            for (pieces, right), scale in zip(
                edge_terms + node_terms, [edge_scale] * 2 + [node_scale] * 2
            )
        ]
        blocked = jnp.concatenate(
            [part.reshape(peer_count, -1, width) for part in parts], axis=1
        )
    reduced = lax.psum_scatter(blocked, peers, scatter_dimension=0, tiled=True)[0]
    edge_first_grad, edge_second_grad, node_first_grad, node_second_grad = split_rows(
        reduced, [m.shape[0] for m in matrices]
    )
    edge_grad_input = outer_back(edge_grad_pre, full_edge_first)
    edge_grads = (edge_cotangent + edge_grad_input[:, :width]) * live_edges
    extended_grads = jax.ops.segment_sum(
        edge_grad_input[:, width : 2 * width], source, node_rows + 4 * ghost
    )
    extended_grads = extended_grads + jax.ops.segment_sum(
        edge_grad_input[:, 2 * width :], target, node_rows + 4 * ghost
    )
    state_grads = state_grads + extended_grads[:node_rows]
    ghost_grads = extended_grads[node_rows:].reshape(4, ghost, width)
    dom_back = padded(jnp.stack([ghost_grads[0], ghost_grads[1]]), (("dom", 0),), 1)
    sub_back = padded(jnp.stack([ghost_grads[2], ghost_grads[3]]), (("sub", 0),), 1)
    returned = jnp.stack([dom_back[3], dom_back[0], sub_back[3], sub_back[0]])
    state_grads = state_grads + jax.ops.segment_sum(
        returned.reshape(-1, width), lists.reshape(-1), node_rows
    )
    return (
        edge_grads,
        state_grads,
        edge_first_grad,
        edge_second_grad,
        node_first_grad,
        node_second_grad,
    )


def solution(mesh):
    in_specs = (
        P(("groups", "dom", "sub"), None),
        P(("groups", "dom", "sub"), None),
        P(("groups", "dom", "sub"), None),
        P(("groups", "dom", "sub"), None),
        P(("groups", "dom", "sub"), None),
        P(("groups", "dom", "sub"), None),
        P(None, ("groups", "dom", "sub")),
        P(("groups", "dom", "sub"), None, None),
        P(("groups", "dom", "sub")),
        P(("groups", "dom", "sub")),
        P(("dom", "sub"), None),
        P(("dom", "sub"), None),
        P(("dom", "sub")),
        P(("dom", "sub")),
        P(("dom", "sub")),
        P(("dom", "sub"), None),
        P(("dom", "sub"), None),
        P(("dom", "sub")),
        P(("dom", "sub")),
    )
    out_specs = (
        P(("groups", "dom", "sub"), None),
        P(("groups", "dom", "sub"), None),
        P(("groups", "dom", "sub"), None),
        P(("groups", "dom", "sub"), None),
        P(("groups", "dom", "sub"), None),
        P(("groups", "dom", "sub"), None),
    )
    return jax.shard_map(shards, mesh=mesh, in_specs=in_specs, out_specs=out_specs, check_vma=False)
```

```python
import math

import jax
import jax.numpy as jnp
from jax import lax
from jax.experimental import pallas as pl
from jax.experimental.pallas import tpu as pltpu
from jax.sharding import PartitionSpec as P

EPSILON = 1e-05


def padded(cells, sides, width):
    for axis, dim in sides:
        count = lax.axis_size(axis)
        ends = count - 1
        head = lax.slice_in_dim(cells, 0, width, axis=dim)
        tail = lax.slice_in_dim(cells, cells.shape[dim] - width, cells.shape[dim], axis=dim)
        cells = jnp.concatenate(
            [
                lax.ppermute(tail, axis, [(i, (i + 1) % count) for i in range(ends)]),
                cells,
                lax.ppermute(head, axis, [((i + 1) % count, i) for i in range(ends)]),
            ],
            axis=dim,
        )
    return cells


def row_offsets(sizes):
    offsets = [0]
    for size in sizes:
        offsets.append(offsets[-1] + size)
    return offsets


def pack_rows(pieces, vectors):
    offsets = row_offsets([piece.shape[0] for piece in pieces])
    width = pieces[0].shape[1]
    length = vectors[0].shape[1]
    count = len(pieces)

    def kernel(*refs):
        out = refs[-1]
        for index, ref in enumerate(refs[:count]):
            out[0, offsets[index] : offsets[index + 1], :] = ref[...]
        row = jnp.concatenate(
            [ref[...] for ref in refs[count:-1]]
            + [jnp.zeros((1, width - len(vectors) * length), jnp.float32)],
            axis=1,
        )
        out[0, offsets[-1] : offsets[-1] + 1, :] = row

    return pl.pallas_call(
        kernel,
        out_shape=jax.ShapeDtypeStruct((1, offsets[-1] + 1, width), pieces[0].dtype),
    )(*pieces, *vectors)


def split_rows(packed, sizes):
    offsets = row_offsets(sizes)

    def kernel(source, *outs):
        for index, out in enumerate(outs):
            out[...] = source[offsets[index] : offsets[index + 1], :]

    return pl.pallas_call(
        kernel,
        out_shape=tuple(jax.ShapeDtypeStruct((size, packed.shape[1]), packed.dtype) for size in sizes),
    )(packed)


def split_bf16(values):
    high = values.astype(jnp.bfloat16)
    low = (values - high.astype(jnp.float32)).astype(jnp.bfloat16)
    return high, low


def inner_three(left, right_high, right_low):
    left_high, left_low = split_bf16(left)

    def dot(a, b):
        return lax.dot_general(
            a, b, (((0,), (0,)), ((), ())), preferred_element_type=jnp.float32
        )

    return dot(left_high, right_high) + dot(left_low, right_high) + dot(left_high, right_low)


def blocked_grads(edge_terms, node_terms, blocks, edge_scale, node_scale):
    terms = [(pairs, edge_scale) for pairs in edge_terms] + [(pairs, node_scale) for pairs in node_terms]
    rows = [sum(left.shape[1] for left, _ in pairs) // blocks for pairs, _ in terms]
    offsets = row_offsets(rows)
    inputs = []
    layout = []
    for pairs, scale in terms:
        layout.append((len(inputs), len(pairs), scale))
        for pair in pairs:
            inputs.extend(pair)
    width = terms[0][0][0][1].shape[1]

    order = sorted(range(len(terms)), key=lambda index: -rows[index] * terms[index][0][0][0].shape[0])
    count_in = len(inputs)

    def kernel(*refs):
        sources = refs[:count_in]
        out = refs[count_in]
        staged = refs[count_in + 1 : 2 * count_in + 1]
        results = refs[2 * count_in + 1 : 2 * count_in + 1 + len(terms)]
        in_sems = refs[-2]
        out_sems = refs[-1]
        loads = [
            pltpu.make_async_copy(sources[k], staged[k], in_sems.at[k]) for k in range(count_in)
        ]
        for load in loads:
            load.start()
        stores = []
        for index in order:
            start, count, scale = layout[index]
            for k in range(start, start + 2 * count):
                loads[k].wait()
            pieces = []
            for k in range(count):
                right_high, right_low = split_bf16(staged[start + 2 * k + 1][...])
                pieces.append(inner_three(staged[start + 2 * k][...], right_high, right_low))
            product = jnp.concatenate(pieces, axis=0) * scale
            results[index][...] = product.reshape(blocks, rows[index], width)
            store = pltpu.make_async_copy(
                results[index], out.at[:, offsets[index] : offsets[index + 1], :], out_sems.at[index]
            )
            store.start()
            stores.append(store)
        for store in stores:
            store.wait()

    any_space = pl.BlockSpec(memory_space=pl.ANY)
    return pl.pallas_call(
        kernel,
        out_shape=jax.ShapeDtypeStruct((blocks, offsets[-1], width), jnp.float32),
        in_specs=[any_space] * count_in,
        out_specs=any_space,
        scratch_shapes=[pltpu.VMEM(x.shape, x.dtype) for x in inputs]
        + [pltpu.VMEM((blocks, size, width), jnp.float32) for size in rows]
        + [pltpu.SemaphoreType.DMA((count_in,)), pltpu.SemaphoreType.DMA((len(terms),))],
    )(*inputs)


def matmul(left, right):
    return jnp.dot(left, right, precision=lax.Precision.HIGH, preferred_element_type=jnp.float32)


def inner(left, right):
    return lax.dot_general(
        left,
        right,
        (((0,), (0,)), ((), ())),
        precision=lax.Precision.HIGH,
        preferred_element_type=jnp.float32,
    )


def outer_back(left, right):
    return lax.dot_general(
        left,
        right,
        (((1,), (1,)), ((), ())),
        precision=lax.Precision.HIGH,
        preferred_element_type=jnp.float32,
    )


def layer_norm(values):
    center = values - jnp.mean(values, axis=-1, keepdims=True)
    inverse = 1.0 / jnp.sqrt(jnp.mean(center * center, axis=-1, keepdims=True) + EPSILON)
    return (center * inverse, inverse)


def norm_back(upstream, normed, inverse):
    first = jnp.mean(upstream, axis=-1, keepdims=True)
    second = jnp.mean(upstream * normed, axis=-1, keepdims=True)
    return inverse * (upstream - first - normed * second)


def shards(
    node_states,
    node_pre,
    edge_states,
    edge_pre,
    node_cotangent,
    edge_cotangent,
    endpoints,
    send_lists,
    node_counts,
    edge_blocks,
    edge_first,
    edge_second,
    edge_bias,
    edge_gain,
    edge_shift,
    node_first,
    node_second,
    node_bias,
    node_gain,
):
    node_rows, width = node_states.shape
    edge_rows = edge_states.shape[0]
    ghost = send_lists.shape[2]
    dom_count = lax.axis_size("dom")
    sub_count = lax.axis_size("sub")
    peer_count = dom_count * sub_count
    lists = send_lists[0]
    outgoing = jnp.take(node_states, lists.reshape(-1), axis=0).reshape(4, ghost, width)
    dom_side = padded(jnp.stack([outgoing[1], outgoing[0]]), (("dom", 0),), 1)
    sub_side = padded(jnp.stack([outgoing[3], outgoing[2]]), (("sub", 0),), 1)
    ghosts = jnp.stack([dom_side[0], dom_side[3], sub_side[0], sub_side[3]])
    ghosts = ghosts.reshape(4 * ghost, width)
    peers = ("dom", "sub")
    matrices = (edge_first, edge_second, node_first, node_second)
    vectors = [v.reshape(1, -1) for v in (edge_bias, edge_gain, edge_shift, node_bias, node_gain)]
    vector_rows = 1
    packed = pack_rows(list(matrices), vectors)
    gathered = lax.all_gather(packed, peers, axis=0, tiled=True)
    pieces = []
    offset = 0
    for rows in [m.shape[0] for m in matrices] + [vector_rows]:
        pieces.append(gathered[:, offset : offset + rows, :])
        offset += rows
    full_edge_first, full_edge_second, full_node_first, full_node_second = (
        piece.reshape(-1, width) for piece in pieces[:4]
    )
    vector_count = edge_bias.shape[0]
    all_vectors = pieces[4].reshape(pieces[4].shape[0], -1)[:, : 5 * vector_count]
    all_vectors = all_vectors.reshape(-1, 5, vector_count).transpose(1, 0, 2).reshape(5, -1)
    full_edge_bias, full_edge_gain, full_edge_shift, full_node_bias, full_node_gain = (
        all_vectors[i] for i in range(5)
    )
    live_nodes = (jnp.arange(node_rows) < node_counts[0]).astype(jnp.float32)[:, None]
    live_edges = (jnp.arange(edge_rows) < edge_blocks[0] * 128).astype(jnp.float32)[:, None]
    source = endpoints[0]
    target = endpoints[1]
    edge_scale = 1.0 / math.sqrt(edge_rows * peer_count)
    node_scale = 1.0 / math.sqrt(node_rows * peer_count)
    edge_act = jnp.maximum(edge_pre, 0.0)
    edge_normed, edge_inverse = layer_norm(matmul(edge_act, full_edge_second) + full_edge_bias)
    message = (edge_normed * full_edge_gain + full_edge_shift) * live_edges
    node_act = jnp.maximum(node_pre, 0.0)
    node_normed, node_inverse = layer_norm(matmul(node_act, full_node_second) + full_node_bias)
    node_upstream = node_cotangent * live_nodes
    node_grad_z = norm_back(node_upstream * full_node_gain, node_normed, node_inverse)
    node_grad_pre = outer_back(node_grad_z, full_node_second) * (node_pre > 0).astype(jnp.float32)
    node_terms = [
        [(node_states, node_grad_pre), (message, jnp.take(node_grad_pre, target, axis=0))],
        [(node_act, node_grad_z)],
    ]
    node_grad_input = outer_back(node_grad_pre, full_node_first)
    state_grads = node_upstream + node_grad_input[:, :width]
    edge_upstream = (
        edge_cotangent + jnp.take(node_grad_input[:, width:], target, axis=0)
    ) * live_edges
    edge_grad_z = norm_back(edge_upstream * full_edge_gain, edge_normed, edge_inverse)
    edge_grad_pre = outer_back(edge_grad_z, full_edge_second) * (edge_pre > 0).astype(jnp.float32)
    extended = jnp.concatenate([node_states, ghosts], axis=0)
    sent = jnp.take(extended, source, axis=0)
    received = jnp.take(extended, target, axis=0)
    edge_terms = [
        [(edge_states, edge_grad_pre), (sent, edge_grad_pre), (received, edge_grad_pre)],
        [(edge_act, edge_grad_z)],
    ]
    if all(m.shape[0] % 8 == 0 for m in matrices):
        blocked = blocked_grads(edge_terms, node_terms, peer_count, edge_scale, node_scale)
    else:
        parts = [
            jnp.concatenate([inner(left, right) for left, right in pairs], axis=0) * scale
            for pairs, scale in zip(edge_terms + node_terms, [edge_scale] * 2 + [node_scale] * 2)
        ]
        blocked = jnp.concatenate(
            [part.reshape(peer_count, -1, width) for part in parts], axis=1
        )
    reduced = lax.psum_scatter(blocked, peers, scatter_dimension=0, tiled=True)[0]
    edge_first_grad, edge_second_grad, node_first_grad, node_second_grad = split_rows(
        reduced, [m.shape[0] for m in matrices]
    )
    edge_grad_input = outer_back(edge_grad_pre, full_edge_first)
    edge_grads = (edge_cotangent + edge_grad_input[:, :width]) * live_edges
    extended_grads = jax.ops.segment_sum(
        edge_grad_input[:, width : 2 * width], source, node_rows + 4 * ghost
    )
    extended_grads = extended_grads + jax.ops.segment_sum(
        edge_grad_input[:, 2 * width :], target, node_rows + 4 * ghost
    )
    state_grads = state_grads + extended_grads[:node_rows]
    ghost_grads = extended_grads[node_rows:].reshape(4, ghost, width)
    dom_back = padded(jnp.stack([ghost_grads[0], ghost_grads[1]]), (("dom", 0),), 1)
    sub_back = padded(jnp.stack([ghost_grads[2], ghost_grads[3]]), (("sub", 0),), 1)
    returned = jnp.stack([dom_back[3], dom_back[0], sub_back[3], sub_back[0]])
    state_grads = state_grads + jax.ops.segment_sum(
        returned.reshape(-1, width), lists.reshape(-1), node_rows
    )
    return (
        edge_grads,
        state_grads,
        edge_first_grad,
        edge_second_grad,
        node_first_grad,
        node_second_grad,
    )


def solution(mesh):
    in_specs = (
        P(("groups", "dom", "sub"), None),
        P(("groups", "dom", "sub"), None),
        P(("groups", "dom", "sub"), None),
        P(("groups", "dom", "sub"), None),
        P(("groups", "dom", "sub"), None),
        P(("groups", "dom", "sub"), None),
        P(None, ("groups", "dom", "sub")),
        P(("groups", "dom", "sub"), None, None),
        P(("groups", "dom", "sub")),
        P(("groups", "dom", "sub")),
        P(("dom", "sub"), None),
        P(("dom", "sub"), None),
        P(("dom", "sub")),
        P(("dom", "sub")),
        P(("dom", "sub")),
        P(("dom", "sub"), None),
        P(("dom", "sub"), None),
        P(("dom", "sub")),
        P(("dom", "sub")),
    )
    out_specs = (
        P(("groups", "dom", "sub"), None),
        P(("groups", "dom", "sub"), None),
        P(("groups", "dom", "sub"), None),
        P(("groups", "dom", "sub"), None),
        P(("groups", "dom", "sub"), None),
        P(("groups", "dom", "sub"), None),
    )
    return jax.shard_map(shards, mesh=mesh, in_specs=in_specs, out_specs=out_specs, check_vma=False)
```

```python
import math

import jax
import jax.numpy as jnp
from jax import lax
from jax.experimental import pallas as pl
from jax.experimental.pallas import tpu as pltpu
from jax.sharding import PartitionSpec as P

EPSILON = 1e-05


def padded(cells, sides, width):
    for axis, dim in sides:
        count = lax.axis_size(axis)
        ends = count - 1
        head = lax.slice_in_dim(cells, 0, width, axis=dim)
        tail = lax.slice_in_dim(cells, cells.shape[dim] - width, cells.shape[dim], axis=dim)
        cells = jnp.concatenate(
            [
                lax.ppermute(tail, axis, [(i, (i + 1) % count) for i in range(ends)]),
                cells,
                lax.ppermute(head, axis, [((i + 1) % count, i) for i in range(ends)]),
            ],
            axis=dim,
        )
    return cells


def row_offsets(sizes):
    offsets = [0]
    for size in sizes:
        offsets.append(offsets[-1] + size)
    return offsets


def pack_rows(pieces, vectors):
    offsets = row_offsets([piece.shape[0] for piece in pieces])
    width = pieces[0].shape[1]
    length = vectors[0].shape[1]
    count = len(pieces)

    def kernel(*refs):
        out = refs[-1]
        for index, ref in enumerate(refs[:count]):
            out[0, offsets[index] : offsets[index + 1], :] = ref[...]
        row = jnp.concatenate(
            [ref[...] for ref in refs[count:-1]]
            + [jnp.zeros((1, width - len(vectors) * length), jnp.float32)],
            axis=1,
        )
        out[0, offsets[-1] : offsets[-1] + 1, :] = row

    return pl.pallas_call(
        kernel,
        out_shape=jax.ShapeDtypeStruct((1, offsets[-1] + 1, width), pieces[0].dtype),
    )(*pieces, *vectors)


def split_rows(packed, sizes):
    offsets = row_offsets(sizes)

    def kernel(source, *outs):
        for index, out in enumerate(outs):
            out[...] = source[offsets[index] : offsets[index + 1], :]

    return pl.pallas_call(
        kernel,
        out_shape=tuple(jax.ShapeDtypeStruct((size, packed.shape[1]), packed.dtype) for size in sizes),
    )(packed)


def split_bf16(values):
    high = values.astype(jnp.bfloat16)
    low = (values - high.astype(jnp.float32)).astype(jnp.bfloat16)
    return high, low


def inner_three(left, right_high, right_low):
    left_high, left_low = split_bf16(left)

    def dot(a, b):
        return lax.dot_general(
            a, b, (((0,), (0,)), ((), ())), preferred_element_type=jnp.float32
        )

    return dot(left_high, right_high) + dot(left_low, right_high) + dot(left_high, right_low)


def blocked_grads(edge_terms, node_terms, blocks, edge_scale, node_scale):
    terms = [(pairs, edge_scale) for pairs in edge_terms] + [(pairs, node_scale) for pairs in node_terms]
    rows = [sum(left.shape[1] for left, _ in pairs) // blocks for pairs, _ in terms]
    offsets = row_offsets(rows)
    inputs = []
    layout = []
    for pairs, scale in terms:
        layout.append((len(inputs), len(pairs), scale))
        for pair in pairs:
            inputs.extend(pair)
    width = terms[0][0][0][1].shape[1]

    order = sorted(range(len(terms)), key=lambda index: -rows[index] * terms[index][0][0][0].shape[0])
    count_in = len(inputs)

    def kernel(*refs):
        sources = refs[:count_in]
        out = refs[count_in]
        staged = refs[count_in + 1 : 2 * count_in + 1]
        results = refs[2 * count_in + 1 : 2 * count_in + 1 + len(terms)]
        in_sems = refs[-2]
        out_sems = refs[-1]
        loads = [
            pltpu.make_async_copy(sources[k], staged[k], in_sems.at[k]) for k in range(count_in)
        ]
        for load in loads:
            load.start()
        stores = []
        for index in order:
            start, count, scale = layout[index]
            for k in range(start, start + 2 * count):
                loads[k].wait()
            pieces = []
            for k in range(count):
                right_high, right_low = split_bf16(staged[start + 2 * k + 1][...])
                pieces.append(inner_three(staged[start + 2 * k][...], right_high, right_low))
            product = jnp.concatenate(pieces, axis=0) * scale
            results[index][...] = product.reshape(blocks, rows[index], width)
            store = pltpu.make_async_copy(
                results[index], out.at[:, offsets[index] : offsets[index + 1], :], out_sems.at[index]
            )
            store.start()
            stores.append(store)
        for store in stores:
            store.wait()

    any_space = pl.BlockSpec(memory_space=pl.ANY)
    return pl.pallas_call(
        kernel,
        out_shape=jax.ShapeDtypeStruct((blocks, offsets[-1], width), jnp.float32),
        in_specs=[any_space] * count_in,
        out_specs=any_space,
        scratch_shapes=[pltpu.VMEM(x.shape, x.dtype) for x in inputs]
        + [pltpu.VMEM((blocks, size, width), jnp.float32) for size in rows]
        + [pltpu.SemaphoreType.DMA((count_in,)), pltpu.SemaphoreType.DMA((len(terms),))],
    )(*inputs)


def matmul(left, right):
    return jnp.dot(left, right, precision=lax.Precision.HIGH, preferred_element_type=jnp.float32)


def inner(left, right):
    return lax.dot_general(
        left,
        right,
        (((0,), (0,)), ((), ())),
        precision=lax.Precision.HIGH,
        preferred_element_type=jnp.float32,
    )


def outer_back(left, right):
    return lax.dot_general(
        left,
        right,
        (((1,), (1,)), ((), ())),
        precision=lax.Precision.HIGH,
        preferred_element_type=jnp.float32,
    )


def layer_norm(values):
    center = values - jnp.mean(values, axis=-1, keepdims=True)
    inverse = 1.0 / jnp.sqrt(jnp.mean(center * center, axis=-1, keepdims=True) + EPSILON)
    return (center * inverse, inverse)


def norm_back(upstream, normed, inverse):
    first = jnp.mean(upstream, axis=-1, keepdims=True)
    second = jnp.mean(upstream * normed, axis=-1, keepdims=True)
    return inverse * (upstream - first - normed * second)


def shards(
    node_states,
    node_pre,
    edge_states,
    edge_pre,
    node_cotangent,
    edge_cotangent,
    endpoints,
    send_lists,
    node_counts,
    edge_blocks,
    edge_first,
    edge_second,
    edge_bias,
    edge_gain,
    edge_shift,
    node_first,
    node_second,
    node_bias,
    node_gain,
):
    node_rows, width = node_states.shape
    edge_rows = edge_states.shape[0]
    ghost = send_lists.shape[2]
    dom_count = lax.axis_size("dom")
    sub_count = lax.axis_size("sub")
    peer_count = dom_count * sub_count
    lists = send_lists[0]
    outgoing = jnp.take(node_states, lists.reshape(-1), axis=0).reshape(4, ghost, width)
    dom_side = padded(jnp.stack([outgoing[1], outgoing[0]]), (("dom", 0),), 1)
    sub_side = padded(jnp.stack([outgoing[3], outgoing[2]]), (("sub", 0),), 1)
    ghosts = jnp.stack([dom_side[0], dom_side[3], sub_side[0], sub_side[3]])
    ghosts = ghosts.reshape(4 * ghost, width)
    peers = ("dom", "sub")
    matrices = (edge_first, edge_second, node_first, node_second)
    vectors = [v.reshape(1, -1) for v in (edge_bias, edge_gain, edge_shift, node_bias, node_gain)]
    vector_rows = 1
    packed = pack_rows(list(matrices), vectors)
    gathered = lax.all_gather(packed, peers, axis=0, tiled=True)
    pieces = []
    offset = 0
    for rows in [m.shape[0] for m in matrices] + [vector_rows]:
        pieces.append(gathered[:, offset : offset + rows, :])
        offset += rows
    full_edge_first, full_edge_second, full_node_first, full_node_second = (
        piece.reshape(-1, width) for piece in pieces[:4]
    )
    vector_count = edge_bias.shape[0]
    all_vectors = pieces[4].reshape(pieces[4].shape[0], -1)[:, : 5 * vector_count]
    all_vectors = all_vectors.reshape(-1, 5, vector_count).transpose(1, 0, 2).reshape(5, -1)
    full_edge_bias, full_edge_gain, full_edge_shift, full_node_bias, full_node_gain = (
        all_vectors[i] for i in range(5)
    )
    live_nodes = (jnp.arange(node_rows) < node_counts[0]).astype(jnp.float32)[:, None]
    live_edges = (jnp.arange(edge_rows) < edge_blocks[0] * 128).astype(jnp.float32)[:, None]
    source = endpoints[0]
    target = endpoints[1]
    edge_scale = 1.0 / math.sqrt(edge_rows * peer_count)
    node_scale = 1.0 / math.sqrt(node_rows * peer_count)
    edge_act = jnp.maximum(edge_pre, 0.0)
    edge_normed, edge_inverse = layer_norm(matmul(edge_act, full_edge_second) + full_edge_bias)
    message = (edge_normed * full_edge_gain + full_edge_shift) * live_edges
    node_act = jnp.maximum(node_pre, 0.0)
    node_normed, node_inverse = layer_norm(matmul(node_act, full_node_second) + full_node_bias)
    node_upstream = node_cotangent * live_nodes
    node_grad_z = norm_back(node_upstream * full_node_gain, node_normed, node_inverse)
    node_grad_pre = outer_back(node_grad_z, full_node_second) * (node_pre > 0).astype(jnp.float32)
    node_terms = [
        [(node_states, node_grad_pre), (message, jnp.take(node_grad_pre, target, axis=0))],
        [(node_act, node_grad_z)],
    ]
    aggregate_grads = outer_back(node_grad_pre, full_node_first[width:])
    edge_upstream = (edge_cotangent + jnp.take(aggregate_grads, target, axis=0)) * live_edges
    edge_grad_z = norm_back(edge_upstream * full_edge_gain, edge_normed, edge_inverse)
    edge_grad_pre = outer_back(edge_grad_z, full_edge_second) * (edge_pre > 0).astype(jnp.float32)
    extended = jnp.concatenate([node_states, ghosts], axis=0)
    sent = jnp.take(extended, source, axis=0)
    received = jnp.take(extended, target, axis=0)
    edge_terms = [
        [(edge_states, edge_grad_pre), (sent, edge_grad_pre), (received, edge_grad_pre)],
        [(edge_act, edge_grad_z)],
    ]
    if all(m.shape[0] % 8 == 0 for m in matrices):
        blocked = blocked_grads(edge_terms, node_terms, peer_count, edge_scale, node_scale)
    else:
        parts = [
            jnp.concatenate([inner(left, right) for left, right in pairs], axis=0) * scale
            for pairs, scale in zip(edge_terms + node_terms, [edge_scale] * 2 + [node_scale] * 2)
        ]
        blocked = jnp.concatenate(
            [part.reshape(peer_count, -1, width) for part in parts], axis=1
        )
    blocked, late_grad_pre = lax.optimization_barrier((blocked, node_grad_pre))
    reduced = lax.psum_scatter(blocked, peers, scatter_dimension=0, tiled=True)[0]
    state_grads = node_upstream + outer_back(late_grad_pre, full_node_first[:width])
    edge_first_grad, edge_second_grad, node_first_grad, node_second_grad = split_rows(
        reduced, [m.shape[0] for m in matrices]
    )
    edge_grad_input = outer_back(edge_grad_pre, full_edge_first)
    edge_grads = (edge_cotangent + edge_grad_input[:, :width]) * live_edges
    extended_grads = jax.ops.segment_sum(
        edge_grad_input[:, width : 2 * width], source, node_rows + 4 * ghost
    )
    extended_grads = extended_grads + jax.ops.segment_sum(
        edge_grad_input[:, 2 * width :], target, node_rows + 4 * ghost
    )
    state_grads = state_grads + extended_grads[:node_rows]
    ghost_grads = extended_grads[node_rows:].reshape(4, ghost, width)
    dom_back = padded(jnp.stack([ghost_grads[0], ghost_grads[1]]), (("dom", 0),), 1)
    sub_back = padded(jnp.stack([ghost_grads[2], ghost_grads[3]]), (("sub", 0),), 1)
    returned = jnp.stack([dom_back[3], dom_back[0], sub_back[3], sub_back[0]])
    state_grads = state_grads + jax.ops.segment_sum(
        returned.reshape(-1, width), lists.reshape(-1), node_rows
    )
    return (
        edge_grads,
        state_grads,
        edge_first_grad,
        edge_second_grad,
        node_first_grad,
        node_second_grad,
    )


def solution(mesh):
    in_specs = (
        P(("groups", "dom", "sub"), None),
        P(("groups", "dom", "sub"), None),
        P(("groups", "dom", "sub"), None),
        P(("groups", "dom", "sub"), None),
        P(("groups", "dom", "sub"), None),
        P(("groups", "dom", "sub"), None),
        P(None, ("groups", "dom", "sub")),
        P(("groups", "dom", "sub"), None, None),
        P(("groups", "dom", "sub")),
        P(("groups", "dom", "sub")),
        P(("dom", "sub"), None),
        P(("dom", "sub"), None),
        P(("dom", "sub")),
        P(("dom", "sub")),
        P(("dom", "sub")),
        P(("dom", "sub"), None),
        P(("dom", "sub"), None),
        P(("dom", "sub")),
        P(("dom", "sub")),
    )
    out_specs = (
        P(("groups", "dom", "sub"), None),
        P(("groups", "dom", "sub"), None),
        P(("groups", "dom", "sub"), None),
        P(("groups", "dom", "sub"), None),
        P(("groups", "dom", "sub"), None),
        P(("groups", "dom", "sub"), None),
    )
    return jax.shard_map(shards, mesh=mesh, in_specs=in_specs, out_specs=out_specs, check_vma=False)
```

```python
import math

import jax
import jax.numpy as jnp
from jax import lax
from jax.experimental import pallas as pl
from jax.experimental.pallas import tpu as pltpu
from jax.sharding import PartitionSpec as P

EPSILON = 1e-05


def padded(cells, sides, width):
    for axis, dim in sides:
        count = lax.axis_size(axis)
        ends = count - 1
        head = lax.slice_in_dim(cells, 0, width, axis=dim)
        tail = lax.slice_in_dim(cells, cells.shape[dim] - width, cells.shape[dim], axis=dim)
        cells = jnp.concatenate(
            [
                lax.ppermute(tail, axis, [(i, (i + 1) % count) for i in range(ends)]),
                cells,
                lax.ppermute(head, axis, [((i + 1) % count, i) for i in range(ends)]),
            ],
            axis=dim,
        )
    return cells


def row_offsets(sizes):
    offsets = [0]
    for size in sizes:
        offsets.append(offsets[-1] + size)
    return offsets


def pack_rows(pieces, vectors):
    offsets = row_offsets([piece.shape[0] for piece in pieces])
    width = pieces[0].shape[1]
    length = vectors[0].shape[1]
    count = len(pieces)

    def kernel(*refs):
        out = refs[-1]
        for index, ref in enumerate(refs[:count]):
            out[0, offsets[index] : offsets[index + 1], :] = ref[...]
        row = jnp.concatenate(
            [ref[...] for ref in refs[count:-1]]
            + [jnp.zeros((1, width - len(vectors) * length), jnp.float32)],
            axis=1,
        )
        out[0, offsets[-1] : offsets[-1] + 1, :] = row

    return pl.pallas_call(
        kernel,
        out_shape=jax.ShapeDtypeStruct((1, offsets[-1] + 1, width), pieces[0].dtype),
    )(*pieces, *vectors)


def split_rows(packed, sizes):
    offsets = row_offsets(sizes)

    def kernel(source, *outs):
        for index, out in enumerate(outs):
            out[...] = source[offsets[index] : offsets[index + 1], :]

    return pl.pallas_call(
        kernel,
        out_shape=tuple(jax.ShapeDtypeStruct((size, packed.shape[1]), packed.dtype) for size in sizes),
    )(packed)


def split_bf16(values):
    high = values.astype(jnp.bfloat16)
    low = (values - high.astype(jnp.float32)).astype(jnp.bfloat16)
    return high, low


def inner_three(left, right_high, right_low):
    left_high, left_low = split_bf16(left)

    def dot(a, b):
        return lax.dot_general(
            a, b, (((0,), (0,)), ((), ())), preferred_element_type=jnp.float32
        )

    return dot(left_high, right_high) + dot(left_low, right_high) + dot(left_high, right_low)


def blocked_grads(edge_terms, node_terms, blocks, edge_scale, node_scale):
    terms = [(pairs, edge_scale) for pairs in edge_terms] + [(pairs, node_scale) for pairs in node_terms]
    rows = [sum(left.shape[1] for left, _ in pairs) // blocks for pairs, _ in terms]
    offsets = row_offsets(rows)
    inputs = []
    layout = []
    for pairs, scale in terms:
        layout.append((len(inputs), len(pairs), scale))
        for pair in pairs:
            inputs.extend(pair)
    width = terms[0][0][0][1].shape[1]

    order = sorted(range(len(terms)), key=lambda index: -rows[index] * terms[index][0][0][0].shape[0])
    count_in = len(inputs)

    def kernel(*refs):
        sources = refs[:count_in]
        out = refs[count_in]
        staged = refs[count_in + 1 : 2 * count_in + 1]
        results = refs[2 * count_in + 1 : 2 * count_in + 1 + len(terms)]
        in_sems = refs[-2]
        out_sems = refs[-1]
        loads = [
            pltpu.make_async_copy(sources[k], staged[k], in_sems.at[k]) for k in range(count_in)
        ]
        for index in order:
            start, count, _ = layout[index]
            for k in range(start, start + 2 * count):
                loads[k].start()
        stores = []
        for index in order:
            start, count, scale = layout[index]
            for k in range(start, start + 2 * count):
                loads[k].wait()
            pieces = []
            for k in range(count):
                right_high, right_low = split_bf16(staged[start + 2 * k + 1][...])
                pieces.append(inner_three(staged[start + 2 * k][...], right_high, right_low))
            product = jnp.concatenate(pieces, axis=0) * scale
            results[index][...] = product.reshape(blocks, rows[index], width)
            store = pltpu.make_async_copy(
                results[index], out.at[:, offsets[index] : offsets[index + 1], :], out_sems.at[index]
            )
            store.start()
            stores.append(store)
        for store in stores:
            store.wait()

    any_space = pl.BlockSpec(memory_space=pl.ANY)
    return pl.pallas_call(
        kernel,
        out_shape=jax.ShapeDtypeStruct((blocks, offsets[-1], width), jnp.float32),
        in_specs=[any_space] * count_in,
        out_specs=any_space,
        scratch_shapes=[pltpu.VMEM(x.shape, x.dtype) for x in inputs]
        + [pltpu.VMEM((blocks, size, width), jnp.float32) for size in rows]
        + [pltpu.SemaphoreType.DMA((count_in,)), pltpu.SemaphoreType.DMA((len(terms),))],
    )(*inputs)


def matmul(left, right):
    return jnp.dot(left, right, precision=lax.Precision.HIGH, preferred_element_type=jnp.float32)


def inner(left, right):
    return lax.dot_general(
        left,
        right,
        (((0,), (0,)), ((), ())),
        precision=lax.Precision.HIGH,
        preferred_element_type=jnp.float32,
    )


def outer_back(left, right):
    return lax.dot_general(
        left,
        right,
        (((1,), (1,)), ((), ())),
        precision=lax.Precision.HIGH,
        preferred_element_type=jnp.float32,
    )


def layer_norm(values):
    center = values - jnp.mean(values, axis=-1, keepdims=True)
    inverse = 1.0 / jnp.sqrt(jnp.mean(center * center, axis=-1, keepdims=True) + EPSILON)
    return (center * inverse, inverse)


def norm_back(upstream, normed, inverse):
    first = jnp.mean(upstream, axis=-1, keepdims=True)
    second = jnp.mean(upstream * normed, axis=-1, keepdims=True)
    return inverse * (upstream - first - normed * second)


def shards(
    node_states,
    node_pre,
    edge_states,
    edge_pre,
    node_cotangent,
    edge_cotangent,
    endpoints,
    send_lists,
    node_counts,
    edge_blocks,
    edge_first,
    edge_second,
    edge_bias,
    edge_gain,
    edge_shift,
    node_first,
    node_second,
    node_bias,
    node_gain,
):
    node_rows, width = node_states.shape
    edge_rows = edge_states.shape[0]
    ghost = send_lists.shape[2]
    dom_count = lax.axis_size("dom")
    sub_count = lax.axis_size("sub")
    peer_count = dom_count * sub_count
    lists = send_lists[0]
    outgoing = jnp.take(node_states, lists.reshape(-1), axis=0).reshape(4, ghost, width)
    dom_side = padded(jnp.stack([outgoing[1], outgoing[0]]), (("dom", 0),), 1)
    sub_side = padded(jnp.stack([outgoing[3], outgoing[2]]), (("sub", 0),), 1)
    ghosts = jnp.stack([dom_side[0], dom_side[3], sub_side[0], sub_side[3]])
    ghosts = ghosts.reshape(4 * ghost, width)
    peers = ("dom", "sub")
    matrices = (edge_first, edge_second, node_first, node_second)
    vectors = [v.reshape(1, -1) for v in (edge_bias, edge_gain, edge_shift, node_bias, node_gain)]
    vector_rows = 1
    packed = pack_rows(list(matrices), vectors)
    gathered = lax.all_gather(packed, peers, axis=0, tiled=True)
    pieces = []
    offset = 0
    for rows in [m.shape[0] for m in matrices] + [vector_rows]:
        pieces.append(gathered[:, offset : offset + rows, :])
        offset += rows
    full_edge_first, full_edge_second, full_node_first, full_node_second = (
        piece.reshape(-1, width) for piece in pieces[:4]
    )
    vector_count = edge_bias.shape[0]
    all_vectors = pieces[4].reshape(pieces[4].shape[0], -1)[:, : 5 * vector_count]
    all_vectors = all_vectors.reshape(-1, 5, vector_count).transpose(1, 0, 2).reshape(5, -1)
    full_edge_bias, full_edge_gain, full_edge_shift, full_node_bias, full_node_gain = (
        all_vectors[i] for i in range(5)
    )
    live_nodes = (jnp.arange(node_rows) < node_counts[0]).astype(jnp.float32)[:, None]
    live_edges = (jnp.arange(edge_rows) < edge_blocks[0] * 128).astype(jnp.float32)[:, None]
    source = endpoints[0]
    target = endpoints[1]
    edge_scale = 1.0 / math.sqrt(edge_rows * peer_count)
    node_scale = 1.0 / math.sqrt(node_rows * peer_count)
    edge_act = jnp.maximum(edge_pre, 0.0)
    edge_normed, edge_inverse = layer_norm(matmul(edge_act, full_edge_second) + full_edge_bias)
    message = (edge_normed * full_edge_gain + full_edge_shift) * live_edges
    node_act = jnp.maximum(node_pre, 0.0)
    node_normed, node_inverse = layer_norm(matmul(node_act, full_node_second) + full_node_bias)
    node_upstream = node_cotangent * live_nodes
    node_grad_z = norm_back(node_upstream * full_node_gain, node_normed, node_inverse)
    node_grad_pre = outer_back(node_grad_z, full_node_second) * (node_pre > 0).astype(jnp.float32)
    node_terms = [
        [(node_states, node_grad_pre), (message, jnp.take(node_grad_pre, target, axis=0))],
        [(node_act, node_grad_z)],
    ]
    node_grad_input = outer_back(node_grad_pre, full_node_first)
    state_grads = node_upstream + node_grad_input[:, :width]
    edge_upstream = (
        edge_cotangent + jnp.take(node_grad_input[:, width:], target, axis=0)
    ) * live_edges
    edge_grad_z = norm_back(edge_upstream * full_edge_gain, edge_normed, edge_inverse)
    edge_grad_pre = outer_back(edge_grad_z, full_edge_second) * (edge_pre > 0).astype(jnp.float32)
    extended = jnp.concatenate([node_states, ghosts], axis=0)
    sent = jnp.take(extended, source, axis=0)
    received = jnp.take(extended, target, axis=0)
    edge_terms = [
        [(edge_states, edge_grad_pre), (sent, edge_grad_pre), (received, edge_grad_pre)],
        [(edge_act, edge_grad_z)],
    ]
    if all(m.shape[0] % 8 == 0 for m in matrices):
        blocked = blocked_grads(edge_terms, node_terms, peer_count, edge_scale, node_scale)
    else:
        parts = [
            jnp.concatenate([inner(left, right) for left, right in pairs], axis=0) * scale
            for pairs, scale in zip(edge_terms + node_terms, [edge_scale] * 2 + [node_scale] * 2)
        ]
        blocked = jnp.concatenate(
            [part.reshape(peer_count, -1, width) for part in parts], axis=1
        )
    reduced = lax.psum_scatter(blocked, peers, scatter_dimension=0, tiled=True)[0]
    edge_first_grad, edge_second_grad, node_first_grad, node_second_grad = split_rows(
        reduced, [m.shape[0] for m in matrices]
    )
    edge_grad_input = outer_back(edge_grad_pre, full_edge_first)
    edge_grads = (edge_cotangent + edge_grad_input[:, :width]) * live_edges
    extended_grads = jax.ops.segment_sum(
        edge_grad_input[:, width : 2 * width], source, node_rows + 4 * ghost
    )
    extended_grads = extended_grads + jax.ops.segment_sum(
        edge_grad_input[:, 2 * width :], target, node_rows + 4 * ghost
    )
    state_grads = state_grads + extended_grads[:node_rows]
    ghost_grads = extended_grads[node_rows:].reshape(4, ghost, width)
    dom_back = padded(jnp.stack([ghost_grads[0], ghost_grads[1]]), (("dom", 0),), 1)
    sub_back = padded(jnp.stack([ghost_grads[2], ghost_grads[3]]), (("sub", 0),), 1)
    returned = jnp.stack([dom_back[3], dom_back[0], sub_back[3], sub_back[0]])
    state_grads = state_grads + jax.ops.segment_sum(
        returned.reshape(-1, width), lists.reshape(-1), node_rows
    )
    return (
        edge_grads,
        state_grads,
        edge_first_grad,
        edge_second_grad,
        node_first_grad,
        node_second_grad,
    )


def solution(mesh):
    in_specs = (
        P(("groups", "dom", "sub"), None),
        P(("groups", "dom", "sub"), None),
        P(("groups", "dom", "sub"), None),
        P(("groups", "dom", "sub"), None),
        P(("groups", "dom", "sub"), None),
        P(("groups", "dom", "sub"), None),
        P(None, ("groups", "dom", "sub")),
        P(("groups", "dom", "sub"), None, None),
        P(("groups", "dom", "sub")),
        P(("groups", "dom", "sub")),
        P(("dom", "sub"), None),
        P(("dom", "sub"), None),
        P(("dom", "sub")),
        P(("dom", "sub")),
        P(("dom", "sub")),
        P(("dom", "sub"), None),
        P(("dom", "sub"), None),
        P(("dom", "sub")),
        P(("dom", "sub")),
    )
    out_specs = (
        P(("groups", "dom", "sub"), None),
        P(("groups", "dom", "sub"), None),
        P(("groups", "dom", "sub"), None),
        P(("groups", "dom", "sub"), None),
        P(("groups", "dom", "sub"), None),
        P(("groups", "dom", "sub"), None),
    )
    return jax.shard_map(shards, mesh=mesh, in_specs=in_specs, out_specs=out_specs, check_vma=False)
```

```python
import math

import jax
import jax.numpy as jnp
from jax import lax
from jax.experimental import pallas as pl
from jax.experimental.pallas import tpu as pltpu
from jax.sharding import PartitionSpec as P

EPSILON = 1e-05


def padded(cells, sides, width):
    for axis, dim in sides:
        count = lax.axis_size(axis)
        ends = count - 1
        head = lax.slice_in_dim(cells, 0, width, axis=dim)
        tail = lax.slice_in_dim(cells, cells.shape[dim] - width, cells.shape[dim], axis=dim)
        cells = jnp.concatenate(
            [
                lax.ppermute(tail, axis, [(i, (i + 1) % count) for i in range(ends)]),
                cells,
                lax.ppermute(head, axis, [((i + 1) % count, i) for i in range(ends)]),
            ],
            axis=dim,
        )
    return cells


def row_offsets(sizes):
    offsets = [0]
    for size in sizes:
        offsets.append(offsets[-1] + size)
    return offsets


def pack_rows(pieces, vectors):
    offsets = row_offsets([piece.shape[0] for piece in pieces])
    width = pieces[0].shape[1]
    length = vectors[0].shape[1]
    count = len(pieces)

    def kernel(*refs):
        out = refs[-1]
        for index, ref in enumerate(refs[:count]):
            out[0, offsets[index] : offsets[index + 1], :] = ref[...]
        row = jnp.concatenate(
            [ref[...] for ref in refs[count:-1]]
            + [jnp.zeros((1, width - len(vectors) * length), jnp.float32)],
            axis=1,
        )
        out[0, offsets[-1] : offsets[-1] + 1, :] = row

    return pl.pallas_call(
        kernel,
        out_shape=jax.ShapeDtypeStruct((1, offsets[-1] + 1, width), pieces[0].dtype),
    )(*pieces, *vectors)


def split_rows(packed, sizes):
    offsets = row_offsets(sizes)

    def kernel(source, *outs):
        for index, out in enumerate(outs):
            out[...] = source[offsets[index] : offsets[index + 1], :]

    return pl.pallas_call(
        kernel,
        out_shape=tuple(jax.ShapeDtypeStruct((size, packed.shape[1]), packed.dtype) for size in sizes),
    )(packed)


def split_bf16(values):
    high = values.astype(jnp.bfloat16)
    low = (values - high.astype(jnp.float32)).astype(jnp.bfloat16)
    return high, low


def inner_three(left, right_high, right_low):
    left_high, left_low = split_bf16(left)

    def dot(a, b):
        return lax.dot_general(
            a, b, (((0,), (0,)), ((), ())), preferred_element_type=jnp.float32
        )

    return dot(left_high, right_high) + dot(left_low, right_high) + dot(left_high, right_low)


def blocked_grads(edge_terms, node_terms, blocks, edge_scale, node_scale):
    terms = [(pairs, edge_scale) for pairs in edge_terms] + [(pairs, node_scale) for pairs in node_terms]
    rows = [sum(left.shape[1] for left, _ in pairs) // blocks for pairs, _ in terms]
    offsets = row_offsets(rows)
    inputs = []
    layout = []

    def slot(value):
        for index, known in enumerate(inputs):
            if known is value:
                return index
        inputs.append(value)
        return len(inputs) - 1

    for pairs, scale in terms:
        layout.append(([(slot(left), slot(right)) for left, right in pairs], scale))
    width = terms[0][0][0][1].shape[1]

    order = sorted(range(len(terms)), key=lambda index: -rows[index] * terms[index][0][0][0].shape[0])
    count_in = len(inputs)

    def kernel(*refs):
        sources = refs[:count_in]
        out = refs[count_in]
        staged = refs[count_in + 1 : 2 * count_in + 1]
        results = refs[2 * count_in + 1 : 2 * count_in + 1 + len(terms)]
        in_sems = refs[-2]
        out_sems = refs[-1]
        loads = [
            pltpu.make_async_copy(sources[k], staged[k], in_sems.at[k]) for k in range(count_in)
        ]
        started = []
        for index in order:
            for pair in layout[index][0]:
                for k in pair:
                    if k not in started:
                        loads[k].start()
                        started.append(k)
        waited = []
        stores = []
        for index in order:
            pairs, scale = layout[index]
            for pair in pairs:
                for k in pair:
                    if k not in waited:
                        loads[k].wait()
                        waited.append(k)
            halves = {}
            pieces = []
            for left, right in pairs:
                if right not in halves:
                    halves[right] = split_bf16(staged[right][...])
                pieces.append(inner_three(staged[left][...], *halves[right]))
            product = jnp.concatenate(pieces, axis=0) * scale
            results[index][...] = product.reshape(blocks, rows[index], width)
            store = pltpu.make_async_copy(
                results[index], out.at[:, offsets[index] : offsets[index + 1], :], out_sems.at[index]
            )
            store.start()
            stores.append(store)
        for store in stores:
            store.wait()

    any_space = pl.BlockSpec(memory_space=pl.ANY)
    return pl.pallas_call(
        kernel,
        out_shape=jax.ShapeDtypeStruct((blocks, offsets[-1], width), jnp.float32),
        in_specs=[any_space] * count_in,
        out_specs=any_space,
        scratch_shapes=[pltpu.VMEM(x.shape, x.dtype) for x in inputs]
        + [pltpu.VMEM((blocks, size, width), jnp.float32) for size in rows]
        + [pltpu.SemaphoreType.DMA((count_in,)), pltpu.SemaphoreType.DMA((len(terms),))],
    )(*inputs)


def matmul(left, right):
    return jnp.dot(left, right, precision=lax.Precision.HIGH, preferred_element_type=jnp.float32)


def inner(left, right):
    return lax.dot_general(
        left,
        right,
        (((0,), (0,)), ((), ())),
        precision=lax.Precision.HIGH,
        preferred_element_type=jnp.float32,
    )


def outer_back(left, right):
    return lax.dot_general(
        left,
        right,
        (((1,), (1,)), ((), ())),
        precision=lax.Precision.HIGH,
        preferred_element_type=jnp.float32,
    )


def layer_norm(values):
    center = values - jnp.mean(values, axis=-1, keepdims=True)
    inverse = 1.0 / jnp.sqrt(jnp.mean(center * center, axis=-1, keepdims=True) + EPSILON)
    return (center * inverse, inverse)


def norm_back(upstream, normed, inverse):
    first = jnp.mean(upstream, axis=-1, keepdims=True)
    second = jnp.mean(upstream * normed, axis=-1, keepdims=True)
    return inverse * (upstream - first - normed * second)


def shards(
    node_states,
    node_pre,
    edge_states,
    edge_pre,
    node_cotangent,
    edge_cotangent,
    endpoints,
    send_lists,
    node_counts,
    edge_blocks,
    edge_first,
    edge_second,
    edge_bias,
    edge_gain,
    edge_shift,
    node_first,
    node_second,
    node_bias,
    node_gain,
):
    node_rows, width = node_states.shape
    edge_rows = edge_states.shape[0]
    ghost = send_lists.shape[2]
    dom_count = lax.axis_size("dom")
    sub_count = lax.axis_size("sub")
    peer_count = dom_count * sub_count
    lists = send_lists[0]
    outgoing = jnp.take(node_states, lists.reshape(-1), axis=0).reshape(4, ghost, width)
    dom_side = padded(jnp.stack([outgoing[1], outgoing[0]]), (("dom", 0),), 1)
    sub_side = padded(jnp.stack([outgoing[3], outgoing[2]]), (("sub", 0),), 1)
    ghosts = jnp.stack([dom_side[0], dom_side[3], sub_side[0], sub_side[3]])
    ghosts = ghosts.reshape(4 * ghost, width)
    peers = ("dom", "sub")
    matrices = (edge_first, edge_second, node_first, node_second)
    vectors = [v.reshape(1, -1) for v in (edge_bias, edge_gain, edge_shift, node_bias, node_gain)]
    vector_rows = 1
    packed = pack_rows(list(matrices), vectors)
    gathered = lax.all_gather(packed, peers, axis=0, tiled=True)
    pieces = []
    offset = 0
    for rows in [m.shape[0] for m in matrices] + [vector_rows]:
        pieces.append(gathered[:, offset : offset + rows, :])
        offset += rows
    full_edge_first, full_edge_second, full_node_first, full_node_second = (
        piece.reshape(-1, width) for piece in pieces[:4]
    )
    vector_count = edge_bias.shape[0]
    all_vectors = pieces[4].reshape(pieces[4].shape[0], -1)[:, : 5 * vector_count]
    all_vectors = all_vectors.reshape(-1, 5, vector_count).transpose(1, 0, 2).reshape(5, -1)
    full_edge_bias, full_edge_gain, full_edge_shift, full_node_bias, full_node_gain = (
        all_vectors[i] for i in range(5)
    )
    live_nodes = (jnp.arange(node_rows) < node_counts[0]).astype(jnp.float32)[:, None]
    live_edges = (jnp.arange(edge_rows) < edge_blocks[0] * 128).astype(jnp.float32)[:, None]
    source = endpoints[0]
    target = endpoints[1]
    edge_scale = 1.0 / math.sqrt(edge_rows * peer_count)
    node_scale = 1.0 / math.sqrt(node_rows * peer_count)
    edge_act = jnp.maximum(edge_pre, 0.0)
    edge_normed, edge_inverse = layer_norm(matmul(edge_act, full_edge_second) + full_edge_bias)
    message = (edge_normed * full_edge_gain + full_edge_shift) * live_edges
    node_act = jnp.maximum(node_pre, 0.0)
    node_normed, node_inverse = layer_norm(matmul(node_act, full_node_second) + full_node_bias)
    node_upstream = node_cotangent * live_nodes
    node_grad_z = norm_back(node_upstream * full_node_gain, node_normed, node_inverse)
    node_grad_pre = outer_back(node_grad_z, full_node_second) * (node_pre > 0).astype(jnp.float32)
    node_terms = [
        [(node_states, node_grad_pre), (message, jnp.take(node_grad_pre, target, axis=0))],
        [(node_act, node_grad_z)],
    ]
    node_grad_input = outer_back(node_grad_pre, full_node_first)
    state_grads = node_upstream + node_grad_input[:, :width]
    edge_upstream = (
        edge_cotangent + jnp.take(node_grad_input[:, width:], target, axis=0)
    ) * live_edges
    edge_grad_z = norm_back(edge_upstream * full_edge_gain, edge_normed, edge_inverse)
    edge_grad_pre = outer_back(edge_grad_z, full_edge_second) * (edge_pre > 0).astype(jnp.float32)
    extended = jnp.concatenate([node_states, ghosts], axis=0)
    sent = jnp.take(extended, source, axis=0)
    received = jnp.take(extended, target, axis=0)
    edge_terms = [
        [(edge_states, edge_grad_pre), (sent, edge_grad_pre), (received, edge_grad_pre)],
        [(edge_act, edge_grad_z)],
    ]
    if all(m.shape[0] % 8 == 0 for m in matrices):
        blocked = blocked_grads(edge_terms, node_terms, peer_count, edge_scale, node_scale)
    else:
        parts = [
            jnp.concatenate([inner(left, right) for left, right in pairs], axis=0) * scale
            for pairs, scale in zip(edge_terms + node_terms, [edge_scale] * 2 + [node_scale] * 2)
        ]
        blocked = jnp.concatenate(
            [part.reshape(peer_count, -1, width) for part in parts], axis=1
        )
    reduced = lax.psum_scatter(blocked, peers, scatter_dimension=0, tiled=True)[0]
    edge_first_grad, edge_second_grad, node_first_grad, node_second_grad = split_rows(
        reduced, [m.shape[0] for m in matrices]
    )
    edge_grad_input = outer_back(edge_grad_pre, full_edge_first)
    edge_grads = (edge_cotangent + edge_grad_input[:, :width]) * live_edges
    extended_grads = jax.ops.segment_sum(
        edge_grad_input[:, width : 2 * width], source, node_rows + 4 * ghost
    )
    extended_grads = extended_grads + jax.ops.segment_sum(
        edge_grad_input[:, 2 * width :], target, node_rows + 4 * ghost
    )
    state_grads = state_grads + extended_grads[:node_rows]
    ghost_grads = extended_grads[node_rows:].reshape(4, ghost, width)
    dom_back = padded(jnp.stack([ghost_grads[0], ghost_grads[1]]), (("dom", 0),), 1)
    sub_back = padded(jnp.stack([ghost_grads[2], ghost_grads[3]]), (("sub", 0),), 1)
    returned = jnp.stack([dom_back[3], dom_back[0], sub_back[3], sub_back[0]])
    state_grads = state_grads + jax.ops.segment_sum(
        returned.reshape(-1, width), lists.reshape(-1), node_rows
    )
    return (
        edge_grads,
        state_grads,
        edge_first_grad,
        edge_second_grad,
        node_first_grad,
        node_second_grad,
    )


def solution(mesh):
    in_specs = (
        P(("groups", "dom", "sub"), None),
        P(("groups", "dom", "sub"), None),
        P(("groups", "dom", "sub"), None),
        P(("groups", "dom", "sub"), None),
        P(("groups", "dom", "sub"), None),
        P(("groups", "dom", "sub"), None),
        P(None, ("groups", "dom", "sub")),
        P(("groups", "dom", "sub"), None, None),
        P(("groups", "dom", "sub")),
        P(("groups", "dom", "sub")),
        P(("dom", "sub"), None),
        P(("dom", "sub"), None),
        P(("dom", "sub")),
        P(("dom", "sub")),
        P(("dom", "sub")),
        P(("dom", "sub"), None),
        P(("dom", "sub"), None),
        P(("dom", "sub")),
        P(("dom", "sub")),
    )
    out_specs = (
        P(("groups", "dom", "sub"), None),
        P(("groups", "dom", "sub"), None),
        P(("groups", "dom", "sub"), None),
        P(("groups", "dom", "sub"), None),
        P(("groups", "dom", "sub"), None),
        P(("groups", "dom", "sub"), None),
    )
    return jax.shard_map(shards, mesh=mesh, in_specs=in_specs, out_specs=out_specs, check_vma=False)
```

```python
import math

import jax
import jax.numpy as jnp
from jax import lax
from jax.experimental import pallas as pl
from jax.experimental.pallas import tpu as pltpu
from jax.sharding import PartitionSpec as P

EPSILON = 1e-05


def padded(cells, sides, width):
    for axis, dim in sides:
        count = lax.axis_size(axis)
        ends = count - 1
        head = lax.slice_in_dim(cells, 0, width, axis=dim)
        tail = lax.slice_in_dim(cells, cells.shape[dim] - width, cells.shape[dim], axis=dim)
        cells = jnp.concatenate(
            [
                lax.ppermute(tail, axis, [(i, (i + 1) % count) for i in range(ends)]),
                cells,
                lax.ppermute(head, axis, [((i + 1) % count, i) for i in range(ends)]),
            ],
            axis=dim,
        )
    return cells


def row_offsets(sizes):
    offsets = [0]
    for size in sizes:
        offsets.append(offsets[-1] + size)
    return offsets


def pack_rows(pieces, vectors):
    offsets = row_offsets([piece.shape[0] for piece in pieces])
    width = pieces[0].shape[1]
    length = vectors[0].shape[1]
    count = len(pieces)

    def kernel(*refs):
        out = refs[-1]
        for index, ref in enumerate(refs[:count]):
            out[0, offsets[index] : offsets[index + 1], :] = ref[...]
        row = jnp.concatenate(
            [ref[...] for ref in refs[count:-1]]
            + [jnp.zeros((1, width - len(vectors) * length), jnp.float32)],
            axis=1,
        )
        out[0, offsets[-1] : offsets[-1] + 1, :] = row

    return pl.pallas_call(
        kernel,
        out_shape=jax.ShapeDtypeStruct((1, offsets[-1] + 1, width), pieces[0].dtype),
    )(*pieces, *vectors)


def split_rows(packed, sizes):
    offsets = row_offsets(sizes)

    def kernel(source, *outs):
        for index, out in enumerate(outs):
            out[...] = source[offsets[index] : offsets[index + 1], :]

    return pl.pallas_call(
        kernel,
        out_shape=tuple(jax.ShapeDtypeStruct((size, packed.shape[1]), packed.dtype) for size in sizes),
    )(packed)


def split_bf16(values):
    high = values.astype(jnp.bfloat16)
    low = (values - high.astype(jnp.float32)).astype(jnp.bfloat16)
    return high, low


def inner_three(left, right_high, right_low):
    left_high, left_low = split_bf16(left)

    def dot(a, b):
        return lax.dot_general(
            a, b, (((0,), (0,)), ((), ())), preferred_element_type=jnp.float32
        )

    return dot(left_high, right_high) + dot(left_low, right_high) + dot(left_high, right_low)


def blocked_grads(edge_terms, node_terms, blocks, edge_scale, node_scale):
    terms = [(pairs, edge_scale) for pairs in edge_terms] + [(pairs, node_scale) for pairs in node_terms]
    rows = [sum(left.shape[1] for left, _ in pairs) // blocks for pairs, _ in terms]
    offsets = row_offsets(rows)
    inputs = []
    layout = []

    def slot(value):
        for index, known in enumerate(inputs):
            if known is value:
                return index
        inputs.append(value)
        return len(inputs) - 1

    for pairs, scale in terms:
        layout.append(([(slot(left), slot(right)) for left, right in pairs], scale))
    width = terms[0][0][0][1].shape[1]

    order = sorted(range(len(terms)), key=lambda index: -rows[index] * terms[index][0][0][0].shape[0])
    count_in = len(inputs)

    def kernel(*refs):
        sources = refs[:count_in]
        out = refs[count_in]
        staged = refs[count_in + 1 : 2 * count_in + 1]
        results = refs[2 * count_in + 1 : 2 * count_in + 1 + len(terms)]
        in_sems = refs[-2]
        out_sems = refs[-1]
        loads = [
            pltpu.make_async_copy(sources[k], staged[k], in_sems.at[k]) for k in range(count_in)
        ]
        started = []
        for index in order:
            for pair in layout[index][0]:
                for k in pair:
                    if k not in started:
                        loads[k].start()
                        started.append(k)
        waited = []
        stores = []
        for index in order:
            pairs, scale = layout[index]
            for pair in pairs:
                for k in pair:
                    if k not in waited:
                        loads[k].wait()
                        waited.append(k)
            halves = {}
            top = 0
            for left, right in pairs:
                if right not in halves:
                    halves[right] = split_bf16(staged[right][...])
                piece = inner_three(staged[left][...], *halves[right]) * scale
                results[index][top : top + piece.shape[0], :] = piece
                top += piece.shape[0]
            size = rows[index]
            for block in range(blocks):
                store = pltpu.make_async_copy(
                    results[index].at[block * size : (block + 1) * size, :],
                    out.at[block, offsets[index] : offsets[index + 1], :],
                    out_sems.at[index * blocks + block],
                )
                store.start()
                stores.append(store)
        for store in stores:
            store.wait()

    any_space = pl.BlockSpec(memory_space=pl.ANY)
    return pl.pallas_call(
        kernel,
        out_shape=jax.ShapeDtypeStruct((blocks, offsets[-1], width), jnp.float32),
        in_specs=[any_space] * count_in,
        out_specs=any_space,
        scratch_shapes=[pltpu.VMEM(x.shape, x.dtype) for x in inputs]
        + [pltpu.VMEM((blocks * size, width), jnp.float32) for size in rows]
        + [pltpu.SemaphoreType.DMA((count_in,)), pltpu.SemaphoreType.DMA((len(terms) * blocks,))],
    )(*inputs)


def matmul(left, right):
    return jnp.dot(left, right, precision=lax.Precision.HIGH, preferred_element_type=jnp.float32)


def inner(left, right):
    return lax.dot_general(
        left,
        right,
        (((0,), (0,)), ((), ())),
        precision=lax.Precision.HIGH,
        preferred_element_type=jnp.float32,
    )


def outer_back(left, right):
    return lax.dot_general(
        left,
        right,
        (((1,), (1,)), ((), ())),
        precision=lax.Precision.HIGH,
        preferred_element_type=jnp.float32,
    )


def layer_norm(values):
    center = values - jnp.mean(values, axis=-1, keepdims=True)
    inverse = 1.0 / jnp.sqrt(jnp.mean(center * center, axis=-1, keepdims=True) + EPSILON)
    return (center * inverse, inverse)


def norm_back(upstream, normed, inverse):
    first = jnp.mean(upstream, axis=-1, keepdims=True)
    second = jnp.mean(upstream * normed, axis=-1, keepdims=True)
    return inverse * (upstream - first - normed * second)


def shards(
    node_states,
    node_pre,
    edge_states,
    edge_pre,
    node_cotangent,
    edge_cotangent,
    endpoints,
    send_lists,
    node_counts,
    edge_blocks,
    edge_first,
    edge_second,
    edge_bias,
    edge_gain,
    edge_shift,
    node_first,
    node_second,
    node_bias,
    node_gain,
):
    node_rows, width = node_states.shape
    edge_rows = edge_states.shape[0]
    ghost = send_lists.shape[2]
    dom_count = lax.axis_size("dom")
    sub_count = lax.axis_size("sub")
    peer_count = dom_count * sub_count
    lists = send_lists[0]
    outgoing = jnp.take(node_states, lists.reshape(-1), axis=0).reshape(4, ghost, width)
    dom_side = padded(jnp.stack([outgoing[1], outgoing[0]]), (("dom", 0),), 1)
    sub_side = padded(jnp.stack([outgoing[3], outgoing[2]]), (("sub", 0),), 1)
    ghosts = jnp.stack([dom_side[0], dom_side[3], sub_side[0], sub_side[3]])
    ghosts = ghosts.reshape(4 * ghost, width)
    peers = ("dom", "sub")
    matrices = (edge_first, edge_second, node_first, node_second)
    vectors = [v.reshape(1, -1) for v in (edge_bias, edge_gain, edge_shift, node_bias, node_gain)]
    vector_rows = 1
    packed = pack_rows(list(matrices), vectors)
    gathered = lax.all_gather(packed, peers, axis=0, tiled=True)
    pieces = []
    offset = 0
    for rows in [m.shape[0] for m in matrices] + [vector_rows]:
        pieces.append(gathered[:, offset : offset + rows, :])
        offset += rows
    full_edge_first, full_edge_second, full_node_first, full_node_second = (
        piece.reshape(-1, width) for piece in pieces[:4]
    )
    vector_count = edge_bias.shape[0]
    all_vectors = pieces[4].reshape(pieces[4].shape[0], -1)[:, : 5 * vector_count]
    all_vectors = all_vectors.reshape(-1, 5, vector_count).transpose(1, 0, 2).reshape(5, -1)
    full_edge_bias, full_edge_gain, full_edge_shift, full_node_bias, full_node_gain = (
        all_vectors[i] for i in range(5)
    )
    live_nodes = (jnp.arange(node_rows) < node_counts[0]).astype(jnp.float32)[:, None]
    live_edges = (jnp.arange(edge_rows) < edge_blocks[0] * 128).astype(jnp.float32)[:, None]
    source = endpoints[0]
    target = endpoints[1]
    edge_scale = 1.0 / math.sqrt(edge_rows * peer_count)
    node_scale = 1.0 / math.sqrt(node_rows * peer_count)
    edge_act = jnp.maximum(edge_pre, 0.0)
    edge_normed, edge_inverse = layer_norm(matmul(edge_act, full_edge_second) + full_edge_bias)
    message = (edge_normed * full_edge_gain + full_edge_shift) * live_edges
    node_act = jnp.maximum(node_pre, 0.0)
    node_normed, node_inverse = layer_norm(matmul(node_act, full_node_second) + full_node_bias)
    node_upstream = node_cotangent * live_nodes
    node_grad_z = norm_back(node_upstream * full_node_gain, node_normed, node_inverse)
    node_grad_pre = outer_back(node_grad_z, full_node_second) * (node_pre > 0).astype(jnp.float32)
    node_terms = [
        [(node_states, node_grad_pre), (message, jnp.take(node_grad_pre, target, axis=0))],
        [(node_act, node_grad_z)],
    ]
    node_grad_input = outer_back(node_grad_pre, full_node_first)
    state_grads = node_upstream + node_grad_input[:, :width]
    edge_upstream = (
        edge_cotangent + jnp.take(node_grad_input[:, width:], target, axis=0)
    ) * live_edges
    edge_grad_z = norm_back(edge_upstream * full_edge_gain, edge_normed, edge_inverse)
    edge_grad_pre = outer_back(edge_grad_z, full_edge_second) * (edge_pre > 0).astype(jnp.float32)
    extended = jnp.concatenate([node_states, ghosts], axis=0)
    sent = jnp.take(extended, source, axis=0)
    received = jnp.take(extended, target, axis=0)
    edge_terms = [
        [(edge_states, edge_grad_pre), (sent, edge_grad_pre), (received, edge_grad_pre)],
        [(edge_act, edge_grad_z)],
    ]
    if all(m.shape[0] % 8 == 0 for m in matrices):
        blocked = blocked_grads(edge_terms, node_terms, peer_count, edge_scale, node_scale)
    else:
        parts = [
            jnp.concatenate([inner(left, right) for left, right in pairs], axis=0) * scale
            for pairs, scale in zip(edge_terms + node_terms, [edge_scale] * 2 + [node_scale] * 2)
        ]
        blocked = jnp.concatenate(
            [part.reshape(peer_count, -1, width) for part in parts], axis=1
        )
    reduced = lax.psum_scatter(blocked, peers, scatter_dimension=0, tiled=True)[0]
    edge_first_grad, edge_second_grad, node_first_grad, node_second_grad = split_rows(
        reduced, [m.shape[0] for m in matrices]
    )
    edge_grad_input = outer_back(edge_grad_pre, full_edge_first)
    edge_grads = (edge_cotangent + edge_grad_input[:, :width]) * live_edges
    extended_grads = jax.ops.segment_sum(
        edge_grad_input[:, width : 2 * width], source, node_rows + 4 * ghost
    )
    extended_grads = extended_grads + jax.ops.segment_sum(
        edge_grad_input[:, 2 * width :], target, node_rows + 4 * ghost
    )
    state_grads = state_grads + extended_grads[:node_rows]
    ghost_grads = extended_grads[node_rows:].reshape(4, ghost, width)
    dom_back = padded(jnp.stack([ghost_grads[0], ghost_grads[1]]), (("dom", 0),), 1)
    sub_back = padded(jnp.stack([ghost_grads[2], ghost_grads[3]]), (("sub", 0),), 1)
    returned = jnp.stack([dom_back[3], dom_back[0], sub_back[3], sub_back[0]])
    state_grads = state_grads + jax.ops.segment_sum(
        returned.reshape(-1, width), lists.reshape(-1), node_rows
    )
    return (
        edge_grads,
        state_grads,
        edge_first_grad,
        edge_second_grad,
        node_first_grad,
        node_second_grad,
    )


def solution(mesh):
    in_specs = (
        P(("groups", "dom", "sub"), None),
        P(("groups", "dom", "sub"), None),
        P(("groups", "dom", "sub"), None),
        P(("groups", "dom", "sub"), None),
        P(("groups", "dom", "sub"), None),
        P(("groups", "dom", "sub"), None),
        P(None, ("groups", "dom", "sub")),
        P(("groups", "dom", "sub"), None, None),
        P(("groups", "dom", "sub")),
        P(("groups", "dom", "sub")),
        P(("dom", "sub"), None),
        P(("dom", "sub"), None),
        P(("dom", "sub")),
        P(("dom", "sub")),
        P(("dom", "sub")),
        P(("dom", "sub"), None),
        P(("dom", "sub"), None),
        P(("dom", "sub")),
        P(("dom", "sub")),
    )
    out_specs = (
        P(("groups", "dom", "sub"), None),
        P(("groups", "dom", "sub"), None),
        P(("groups", "dom", "sub"), None),
        P(("groups", "dom", "sub"), None),
        P(("groups", "dom", "sub"), None),
        P(("groups", "dom", "sub"), None),
    )
    return jax.shard_map(shards, mesh=mesh, in_specs=in_specs, out_specs=out_specs, check_vma=False)
```

```python
import math

import jax
import jax.numpy as jnp
from jax import lax
from jax.experimental import pallas as pl
from jax.experimental.pallas import tpu as pltpu
from jax.sharding import PartitionSpec as P

EPSILON = 1e-05


def padded(cells, sides, width):
    for axis, dim in sides:
        count = lax.axis_size(axis)
        ends = count - 1
        head = lax.slice_in_dim(cells, 0, width, axis=dim)
        tail = lax.slice_in_dim(cells, cells.shape[dim] - width, cells.shape[dim], axis=dim)
        cells = jnp.concatenate(
            [
                lax.ppermute(tail, axis, [(i, (i + 1) % count) for i in range(ends)]),
                cells,
                lax.ppermute(head, axis, [((i + 1) % count, i) for i in range(ends)]),
            ],
            axis=dim,
        )
    return cells


def row_offsets(sizes):
    offsets = [0]
    for size in sizes:
        offsets.append(offsets[-1] + size)
    return offsets


def pack_rows(pieces, vectors):
    offsets = row_offsets([piece.shape[0] for piece in pieces])
    width = pieces[0].shape[1]
    length = vectors[0].shape[1]
    count = len(pieces)

    def kernel(*refs):
        out = refs[-1]
        for index, ref in enumerate(refs[:count]):
            out[0, offsets[index] : offsets[index + 1], :] = ref[...]
        row = jnp.concatenate(
            [ref[...] for ref in refs[count:-1]]
            + [jnp.zeros((1, width - len(vectors) * length), jnp.float32)],
            axis=1,
        )
        out[0, offsets[-1] : offsets[-1] + 1, :] = row

    return pl.pallas_call(
        kernel,
        out_shape=jax.ShapeDtypeStruct((1, offsets[-1] + 1, width), pieces[0].dtype),
    )(*pieces, *vectors)


def split_rows(packed, sizes):
    offsets = row_offsets(sizes)

    def kernel(source, *outs):
        for index, out in enumerate(outs):
            out[...] = source[offsets[index] : offsets[index + 1], :]

    return pl.pallas_call(
        kernel,
        out_shape=tuple(jax.ShapeDtypeStruct((size, packed.shape[1]), packed.dtype) for size in sizes),
    )(packed)


def split_bf16(values):
    high = values.astype(jnp.bfloat16)
    low = (values - high.astype(jnp.float32)).astype(jnp.bfloat16)
    return high, low


def inner_three(left, right_high, right_low):
    left_high, left_low = split_bf16(left)

    def dot(a, b):
        return lax.dot_general(
            a, b, (((0,), (0,)), ((), ())), preferred_element_type=jnp.float32
        )

    return dot(left_high, right_high) + dot(left_low, right_high) + dot(left_high, right_low)


def blocked_grads(edge_terms, node_terms, blocks, edge_scale, node_scale):
    terms = [(pairs, edge_scale) for pairs in edge_terms] + [(pairs, node_scale) for pairs in node_terms]
    rows = [sum(left.shape[1] for left, _ in pairs) // blocks for pairs, _ in terms]
    offsets = row_offsets(rows)
    inputs = []
    layout = []
    for pairs, scale in terms:
        layout.append((len(inputs), len(pairs), scale))
        for pair in pairs:
            inputs.extend(pair)
    width = terms[0][0][0][1].shape[1]

    order = sorted(range(len(terms)), key=lambda index: -rows[index] * terms[index][0][0][0].shape[0])
    count_in = len(inputs)

    def kernel(*refs):
        sources = refs[:count_in]
        out = refs[count_in]
        staged = refs[count_in + 1 : 2 * count_in + 1]
        results = refs[2 * count_in + 1 : 2 * count_in + 1 + len(terms)]
        in_sems = refs[-2]
        out_sems = refs[-1]
        loads = [
            pltpu.make_async_copy(sources[k], staged[k], in_sems.at[k]) for k in range(count_in)
        ]
        for index in order:
            start, count, _ = layout[index]
            for k in range(start, start + 2 * count):
                loads[k].start()
        stores = []
        for index in order:
            start, count, scale = layout[index]
            for k in range(start, start + 2 * count):
                loads[k].wait()
            pieces = []
            for k in range(count):
                right_high, right_low = split_bf16(staged[start + 2 * k + 1][...] * scale)
                pieces.append(inner_three(staged[start + 2 * k][...], right_high, right_low))
            product = jnp.concatenate(pieces, axis=0)
            results[index][...] = product.reshape(blocks, rows[index], width)
            store = pltpu.make_async_copy(
                results[index], out.at[:, offsets[index] : offsets[index + 1], :], out_sems.at[index]
            )
            store.start()
            stores.append(store)
        for store in stores:
            store.wait()

    any_space = pl.BlockSpec(memory_space=pl.ANY)
    return pl.pallas_call(
        kernel,
        out_shape=jax.ShapeDtypeStruct((blocks, offsets[-1], width), jnp.float32),
        in_specs=[any_space] * count_in,
        out_specs=any_space,
        scratch_shapes=[pltpu.VMEM(x.shape, x.dtype) for x in inputs]
        + [pltpu.VMEM((blocks, size, width), jnp.float32) for size in rows]
        + [pltpu.SemaphoreType.DMA((count_in,)), pltpu.SemaphoreType.DMA((len(terms),))],
    )(*inputs)


def matmul(left, right):
    return jnp.dot(left, right, precision=lax.Precision.HIGH, preferred_element_type=jnp.float32)


def inner(left, right):
    return lax.dot_general(
        left,
        right,
        (((0,), (0,)), ((), ())),
        precision=lax.Precision.HIGH,
        preferred_element_type=jnp.float32,
    )


def outer_back(left, right):
    return lax.dot_general(
        left,
        right,
        (((1,), (1,)), ((), ())),
        precision=lax.Precision.HIGH,
        preferred_element_type=jnp.float32,
    )


def layer_norm(values):
    center = values - jnp.mean(values, axis=-1, keepdims=True)
    inverse = 1.0 / jnp.sqrt(jnp.mean(center * center, axis=-1, keepdims=True) + EPSILON)
    return (center * inverse, inverse)


def norm_back(upstream, normed, inverse):
    first = jnp.mean(upstream, axis=-1, keepdims=True)
    second = jnp.mean(upstream * normed, axis=-1, keepdims=True)
    return inverse * (upstream - first - normed * second)


def shards(
    node_states,
    node_pre,
    edge_states,
    edge_pre,
    node_cotangent,
    edge_cotangent,
    endpoints,
    send_lists,
    node_counts,
    edge_blocks,
    edge_first,
    edge_second,
    edge_bias,
    edge_gain,
    edge_shift,
    node_first,
    node_second,
    node_bias,
    node_gain,
):
    node_rows, width = node_states.shape
    edge_rows = edge_states.shape[0]
    ghost = send_lists.shape[2]
    dom_count = lax.axis_size("dom")
    sub_count = lax.axis_size("sub")
    peer_count = dom_count * sub_count
    lists = send_lists[0]
    outgoing = jnp.take(node_states, lists.reshape(-1), axis=0).reshape(4, ghost, width)
    dom_side = padded(jnp.stack([outgoing[1], outgoing[0]]), (("dom", 0),), 1)
    sub_side = padded(jnp.stack([outgoing[3], outgoing[2]]), (("sub", 0),), 1)
    ghosts = jnp.stack([dom_side[0], dom_side[3], sub_side[0], sub_side[3]])
    ghosts = ghosts.reshape(4 * ghost, width)
    peers = ("dom", "sub")
    matrices = (edge_first, edge_second, node_first, node_second)
    vectors = [v.reshape(1, -1) for v in (edge_bias, edge_gain, edge_shift, node_bias, node_gain)]
    vector_rows = 1
    packed = pack_rows(list(matrices), vectors)
    gathered = lax.all_gather(packed, peers, axis=0, tiled=True)
    pieces = []
    offset = 0
    for rows in [m.shape[0] for m in matrices] + [vector_rows]:
        pieces.append(gathered[:, offset : offset + rows, :])
        offset += rows
    full_edge_first, full_edge_second, full_node_first, full_node_second = (
        piece.reshape(-1, width) for piece in pieces[:4]
    )
    vector_count = edge_bias.shape[0]
    all_vectors = pieces[4].reshape(pieces[4].shape[0], -1)[:, : 5 * vector_count]
    all_vectors = all_vectors.reshape(-1, 5, vector_count).transpose(1, 0, 2).reshape(5, -1)
    full_edge_bias, full_edge_gain, full_edge_shift, full_node_bias, full_node_gain = (
        all_vectors[i] for i in range(5)
    )
    live_nodes = (jnp.arange(node_rows) < node_counts[0]).astype(jnp.float32)[:, None]
    live_edges = (jnp.arange(edge_rows) < edge_blocks[0] * 128).astype(jnp.float32)[:, None]
    source = endpoints[0]
    target = endpoints[1]
    edge_scale = 1.0 / math.sqrt(edge_rows * peer_count)
    node_scale = 1.0 / math.sqrt(node_rows * peer_count)
    edge_act = jnp.maximum(edge_pre, 0.0)
    edge_normed, edge_inverse = layer_norm(matmul(edge_act, full_edge_second) + full_edge_bias)
    message = (edge_normed * full_edge_gain + full_edge_shift) * live_edges
    node_act = jnp.maximum(node_pre, 0.0)
    node_normed, node_inverse = layer_norm(matmul(node_act, full_node_second) + full_node_bias)
    node_upstream = node_cotangent * live_nodes
    node_grad_z = norm_back(node_upstream * full_node_gain, node_normed, node_inverse)
    node_grad_pre = outer_back(node_grad_z, full_node_second) * (node_pre > 0).astype(jnp.float32)
    node_terms = [
        [(node_states, node_grad_pre), (message, jnp.take(node_grad_pre, target, axis=0))],
        [(node_act, node_grad_z)],
    ]
    node_grad_input = outer_back(node_grad_pre, full_node_first)
    state_grads = node_upstream + node_grad_input[:, :width]
    edge_upstream = (
        edge_cotangent + jnp.take(node_grad_input[:, width:], target, axis=0)
    ) * live_edges
    edge_grad_z = norm_back(edge_upstream * full_edge_gain, edge_normed, edge_inverse)
    edge_grad_pre = outer_back(edge_grad_z, full_edge_second) * (edge_pre > 0).astype(jnp.float32)
    extended = jnp.concatenate([node_states, ghosts], axis=0)
    sent = jnp.take(extended, source, axis=0)
    received = jnp.take(extended, target, axis=0)
    edge_terms = [
        [(edge_states, edge_grad_pre), (sent, edge_grad_pre), (received, edge_grad_pre)],
        [(edge_act, edge_grad_z)],
    ]
    if all(m.shape[0] % 8 == 0 for m in matrices):
        blocked = blocked_grads(edge_terms, node_terms, peer_count, edge_scale, node_scale)
    else:
        parts = [
            jnp.concatenate([inner(left, right) for left, right in pairs], axis=0) * scale
            for pairs, scale in zip(edge_terms + node_terms, [edge_scale] * 2 + [node_scale] * 2)
        ]
        blocked = jnp.concatenate(
            [part.reshape(peer_count, -1, width) for part in parts], axis=1
        )
    reduced = lax.psum_scatter(blocked, peers, scatter_dimension=0, tiled=True)[0]
    edge_first_grad, edge_second_grad, node_first_grad, node_second_grad = split_rows(
        reduced, [m.shape[0] for m in matrices]
    )
    edge_grad_input = outer_back(edge_grad_pre, full_edge_first)
    edge_grads = (edge_cotangent + edge_grad_input[:, :width]) * live_edges
    extended_grads = jax.ops.segment_sum(
        edge_grad_input[:, width : 2 * width], source, node_rows + 4 * ghost
    )
    extended_grads = extended_grads + jax.ops.segment_sum(
        edge_grad_input[:, 2 * width :], target, node_rows + 4 * ghost
    )
    state_grads = state_grads + extended_grads[:node_rows]
    ghost_grads = extended_grads[node_rows:].reshape(4, ghost, width)
    dom_back = padded(jnp.stack([ghost_grads[0], ghost_grads[1]]), (("dom", 0),), 1)
    sub_back = padded(jnp.stack([ghost_grads[2], ghost_grads[3]]), (("sub", 0),), 1)
    returned = jnp.stack([dom_back[3], dom_back[0], sub_back[3], sub_back[0]])
    state_grads = state_grads + jax.ops.segment_sum(
        returned.reshape(-1, width), lists.reshape(-1), node_rows
    )
    return (
        edge_grads,
        state_grads,
        edge_first_grad,
        edge_second_grad,
        node_first_grad,
        node_second_grad,
    )


def solution(mesh):
    in_specs = (
        P(("groups", "dom", "sub"), None),
        P(("groups", "dom", "sub"), None),
        P(("groups", "dom", "sub"), None),
        P(("groups", "dom", "sub"), None),
        P(("groups", "dom", "sub"), None),
        P(("groups", "dom", "sub"), None),
        P(None, ("groups", "dom", "sub")),
        P(("groups", "dom", "sub"), None, None),
        P(("groups", "dom", "sub")),
        P(("groups", "dom", "sub")),
        P(("dom", "sub"), None),
        P(("dom", "sub"), None),
        P(("dom", "sub")),
        P(("dom", "sub")),
        P(("dom", "sub")),
        P(("dom", "sub"), None),
        P(("dom", "sub"), None),
        P(("dom", "sub")),
        P(("dom", "sub")),
    )
    out_specs = (
        P(("groups", "dom", "sub"), None),
        P(("groups", "dom", "sub"), None),
        P(("groups", "dom", "sub"), None),
        P(("groups", "dom", "sub"), None),
        P(("groups", "dom", "sub"), None),
        P(("groups", "dom", "sub"), None),
    )
    return jax.shard_map(shards, mesh=mesh, in_specs=in_specs, out_specs=out_specs, check_vma=False)
```

```python
import math

import jax
import jax.numpy as jnp
from jax import lax
from jax.experimental import pallas as pl
from jax.experimental.pallas import tpu as pltpu
from jax.sharding import PartitionSpec as P

EPSILON = 1e-05


def padded(cells, sides, width):
    for axis, dim in sides:
        count = lax.axis_size(axis)
        ends = count - 1
        head = lax.slice_in_dim(cells, 0, width, axis=dim)
        tail = lax.slice_in_dim(cells, cells.shape[dim] - width, cells.shape[dim], axis=dim)
        cells = jnp.concatenate(
            [
                lax.ppermute(tail, axis, [(i, (i + 1) % count) for i in range(ends)]),
                cells,
                lax.ppermute(head, axis, [((i + 1) % count, i) for i in range(ends)]),
            ],
            axis=dim,
        )
    return cells


def row_offsets(sizes):
    offsets = [0]
    for size in sizes:
        offsets.append(offsets[-1] + size)
    return offsets


def pack_rows(pieces, vectors):
    offsets = row_offsets([piece.shape[0] for piece in pieces])
    width = pieces[0].shape[1]
    length = vectors[0].shape[1]
    count = len(pieces)

    def kernel(*refs):
        out = refs[-1]
        for index, ref in enumerate(refs[:count]):
            out[0, offsets[index] : offsets[index + 1], :] = ref[...]
        row = jnp.concatenate(
            [ref[...] for ref in refs[count:-1]]
            + [jnp.zeros((1, width - len(vectors) * length), jnp.float32)],
            axis=1,
        )
        out[0, offsets[-1] : offsets[-1] + 1, :] = row

    return pl.pallas_call(
        kernel,
        out_shape=jax.ShapeDtypeStruct((1, offsets[-1] + 1, width), pieces[0].dtype),
    )(*pieces, *vectors)


def split_rows(packed, sizes):
    offsets = row_offsets(sizes)

    if any(size % 8 for size in sizes):

        def staged(source, *outs):
            for index, out in enumerate(outs):
                out[...] = source[offsets[index] : offsets[index + 1], :]

        return pl.pallas_call(
            staged,
            out_shape=tuple(jax.ShapeDtypeStruct((size, packed.shape[1]), packed.dtype) for size in sizes),
        )(packed)

    def kernel(source, *refs):
        outs = refs[:-1]
        sems = refs[-1]
        copies = [
            pltpu.make_async_copy(source.at[offsets[index] : offsets[index + 1], :], out, sems.at[index])
            for index, out in enumerate(outs)
        ]
        for copy in copies:
            copy.start()
        for copy in copies:
            copy.wait()

    any_space = pl.BlockSpec(memory_space=pl.ANY)
    return pl.pallas_call(
        kernel,
        out_shape=tuple(jax.ShapeDtypeStruct((size, packed.shape[1]), packed.dtype) for size in sizes),
        in_specs=[any_space],
        out_specs=tuple(any_space for _ in sizes),
        scratch_shapes=[pltpu.SemaphoreType.DMA((len(sizes),))],
    )(packed)


def split_bf16(values):
    high = values.astype(jnp.bfloat16)
    low = (values - high.astype(jnp.float32)).astype(jnp.bfloat16)
    return high, low


def inner_three(left, right_high, right_low):
    left_high, left_low = split_bf16(left)

    def dot(a, b):
        return lax.dot_general(
            a, b, (((0,), (0,)), ((), ())), preferred_element_type=jnp.float32
        )

    return dot(left_high, right_high) + dot(left_low, right_high) + dot(left_high, right_low)


def blocked_grads(edge_terms, node_terms, blocks, edge_scale, node_scale):
    terms = [(pairs, edge_scale) for pairs in edge_terms] + [(pairs, node_scale) for pairs in node_terms]
    rows = [sum(left.shape[1] for left, _ in pairs) // blocks for pairs, _ in terms]
    offsets = row_offsets(rows)
    inputs = []
    layout = []
    for pairs, scale in terms:
        layout.append((len(inputs), len(pairs), scale))
        for pair in pairs:
            inputs.extend(pair)
    width = terms[0][0][0][1].shape[1]

    order = sorted(range(len(terms)), key=lambda index: -rows[index] * terms[index][0][0][0].shape[0])
    count_in = len(inputs)

    def kernel(*refs):
        sources = refs[:count_in]
        out = refs[count_in]
        staged = refs[count_in + 1 : 2 * count_in + 1]
        results = refs[2 * count_in + 1 : 2 * count_in + 1 + len(terms)]
        in_sems = refs[-2]
        out_sems = refs[-1]
        loads = [
            pltpu.make_async_copy(sources[k], staged[k], in_sems.at[k]) for k in range(count_in)
        ]
        for index in order:
            start, count, _ = layout[index]
            for k in range(start, start + 2 * count):
                loads[k].start()
        stores = []
        for index in order:
            start, count, scale = layout[index]
            for k in range(start, start + 2 * count):
                loads[k].wait()
            pieces = []
            for k in range(count):
                right_high, right_low = split_bf16(staged[start + 2 * k + 1][...])
                pieces.append(inner_three(staged[start + 2 * k][...], right_high, right_low))
            product = jnp.concatenate(pieces, axis=0) * scale
            results[index][...] = product.reshape(blocks, rows[index], width)
            store = pltpu.make_async_copy(
                results[index], out.at[:, offsets[index] : offsets[index + 1], :], out_sems.at[index]
            )
            store.start()
            stores.append(store)
        for store in stores:
            store.wait()

    any_space = pl.BlockSpec(memory_space=pl.ANY)
    return pl.pallas_call(
        kernel,
        out_shape=jax.ShapeDtypeStruct((blocks, offsets[-1], width), jnp.float32),
        in_specs=[any_space] * count_in,
        out_specs=any_space,
        scratch_shapes=[pltpu.VMEM(x.shape, x.dtype) for x in inputs]
        + [pltpu.VMEM((blocks, size, width), jnp.float32) for size in rows]
        + [pltpu.SemaphoreType.DMA((count_in,)), pltpu.SemaphoreType.DMA((len(terms),))],
    )(*inputs)


def matmul(left, right):
    return jnp.dot(left, right, precision=lax.Precision.HIGH, preferred_element_type=jnp.float32)


def inner(left, right):
    return lax.dot_general(
        left,
        right,
        (((0,), (0,)), ((), ())),
        precision=lax.Precision.HIGH,
        preferred_element_type=jnp.float32,
    )


def outer_back(left, right):
    return lax.dot_general(
        left,
        right,
        (((1,), (1,)), ((), ())),
        precision=lax.Precision.HIGH,
        preferred_element_type=jnp.float32,
    )


def layer_norm(values):
    center = values - jnp.mean(values, axis=-1, keepdims=True)
    inverse = 1.0 / jnp.sqrt(jnp.mean(center * center, axis=-1, keepdims=True) + EPSILON)
    return (center * inverse, inverse)


def norm_back(upstream, normed, inverse):
    first = jnp.mean(upstream, axis=-1, keepdims=True)
    second = jnp.mean(upstream * normed, axis=-1, keepdims=True)
    return inverse * (upstream - first - normed * second)


def shards(
    node_states,
    node_pre,
    edge_states,
    edge_pre,
    node_cotangent,
    edge_cotangent,
    endpoints,
    send_lists,
    node_counts,
    edge_blocks,
    edge_first,
    edge_second,
    edge_bias,
    edge_gain,
    edge_shift,
    node_first,
    node_second,
    node_bias,
    node_gain,
):
    node_rows, width = node_states.shape
    edge_rows = edge_states.shape[0]
    ghost = send_lists.shape[2]
    dom_count = lax.axis_size("dom")
    sub_count = lax.axis_size("sub")
    peer_count = dom_count * sub_count
    lists = send_lists[0]
    outgoing = jnp.take(node_states, lists.reshape(-1), axis=0).reshape(4, ghost, width)
    dom_side = padded(jnp.stack([outgoing[1], outgoing[0]]), (("dom", 0),), 1)
    sub_side = padded(jnp.stack([outgoing[3], outgoing[2]]), (("sub", 0),), 1)
    ghosts = jnp.stack([dom_side[0], dom_side[3], sub_side[0], sub_side[3]])
    ghosts = ghosts.reshape(4 * ghost, width)
    peers = ("dom", "sub")
    matrices = (edge_first, edge_second, node_first, node_second)
    vectors = [v.reshape(1, -1) for v in (edge_bias, edge_gain, edge_shift, node_bias, node_gain)]
    vector_rows = 1
    packed = pack_rows(list(matrices), vectors)
    gathered = lax.all_gather(packed, peers, axis=0, tiled=True)
    pieces = []
    offset = 0
    for rows in [m.shape[0] for m in matrices] + [vector_rows]:
        pieces.append(gathered[:, offset : offset + rows, :])
        offset += rows
    full_edge_first, full_edge_second, full_node_first, full_node_second = (
        piece.reshape(-1, width) for piece in pieces[:4]
    )
    vector_count = edge_bias.shape[0]
    all_vectors = pieces[4].reshape(pieces[4].shape[0], -1)[:, : 5 * vector_count]
    all_vectors = all_vectors.reshape(-1, 5, vector_count).transpose(1, 0, 2).reshape(5, -1)
    full_edge_bias, full_edge_gain, full_edge_shift, full_node_bias, full_node_gain = (
        all_vectors[i] for i in range(5)
    )
    live_nodes = (jnp.arange(node_rows) < node_counts[0]).astype(jnp.float32)[:, None]
    live_edges = (jnp.arange(edge_rows) < edge_blocks[0] * 128).astype(jnp.float32)[:, None]
    source = endpoints[0]
    target = endpoints[1]
    edge_scale = 1.0 / math.sqrt(edge_rows * peer_count)
    node_scale = 1.0 / math.sqrt(node_rows * peer_count)
    edge_act = jnp.maximum(edge_pre, 0.0)
    edge_normed, edge_inverse = layer_norm(matmul(edge_act, full_edge_second) + full_edge_bias)
    message = (edge_normed * full_edge_gain + full_edge_shift) * live_edges
    node_act = jnp.maximum(node_pre, 0.0)
    node_normed, node_inverse = layer_norm(matmul(node_act, full_node_second) + full_node_bias)
    node_upstream = node_cotangent * live_nodes
    node_grad_z = norm_back(node_upstream * full_node_gain, node_normed, node_inverse)
    node_grad_pre = outer_back(node_grad_z, full_node_second) * (node_pre > 0).astype(jnp.float32)
    node_terms = [
        [(node_states, node_grad_pre), (message, jnp.take(node_grad_pre, target, axis=0))],
        [(node_act, node_grad_z)],
    ]
    node_grad_input = outer_back(node_grad_pre, full_node_first)
    state_grads = node_upstream + node_grad_input[:, :width]
    edge_upstream = (
        edge_cotangent + jnp.take(node_grad_input[:, width:], target, axis=0)
    ) * live_edges
    edge_grad_z = norm_back(edge_upstream * full_edge_gain, edge_normed, edge_inverse)
    edge_grad_pre = outer_back(edge_grad_z, full_edge_second) * (edge_pre > 0).astype(jnp.float32)
    extended = jnp.concatenate([node_states, ghosts], axis=0)
    sent = jnp.take(extended, source, axis=0)
    received = jnp.take(extended, target, axis=0)
    edge_terms = [
        [(edge_states, edge_grad_pre), (sent, edge_grad_pre), (received, edge_grad_pre)],
        [(edge_act, edge_grad_z)],
    ]
    if all(m.shape[0] % 8 == 0 for m in matrices):
        blocked = blocked_grads(edge_terms, node_terms, peer_count, edge_scale, node_scale)
    else:
        parts = [
            jnp.concatenate([inner(left, right) for left, right in pairs], axis=0) * scale
            for pairs, scale in zip(edge_terms + node_terms, [edge_scale] * 2 + [node_scale] * 2)
        ]
        blocked = jnp.concatenate(
            [part.reshape(peer_count, -1, width) for part in parts], axis=1
        )
    reduced = lax.psum_scatter(blocked, peers, scatter_dimension=0, tiled=True)[0]
    edge_first_grad, edge_second_grad, node_first_grad, node_second_grad = split_rows(
        reduced, [m.shape[0] for m in matrices]
    )
    edge_grad_input = outer_back(edge_grad_pre, full_edge_first)
    edge_grads = (edge_cotangent + edge_grad_input[:, :width]) * live_edges
    extended_grads = jax.ops.segment_sum(
        edge_grad_input[:, width : 2 * width], source, node_rows + 4 * ghost
    )
    extended_grads = extended_grads + jax.ops.segment_sum(
        edge_grad_input[:, 2 * width :], target, node_rows + 4 * ghost
    )
    state_grads = state_grads + extended_grads[:node_rows]
    ghost_grads = extended_grads[node_rows:].reshape(4, ghost, width)
    dom_back = padded(jnp.stack([ghost_grads[0], ghost_grads[1]]), (("dom", 0),), 1)
    sub_back = padded(jnp.stack([ghost_grads[2], ghost_grads[3]]), (("sub", 0),), 1)
    returned = jnp.stack([dom_back[3], dom_back[0], sub_back[3], sub_back[0]])
    state_grads = state_grads + jax.ops.segment_sum(
        returned.reshape(-1, width), lists.reshape(-1), node_rows
    )
    return (
        edge_grads,
        state_grads,
        edge_first_grad,
        edge_second_grad,
        node_first_grad,
        node_second_grad,
    )


def solution(mesh):
    in_specs = (
        P(("groups", "dom", "sub"), None),
        P(("groups", "dom", "sub"), None),
        P(("groups", "dom", "sub"), None),
        P(("groups", "dom", "sub"), None),
        P(("groups", "dom", "sub"), None),
        P(("groups", "dom", "sub"), None),
        P(None, ("groups", "dom", "sub")),
        P(("groups", "dom", "sub"), None, None),
        P(("groups", "dom", "sub")),
        P(("groups", "dom", "sub")),
        P(("dom", "sub"), None),
        P(("dom", "sub"), None),
        P(("dom", "sub")),
        P(("dom", "sub")),
        P(("dom", "sub")),
        P(("dom", "sub"), None),
        P(("dom", "sub"), None),
        P(("dom", "sub")),
        P(("dom", "sub")),
    )
    out_specs = (
        P(("groups", "dom", "sub"), None),
        P(("groups", "dom", "sub"), None),
        P(("groups", "dom", "sub"), None),
        P(("groups", "dom", "sub"), None),
        P(("groups", "dom", "sub"), None),
        P(("groups", "dom", "sub"), None),
    )
    return jax.shard_map(shards, mesh=mesh, in_specs=in_specs, out_specs=out_specs, check_vma=False)
```

```python
import math

import jax
import jax.numpy as jnp
from jax import lax
from jax.experimental import pallas as pl
from jax.experimental.pallas import tpu as pltpu
from jax.sharding import PartitionSpec as P

EPSILON = 1e-05


def padded(cells, sides, width):
    for axis, dim in sides:
        count = lax.axis_size(axis)
        ends = count - 1
        head = lax.slice_in_dim(cells, 0, width, axis=dim)
        tail = lax.slice_in_dim(cells, cells.shape[dim] - width, cells.shape[dim], axis=dim)
        cells = jnp.concatenate(
            [
                lax.ppermute(tail, axis, [(i, (i + 1) % count) for i in range(ends)]),
                cells,
                lax.ppermute(head, axis, [((i + 1) % count, i) for i in range(ends)]),
            ],
            axis=dim,
        )
    return cells


def row_offsets(sizes):
    offsets = [0]
    for size in sizes:
        offsets.append(offsets[-1] + size)
    return offsets


def pack_rows(pieces, vectors):
    offsets = row_offsets([piece.shape[0] for piece in pieces])
    width = pieces[0].shape[1]
    length = vectors[0].shape[1]
    count = len(pieces)

    def kernel(*refs):
        out = refs[-1]
        for index, ref in enumerate(refs[:count]):
            out[0, offsets[index] : offsets[index + 1], :] = ref[...]
        row = jnp.concatenate(
            [ref[...] for ref in refs[count:-1]]
            + [jnp.zeros((1, width - len(vectors) * length), jnp.float32)],
            axis=1,
        )
        out[0, offsets[-1] : offsets[-1] + 1, :] = row

    return pl.pallas_call(
        kernel,
        out_shape=jax.ShapeDtypeStruct((1, offsets[-1] + 1, width), pieces[0].dtype),
    )(*pieces, *vectors)


def split_rows(packed, sizes):
    offsets = row_offsets(sizes)

    def kernel(source, *outs):
        for index, out in enumerate(outs):
            out[...] = source[offsets[index] : offsets[index + 1], :]

    return pl.pallas_call(
        kernel,
        out_shape=tuple(jax.ShapeDtypeStruct((size, packed.shape[1]), packed.dtype) for size in sizes),
    )(packed)


def split_bf16(values):
    high = values.astype(jnp.bfloat16)
    low = (values - high.astype(jnp.float32)).astype(jnp.bfloat16)
    return high, low


def inner_three(left, right_high, right_low):
    left_high, left_low = split_bf16(left)

    def dot(a, b):
        return lax.dot_general(
            a, b, (((0,), (0,)), ((), ())), preferred_element_type=jnp.float32
        )

    return dot(left_high, right_high) + dot(left_low, right_high) + dot(left_high, right_low)


def blocked_grads(edge_terms, node_terms, blocks, edge_scale, node_scale):
    terms = [(pairs, edge_scale) for pairs in edge_terms] + [(pairs, node_scale) for pairs in node_terms]
    rows = [sum(left.shape[1] for left, _ in pairs) // blocks for pairs, _ in terms]
    offsets = row_offsets(rows)
    inputs = []
    layout = []
    for pairs, scale in terms:
        layout.append((len(inputs), len(pairs), scale))
        for pair in pairs:
            inputs.extend(pair)
    width = terms[0][0][0][1].shape[1]

    order = sorted(range(len(terms)), key=lambda index: -rows[index] * terms[index][0][0][0].shape[0])
    order = order[-1:] + order[:-1]
    count_in = len(inputs)

    def kernel(*refs):
        sources = refs[:count_in]
        out = refs[count_in]
        staged = refs[count_in + 1 : 2 * count_in + 1]
        results = refs[2 * count_in + 1 : 2 * count_in + 1 + len(terms)]
        in_sems = refs[-2]
        out_sems = refs[-1]
        loads = [
            pltpu.make_async_copy(sources[k], staged[k], in_sems.at[k]) for k in range(count_in)
        ]
        for index in order:
            start, count, _ = layout[index]
            for k in range(start, start + 2 * count):
                loads[k].start()
        stores = []
        for index in order:
            start, count, scale = layout[index]
            for k in range(start, start + 2 * count):
                loads[k].wait()
            pieces = []
            for k in range(count):
                right_high, right_low = split_bf16(staged[start + 2 * k + 1][...])
                pieces.append(inner_three(staged[start + 2 * k][...], right_high, right_low))
            product = jnp.concatenate(pieces, axis=0) * scale
            results[index][...] = product.reshape(blocks, rows[index], width)
            store = pltpu.make_async_copy(
                results[index], out.at[:, offsets[index] : offsets[index + 1], :], out_sems.at[index]
            )
            store.start()
            stores.append(store)
        for store in stores:
            store.wait()

    any_space = pl.BlockSpec(memory_space=pl.ANY)
    return pl.pallas_call(
        kernel,
        out_shape=jax.ShapeDtypeStruct((blocks, offsets[-1], width), jnp.float32),
        in_specs=[any_space] * count_in,
        out_specs=any_space,
        scratch_shapes=[pltpu.VMEM(x.shape, x.dtype) for x in inputs]
        + [pltpu.VMEM((blocks, size, width), jnp.float32) for size in rows]
        + [pltpu.SemaphoreType.DMA((count_in,)), pltpu.SemaphoreType.DMA((len(terms),))],
    )(*inputs)


def matmul(left, right):
    return jnp.dot(left, right, precision=lax.Precision.HIGH, preferred_element_type=jnp.float32)


def inner(left, right):
    return lax.dot_general(
        left,
        right,
        (((0,), (0,)), ((), ())),
        precision=lax.Precision.HIGH,
        preferred_element_type=jnp.float32,
    )


def outer_back(left, right):
    return lax.dot_general(
        left,
        right,
        (((1,), (1,)), ((), ())),
        precision=lax.Precision.HIGH,
        preferred_element_type=jnp.float32,
    )


def layer_norm(values):
    center = values - jnp.mean(values, axis=-1, keepdims=True)
    inverse = 1.0 / jnp.sqrt(jnp.mean(center * center, axis=-1, keepdims=True) + EPSILON)
    return (center * inverse, inverse)


def norm_back(upstream, normed, inverse):
    first = jnp.mean(upstream, axis=-1, keepdims=True)
    second = jnp.mean(upstream * normed, axis=-1, keepdims=True)
    return inverse * (upstream - first - normed * second)


def shards(
    node_states,
    node_pre,
    edge_states,
    edge_pre,
    node_cotangent,
    edge_cotangent,
    endpoints,
    send_lists,
    node_counts,
    edge_blocks,
    edge_first,
    edge_second,
    edge_bias,
    edge_gain,
    edge_shift,
    node_first,
    node_second,
    node_bias,
    node_gain,
):
    node_rows, width = node_states.shape
    edge_rows = edge_states.shape[0]
    ghost = send_lists.shape[2]
    dom_count = lax.axis_size("dom")
    sub_count = lax.axis_size("sub")
    peer_count = dom_count * sub_count
    lists = send_lists[0]
    outgoing = jnp.take(node_states, lists.reshape(-1), axis=0).reshape(4, ghost, width)
    dom_side = padded(jnp.stack([outgoing[1], outgoing[0]]), (("dom", 0),), 1)
    sub_side = padded(jnp.stack([outgoing[3], outgoing[2]]), (("sub", 0),), 1)
    ghosts = jnp.stack([dom_side[0], dom_side[3], sub_side[0], sub_side[3]])
    ghosts = ghosts.reshape(4 * ghost, width)
    peers = ("dom", "sub")
    matrices = (edge_first, edge_second, node_first, node_second)
    vectors = [v.reshape(1, -1) for v in (edge_bias, edge_gain, edge_shift, node_bias, node_gain)]
    vector_rows = 1
    packed = pack_rows(list(matrices), vectors)
    gathered = lax.all_gather(packed, peers, axis=0, tiled=True)
    pieces = []
    offset = 0
    for rows in [m.shape[0] for m in matrices] + [vector_rows]:
        pieces.append(gathered[:, offset : offset + rows, :])
        offset += rows
    full_edge_first, full_edge_second, full_node_first, full_node_second = (
        piece.reshape(-1, width) for piece in pieces[:4]
    )
    vector_count = edge_bias.shape[0]
    all_vectors = pieces[4].reshape(pieces[4].shape[0], -1)[:, : 5 * vector_count]
    all_vectors = all_vectors.reshape(-1, 5, vector_count).transpose(1, 0, 2).reshape(5, -1)
    full_edge_bias, full_edge_gain, full_edge_shift, full_node_bias, full_node_gain = (
        all_vectors[i] for i in range(5)
    )
    live_nodes = (jnp.arange(node_rows) < node_counts[0]).astype(jnp.float32)[:, None]
    live_edges = (jnp.arange(edge_rows) < edge_blocks[0] * 128).astype(jnp.float32)[:, None]
    source = endpoints[0]
    target = endpoints[1]
    edge_scale = 1.0 / math.sqrt(edge_rows * peer_count)
    node_scale = 1.0 / math.sqrt(node_rows * peer_count)
    edge_act = jnp.maximum(edge_pre, 0.0)
    edge_normed, edge_inverse = layer_norm(matmul(edge_act, full_edge_second) + full_edge_bias)
    message = (edge_normed * full_edge_gain + full_edge_shift) * live_edges
    node_act = jnp.maximum(node_pre, 0.0)
    node_normed, node_inverse = layer_norm(matmul(node_act, full_node_second) + full_node_bias)
    node_upstream = node_cotangent * live_nodes
    node_grad_z = norm_back(node_upstream * full_node_gain, node_normed, node_inverse)
    node_grad_pre = outer_back(node_grad_z, full_node_second) * (node_pre > 0).astype(jnp.float32)
    node_terms = [
        [(node_states, node_grad_pre), (message, jnp.take(node_grad_pre, target, axis=0))],
        [(node_act, node_grad_z)],
    ]
    node_grad_input = outer_back(node_grad_pre, full_node_first)
    state_grads = node_upstream + node_grad_input[:, :width]
    edge_upstream = (
        edge_cotangent + jnp.take(node_grad_input[:, width:], target, axis=0)
    ) * live_edges
    edge_grad_z = norm_back(edge_upstream * full_edge_gain, edge_normed, edge_inverse)
    edge_grad_pre = outer_back(edge_grad_z, full_edge_second) * (edge_pre > 0).astype(jnp.float32)
    extended = jnp.concatenate([node_states, ghosts], axis=0)
    sent = jnp.take(extended, source, axis=0)
    received = jnp.take(extended, target, axis=0)
    edge_terms = [
        [(edge_states, edge_grad_pre), (sent, edge_grad_pre), (received, edge_grad_pre)],
        [(edge_act, edge_grad_z)],
    ]
    if all(m.shape[0] % 8 == 0 for m in matrices):
        blocked = blocked_grads(edge_terms, node_terms, peer_count, edge_scale, node_scale)
    else:
        parts = [
            jnp.concatenate([inner(left, right) for left, right in pairs], axis=0) * scale
            for pairs, scale in zip(edge_terms + node_terms, [edge_scale] * 2 + [node_scale] * 2)
        ]
        blocked = jnp.concatenate(
            [part.reshape(peer_count, -1, width) for part in parts], axis=1
        )
    reduced = lax.psum_scatter(blocked, peers, scatter_dimension=0, tiled=True)[0]
    edge_first_grad, edge_second_grad, node_first_grad, node_second_grad = split_rows(
        reduced, [m.shape[0] for m in matrices]
    )
    edge_grad_input = outer_back(edge_grad_pre, full_edge_first)
    edge_grads = (edge_cotangent + edge_grad_input[:, :width]) * live_edges
    extended_grads = jax.ops.segment_sum(
        edge_grad_input[:, width : 2 * width], source, node_rows + 4 * ghost
    )
    extended_grads = extended_grads + jax.ops.segment_sum(
        edge_grad_input[:, 2 * width :], target, node_rows + 4 * ghost
    )
    state_grads = state_grads + extended_grads[:node_rows]
    ghost_grads = extended_grads[node_rows:].reshape(4, ghost, width)
    dom_back = padded(jnp.stack([ghost_grads[0], ghost_grads[1]]), (("dom", 0),), 1)
    sub_back = padded(jnp.stack([ghost_grads[2], ghost_grads[3]]), (("sub", 0),), 1)
    returned = jnp.stack([dom_back[3], dom_back[0], sub_back[3], sub_back[0]])
    state_grads = state_grads + jax.ops.segment_sum(
        returned.reshape(-1, width), lists.reshape(-1), node_rows
    )
    return (
        edge_grads,
        state_grads,
        edge_first_grad,
        edge_second_grad,
        node_first_grad,
        node_second_grad,
    )


def solution(mesh):
    in_specs = (
        P(("groups", "dom", "sub"), None),
        P(("groups", "dom", "sub"), None),
        P(("groups", "dom", "sub"), None),
        P(("groups", "dom", "sub"), None),
        P(("groups", "dom", "sub"), None),
        P(("groups", "dom", "sub"), None),
        P(None, ("groups", "dom", "sub")),
        P(("groups", "dom", "sub"), None, None),
        P(("groups", "dom", "sub")),
        P(("groups", "dom", "sub")),
        P(("dom", "sub"), None),
        P(("dom", "sub"), None),
        P(("dom", "sub")),
        P(("dom", "sub")),
        P(("dom", "sub")),
        P(("dom", "sub"), None),
        P(("dom", "sub"), None),
        P(("dom", "sub")),
        P(("dom", "sub")),
    )
    out_specs = (
        P(("groups", "dom", "sub"), None),
        P(("groups", "dom", "sub"), None),
        P(("groups", "dom", "sub"), None),
        P(("groups", "dom", "sub"), None),
        P(("groups", "dom", "sub"), None),
        P(("groups", "dom", "sub"), None),
    )
    return jax.shard_map(shards, mesh=mesh, in_specs=in_specs, out_specs=out_specs, check_vma=False)
```

```python
import math

import jax
import jax.numpy as jnp
from jax import lax
from jax.experimental import pallas as pl
from jax.experimental.pallas import tpu as pltpu
from jax.sharding import PartitionSpec as P

EPSILON = 1e-05


def padded(cells, sides, width):
    for axis, dim in sides:
        count = lax.axis_size(axis)
        ends = count - 1
        head = lax.slice_in_dim(cells, 0, width, axis=dim)
        tail = lax.slice_in_dim(cells, cells.shape[dim] - width, cells.shape[dim], axis=dim)
        cells = jnp.concatenate(
            [
                lax.ppermute(tail, axis, [(i, (i + 1) % count) for i in range(ends)]),
                cells,
                lax.ppermute(head, axis, [((i + 1) % count, i) for i in range(ends)]),
            ],
            axis=dim,
        )
    return cells


def row_offsets(sizes):
    offsets = [0]
    for size in sizes:
        offsets.append(offsets[-1] + size)
    return offsets


def pack_rows(pieces, vectors):
    offsets = row_offsets([piece.shape[0] for piece in pieces])
    width = pieces[0].shape[1]
    length = vectors[0].shape[1]
    count = len(pieces)

    def kernel(*refs):
        out = refs[-1]
        for index, ref in enumerate(refs[:count]):
            out[0, offsets[index] : offsets[index + 1], :] = ref[...]
        row = jnp.concatenate(
            [ref[...] for ref in refs[count:-1]]
            + [jnp.zeros((1, width - len(vectors) * length), jnp.float32)],
            axis=1,
        )
        out[0, offsets[-1] : offsets[-1] + 1, :] = row

    return pl.pallas_call(
        kernel,
        out_shape=jax.ShapeDtypeStruct((1, offsets[-1] + 1, width), pieces[0].dtype),
    )(*pieces, *vectors)


def split_rows(packed, sizes):
    offsets = row_offsets(sizes)

    def kernel(source, *outs):
        for index, out in enumerate(outs):
            out[...] = source[offsets[index] : offsets[index + 1], :]

    return pl.pallas_call(
        kernel,
        out_shape=tuple(jax.ShapeDtypeStruct((size, packed.shape[1]), packed.dtype) for size in sizes),
    )(packed)


def split_bf16(values):
    high = values.astype(jnp.bfloat16)
    low = (values - high.astype(jnp.float32)).astype(jnp.bfloat16)
    return high, low


def inner_three(left, right_high, right_low):
    left_high, left_low = split_bf16(left)

    def dot(a, b):
        return lax.dot_general(
            a, b, (((0,), (0,)), ((), ())), preferred_element_type=jnp.float32
        )

    return dot(left_high, right_high) + dot(left_low, right_high) + dot(left_high, right_low)


def blocked_grads(edge_terms, node_terms, blocks, edge_scale, node_scale):
    terms = [(pairs, edge_scale) for pairs in edge_terms] + [(pairs, node_scale) for pairs in node_terms]
    rows = [sum(left.shape[1] for left, _ in pairs) // blocks for pairs, _ in terms]
    offsets = row_offsets(rows)
    inputs = []
    layout = []
    for pairs, scale in terms:
        layout.append((len(inputs), len(pairs), scale))
        for pair in pairs:
            inputs.extend(pair)
    width = terms[0][0][0][1].shape[1]

    order = sorted(range(len(terms)), key=lambda index: -rows[index] * width)
    count_in = len(inputs)

    def kernel(*refs):
        sources = refs[:count_in]
        out = refs[count_in]
        staged = refs[count_in + 1 : 2 * count_in + 1]
        results = refs[2 * count_in + 1 : 2 * count_in + 1 + len(terms)]
        in_sems = refs[-2]
        out_sems = refs[-1]
        loads = [
            pltpu.make_async_copy(sources[k], staged[k], in_sems.at[k]) for k in range(count_in)
        ]
        for index in order:
            start, count, _ = layout[index]
            for k in range(start, start + 2 * count):
                loads[k].start()
        stores = []
        for index in order:
            start, count, scale = layout[index]
            for k in range(start, start + 2 * count):
                loads[k].wait()
            pieces = []
            for k in range(count):
                right_high, right_low = split_bf16(staged[start + 2 * k + 1][...])
                pieces.append(inner_three(staged[start + 2 * k][...], right_high, right_low))
            product = jnp.concatenate(pieces, axis=0) * scale
            results[index][...] = product.reshape(blocks, rows[index], width)
            store = pltpu.make_async_copy(
                results[index], out.at[:, offsets[index] : offsets[index + 1], :], out_sems.at[index]
            )
            store.start()
            stores.append(store)
        for store in stores:
            store.wait()

    any_space = pl.BlockSpec(memory_space=pl.ANY)
    return pl.pallas_call(
        kernel,
        out_shape=jax.ShapeDtypeStruct((blocks, offsets[-1], width), jnp.float32),
        in_specs=[any_space] * count_in,
        out_specs=any_space,
        scratch_shapes=[pltpu.VMEM(x.shape, x.dtype) for x in inputs]
        + [pltpu.VMEM((blocks, size, width), jnp.float32) for size in rows]
        + [pltpu.SemaphoreType.DMA((count_in,)), pltpu.SemaphoreType.DMA((len(terms),))],
    )(*inputs)


def matmul(left, right):
    return jnp.dot(left, right, precision=lax.Precision.HIGH, preferred_element_type=jnp.float32)


def inner(left, right):
    return lax.dot_general(
        left,
        right,
        (((0,), (0,)), ((), ())),
        precision=lax.Precision.HIGH,
        preferred_element_type=jnp.float32,
    )


def outer_back(left, right):
    return lax.dot_general(
        left,
        right,
        (((1,), (1,)), ((), ())),
        precision=lax.Precision.HIGH,
        preferred_element_type=jnp.float32,
    )


def layer_norm(values):
    center = values - jnp.mean(values, axis=-1, keepdims=True)
    inverse = 1.0 / jnp.sqrt(jnp.mean(center * center, axis=-1, keepdims=True) + EPSILON)
    return (center * inverse, inverse)


def norm_back(upstream, normed, inverse):
    first = jnp.mean(upstream, axis=-1, keepdims=True)
    second = jnp.mean(upstream * normed, axis=-1, keepdims=True)
    return inverse * (upstream - first - normed * second)


def shards(
    node_states,
    node_pre,
    edge_states,
    edge_pre,
    node_cotangent,
    edge_cotangent,
    endpoints,
    send_lists,
    node_counts,
    edge_blocks,
    edge_first,
    edge_second,
    edge_bias,
    edge_gain,
    edge_shift,
    node_first,
    node_second,
    node_bias,
    node_gain,
):
    node_rows, width = node_states.shape
    edge_rows = edge_states.shape[0]
    ghost = send_lists.shape[2]
    dom_count = lax.axis_size("dom")
    sub_count = lax.axis_size("sub")
    peer_count = dom_count * sub_count
    lists = send_lists[0]
    outgoing = jnp.take(node_states, lists.reshape(-1), axis=0).reshape(4, ghost, width)
    dom_side = padded(jnp.stack([outgoing[1], outgoing[0]]), (("dom", 0),), 1)
    sub_side = padded(jnp.stack([outgoing[3], outgoing[2]]), (("sub", 0),), 1)
    ghosts = jnp.stack([dom_side[0], dom_side[3], sub_side[0], sub_side[3]])
    ghosts = ghosts.reshape(4 * ghost, width)
    peers = ("dom", "sub")
    matrices = (edge_first, edge_second, node_first, node_second)
    vectors = [v.reshape(1, -1) for v in (edge_bias, edge_gain, edge_shift, node_bias, node_gain)]
    vector_rows = 1
    packed = pack_rows(list(matrices), vectors)
    gathered = lax.all_gather(packed, peers, axis=0, tiled=True)
    pieces = []
    offset = 0
    for rows in [m.shape[0] for m in matrices] + [vector_rows]:
        pieces.append(gathered[:, offset : offset + rows, :])
        offset += rows
    full_edge_first, full_edge_second, full_node_first, full_node_second = (
        piece.reshape(-1, width) for piece in pieces[:4]
    )
    vector_count = edge_bias.shape[0]
    all_vectors = pieces[4].reshape(pieces[4].shape[0], -1)[:, : 5 * vector_count]
    all_vectors = all_vectors.reshape(-1, 5, vector_count).transpose(1, 0, 2).reshape(5, -1)
    full_edge_bias, full_edge_gain, full_edge_shift, full_node_bias, full_node_gain = (
        all_vectors[i] for i in range(5)
    )
    live_nodes = (jnp.arange(node_rows) < node_counts[0]).astype(jnp.float32)[:, None]
    live_edges = (jnp.arange(edge_rows) < edge_blocks[0] * 128).astype(jnp.float32)[:, None]
    source = endpoints[0]
    target = endpoints[1]
    edge_scale = 1.0 / math.sqrt(edge_rows * peer_count)
    node_scale = 1.0 / math.sqrt(node_rows * peer_count)
    edge_act = jnp.maximum(edge_pre, 0.0)
    edge_normed, edge_inverse = layer_norm(matmul(edge_act, full_edge_second) + full_edge_bias)
    message = (edge_normed * full_edge_gain + full_edge_shift) * live_edges
    node_act = jnp.maximum(node_pre, 0.0)
    node_normed, node_inverse = layer_norm(matmul(node_act, full_node_second) + full_node_bias)
    node_upstream = node_cotangent * live_nodes
    node_grad_z = norm_back(node_upstream * full_node_gain, node_normed, node_inverse)
    node_grad_pre = outer_back(node_grad_z, full_node_second) * (node_pre > 0).astype(jnp.float32)
    node_terms = [
        [(node_states, node_grad_pre), (message, jnp.take(node_grad_pre, target, axis=0))],
        [(node_act, node_grad_z)],
    ]
    node_grad_input = outer_back(node_grad_pre, full_node_first)
    state_grads = node_upstream + node_grad_input[:, :width]
    edge_upstream = (
        edge_cotangent + jnp.take(node_grad_input[:, width:], target, axis=0)
    ) * live_edges
    edge_grad_z = norm_back(edge_upstream * full_edge_gain, edge_normed, edge_inverse)
    edge_grad_pre = outer_back(edge_grad_z, full_edge_second) * (edge_pre > 0).astype(jnp.float32)
    extended = jnp.concatenate([node_states, ghosts], axis=0)
    sent = jnp.take(extended, source, axis=0)
    received = jnp.take(extended, target, axis=0)
    edge_terms = [
        [(edge_states, edge_grad_pre), (sent, edge_grad_pre), (received, edge_grad_pre)],
        [(edge_act, edge_grad_z)],
    ]
    if all(m.shape[0] % 8 == 0 for m in matrices):
        blocked = blocked_grads(edge_terms, node_terms, peer_count, edge_scale, node_scale)
    else:
        parts = [
            jnp.concatenate([inner(left, right) for left, right in pairs], axis=0) * scale
            for pairs, scale in zip(edge_terms + node_terms, [edge_scale] * 2 + [node_scale] * 2)
        ]
        blocked = jnp.concatenate(
            [part.reshape(peer_count, -1, width) for part in parts], axis=1
        )
    reduced = lax.psum_scatter(blocked, peers, scatter_dimension=0, tiled=True)[0]
    edge_first_grad, edge_second_grad, node_first_grad, node_second_grad = split_rows(
        reduced, [m.shape[0] for m in matrices]
    )
    edge_grad_input = outer_back(edge_grad_pre, full_edge_first)
    edge_grads = (edge_cotangent + edge_grad_input[:, :width]) * live_edges
    extended_grads = jax.ops.segment_sum(
        edge_grad_input[:, width : 2 * width], source, node_rows + 4 * ghost
    )
    extended_grads = extended_grads + jax.ops.segment_sum(
        edge_grad_input[:, 2 * width :], target, node_rows + 4 * ghost
    )
    state_grads = state_grads + extended_grads[:node_rows]
    ghost_grads = extended_grads[node_rows:].reshape(4, ghost, width)
    dom_back = padded(jnp.stack([ghost_grads[0], ghost_grads[1]]), (("dom", 0),), 1)
    sub_back = padded(jnp.stack([ghost_grads[2], ghost_grads[3]]), (("sub", 0),), 1)
    returned = jnp.stack([dom_back[3], dom_back[0], sub_back[3], sub_back[0]])
    state_grads = state_grads + jax.ops.segment_sum(
        returned.reshape(-1, width), lists.reshape(-1), node_rows
    )
    return (
        edge_grads,
        state_grads,
        edge_first_grad,
        edge_second_grad,
        node_first_grad,
        node_second_grad,
    )


def solution(mesh):
    in_specs = (
        P(("groups", "dom", "sub"), None),
        P(("groups", "dom", "sub"), None),
        P(("groups", "dom", "sub"), None),
        P(("groups", "dom", "sub"), None),
        P(("groups", "dom", "sub"), None),
        P(("groups", "dom", "sub"), None),
        P(None, ("groups", "dom", "sub")),
        P(("groups", "dom", "sub"), None, None),
        P(("groups", "dom", "sub")),
        P(("groups", "dom", "sub")),
        P(("dom", "sub"), None),
        P(("dom", "sub"), None),
        P(("dom", "sub")),
        P(("dom", "sub")),
        P(("dom", "sub")),
        P(("dom", "sub"), None),
        P(("dom", "sub"), None),
        P(("dom", "sub")),
        P(("dom", "sub")),
    )
    out_specs = (
        P(("groups", "dom", "sub"), None),
        P(("groups", "dom", "sub"), None),
        P(("groups", "dom", "sub"), None),
        P(("groups", "dom", "sub"), None),
        P(("groups", "dom", "sub"), None),
        P(("groups", "dom", "sub"), None),
    )
    return jax.shard_map(shards, mesh=mesh, in_specs=in_specs, out_specs=out_specs, check_vma=False)
```
